128 devices in a mesh: dp: 2 (over z_hi), context: 16 (over z_lo, y, core), tensor: 4 (over x).
Axes of the slice: x: 4, y: 4, z: 4 (z_hi: 2, z_lo: 2; z = z_hi * 2 + z_lo), core: 2. Of those that a mesh axis runs over, the one named last changes fastest.
Arguments:
- streams: bfloat16 [4096, 3, 4096], P(('dp', 'context'), None, 'tensor'), parts along dimension 0, may hold values from -6 to 6
- stream_tail: bfloat16 [4, 3, 4096], P('dp', None, 'tensor'), parts along dimension 0, may hold values from -6 to 6
- short_taps: float32 [3, 3, 4096], P(None, None, 'tensor'), may hold values from -3 to 3
- decay_rates: float32 [16, 4096], P(None, 'tensor'), may hold values from 0.00012207031 to 0.05
- residues: float32 [16, 4096], P(None, 'tensor'), may hold values from -1.5 to 1.5
- hyena_state: float32 [32, 4096], P('dp', 'tensor'), parts along dimension 0, may hold values from -6 to 6
- skip_weight: float32 [4096], P('tensor'), may hold values from -4 to 4
- residual: bfloat16 [4096, 4096], P(('dp', 'context'), 'tensor'), parts along dimension 0, may hold values from -6 to 6
- norm_gain: float32 [4096], replicated, may hold values from 0.1 to 1.9
- qkv_weight: bfloat16 [4096, 3, 4096], P(None, None, 'tensor'), may hold values from -0.09375 to 0.09375
- start_offset: int32 [2], P('dp'), parts along dimension 0, may hold values from 2048 to 65535
- cache_keys: bfloat16 [4096, 4096], P(('dp', 'context'), 'tensor'), parts along dimension 0, may hold values from -300 to 300
- cache_values: bfloat16 [4096, 4096], P(('dp', 'context'), 'tensor'), parts along dimension 0, may hold values from -6 to 6
Outputs:
- attended: bfloat16 [4096, 4096], P(('dp', 'context'), 'tensor'), parts along dimension 0
The draws below stay inside these ranges and needn't reach their ends.
There are 2 independent parts, one for each index of `dp`. The reference program is written for one: setup_inputs(seed, part) draws one part's arguments, and reference() takes and returns one part's arrays. A program takes and returns all parts, laid end to end along the dimension named above; an argument that names none is the same for every part. Nothing has to cross between parts.
All inputs are finite; a program needn't handle non-finite values.
Results may differ from the reference program's by a relative error of at most 0.04.
Values may be sent and summed in bfloat16 or wider, within the bound.
No kernel may reach another device: no remote copies, remote signals or barrier semaphores. Data moves between devices by JAX's collectives and lax.ppermute only.
A program may use at most 128 MiB of HBM per device.

```python
import math
import jax
import jax.numpy as jnp
from jax import lax

D = 4096
HEADS = 32
HEAD = 128
ORDER = 16
SHORT = 3
TOKENS = 2048
HISTORY = 2048
HD = 4096


def draw_cache_keys(key, part):
    drawn_keys = jnp.clip(jax.random.normal(key, (HISTORY, HD), jnp.float32), -5.0, 5.0)
    return drawn_keys.astype(jnp.bfloat16)


def level_of(key, dims, pieces, low, high):
    factor_of = 1.0
    for axis_at, parts in pieces:
        draws = jax.random.uniform(jax.random.fold_in(jax.random.fold_in(key, 6), axis_at), (parts,), jnp.float32, low / len(pieces), high / len(pieces))
        factor_of = factor_of * jnp.repeat(jnp.exp(draws), dims[axis_at] // parts).reshape((-1,) + (1,) * (len(dims) - 1 - axis_at))
    return factor_of


def normal_values(own_key, shape, width, limit, cuts=(), held_as=jnp.bfloat16):
    values = jax.random.normal(own_key, shape, jnp.float32) * width
    if len(cuts) > 0:
        values = level_of(own_key, shape, cuts, -0.22, 0.18) * values
    return jnp.clip(values, min=-limit, max=limit).astype(held_as)


def setup_inputs(seed: int = 0, part: int = 0) -> dict:
    keys = jax.random.split(jax.random.key(seed), 14)
    part_keys = jax.random.split(jax.random.fold_in(keys[13], part), 14)
    return {
        "streams": normal_values(part_keys[0], (TOKENS, 3, D), 1.0, 6.0, ((0, 16), (2, 4))),
        "stream_tail": normal_values(part_keys[1], (SHORT - 1, 3, D), 1.0, 6.0, ((2, 4),)),
        "short_taps": normal_values(keys[2], (SHORT, 3, D), 0.6, 3.0, ((2, 4),), jnp.float32),
        "decay_rates": jnp.clip(jnp.exp(math.log(0.05) - 6.015181 * jax.random.uniform(keys[3], (ORDER, D), jnp.float32) ** level_of(keys[3], (ORDER, D), ((1, 4),), -0.2, 0.2)), 0.00012207031, 0.05),
        "residues": normal_values(keys[4], (ORDER, D), ORDER ** -0.5, 1.5, ((1, 4),), jnp.float32),
        "hyena_state": normal_values(part_keys[5], (ORDER, D), 1.0, 6.0, ((1, 4),), jnp.float32),
        "skip_weight": normal_values(keys[6], (D,), 1.0, 4.0, ((0, 4),), jnp.float32),
        "residual": normal_values(part_keys[7], (TOKENS, D), 1.0, 6.0, ((0, 16), (1, 4))),
        "norm_gain": jnp.clip(1.0 + 0.18 * jax.random.normal(keys[8], (D,), jnp.float32), 0.1, 1.9),
        "qkv_weight": normal_values(keys[9], (D, 3, HD), D ** -0.5, 0.09375, ((2, 4),)),
        "start_offset": jax.random.randint(part_keys[10], (1,), HISTORY, 65536).astype(jnp.int32),
        "cache_keys": draw_cache_keys(jax.random.fold_in(jax.random.fold_in(keys[13], part), 71), part),
        "cache_values": normal_values(part_keys[12], (HISTORY, HD), 1.0, 6.0, ((0, 16), (1, 4))),
    }


ROTARY_BASE = 1000000.0
NORM_EPSILON = 1e-06

def short_filter(streams, stream_tail, short_taps):
    tap_count = short_taps.shape[0]
    token_count = streams.shape[0]
    extended = jnp.concatenate([stream_tail, streams], axis=0).astype(jnp.float32)
    filtered = jnp.zeros(streams.shape, jnp.float32)
    for step_back in range(tap_count):
        begin = tap_count - 1 - step_back
        filtered = filtered + short_taps[step_back][None] * extended[begin:begin + token_count]
    return filtered

def modal_filter(signal, decay_rates, residues, hyena_state):
    mode_decay = jnp.exp(-decay_rates)
    mode_gain = jnp.sqrt(1.0 - jnp.exp(-2.0 * decay_rates))

    def advance(carried, signal_row):
        carried = mode_decay * carried + mode_gain * signal_row[None, :]
        return (carried, lax.optimization_barrier(jnp.sum(residues * carried, axis=0)))
    unused_state, outputs = lax.scan(advance, hyena_state, signal)
    return outputs

def rotate(features, positions):
    half_width = features.shape[-1] // 2
    exponents = jnp.arange(half_width, dtype=jnp.float32) * (2.0 / features.shape[-1])
    frequency = jnp.exp(-math.log(ROTARY_BASE) * exponents)
    angles = positions[:, None] * frequency[None, :]
    cosine = jnp.cos(angles)[:, None, :]
    sine_values = jnp.sin(angles)[:, None, :]
    front = features[..., :half_width]
    back = features[..., half_width:]
    return jnp.concatenate([front * cosine - back * sine_values, back * cosine + front * sine_values], axis=-1)

def reference(streams, stream_tail, short_taps, decay_rates, residues, hyena_state, skip_weight, residual, norm_gain, qkv_weight, start_offset, cache_keys, cache_values):
    filtered = short_filter(streams, stream_tail, short_taps)
    product = (filtered[:, 0] * filtered[:, 2]).astype(jnp.bfloat16)
    long_out = modal_filter(product.astype(jnp.float32), decay_rates, residues, hyena_state).astype(jnp.bfloat16)
    hidden = (residual.astype(jnp.float32) + filtered[:, 1] * (long_out.astype(jnp.float32) + skip_weight[None, :] * product.astype(jnp.float32))).astype(jnp.bfloat16)
    hidden_float = hidden.astype(jnp.float32)
    mean_square = lax.optimization_barrier(jnp.mean(hidden_float * hidden_float, axis=1, keepdims=True))
    normed = (hidden_float * lax.rsqrt(mean_square + NORM_EPSILON) * norm_gain[None, :]).astype(jnp.bfloat16)
    projected = jnp.dot(normed, qkv_weight.reshape(D, 3 * HD), preferred_element_type=jnp.float32).reshape(TOKENS, 3, HEADS, HEAD)
    positions = (start_offset[0] + jnp.arange(TOKENS, dtype=jnp.int32)).astype(jnp.float32)
    queries = rotate(projected[:, 0], positions).astype(jnp.bfloat16)
    new_keys = rotate(projected[:, 1], positions).astype(jnp.bfloat16)
    new_values = projected[:, 2].astype(jnp.bfloat16)
    all_keys = jnp.concatenate([cache_keys.reshape(HISTORY, HEADS, HEAD), new_keys], axis=0)
    all_values = jnp.concatenate([cache_values.reshape(HISTORY, HEADS, HEAD), new_values], axis=0)
    key_index = jnp.arange(HISTORY + TOKENS, dtype=jnp.int32)
    query_index = jnp.arange(TOKENS, dtype=jnp.int32)
    visible = (key_index[None, :] < HISTORY) | (key_index[None, :] - HISTORY <= query_index[:, None])
    score_scale = 1.0 / math.sqrt(HEAD)

    def head_attend(operands):
        head_query, head_keys, head_values = operands
        scores = jnp.dot(head_query, head_keys.T, preferred_element_type=jnp.float32) * score_scale
        row_max = lax.optimization_barrier(jnp.max(jnp.where(visible, scores, -jnp.inf), axis=1, keepdims=True))
        weights = jnp.where(visible, jnp.exp(scores - row_max), 0.0).astype(jnp.bfloat16)
        weight_sum = lax.optimization_barrier(jnp.sum(weights.astype(jnp.float32), axis=1, keepdims=True))
        numerator = jnp.dot(weights, head_values, preferred_element_type=jnp.float32)
        return (numerator / weight_sum).astype(jnp.bfloat16)
    per_head = lax.map(head_attend, (queries.transpose(1, 0, 2), all_keys.transpose(1, 0, 2), all_values.transpose(1, 0, 2)))
    return per_head.transpose(1, 0, 2).reshape(TOKENS, HD)
```

```python
import math

import jax
import jax.numpy as jnp
from jax import lax
from jax.sharding import PartitionSpec as P

HEAD = 128


ROTARY_BASE = 1000000.0
NORM_EPSILON = 1e-06


def shifted(x, axis, by):
    devices = lax.axis_size(axis)
    pairs = [(i, i + by) for i in range(devices) if 0 <= i + by < devices]
    return lax.ppermute(x, axis, pairs)


def rotate(features, positions):
    half_width = features.shape[-1] // 2
    exponents = jnp.arange(half_width, dtype=jnp.float32) * (2.0 / features.shape[-1])
    frequency = jnp.exp(-math.log(ROTARY_BASE) * exponents)
    angles = positions[:, None] * frequency[None, :]
    cosine = jnp.cos(angles)[:, None, :]
    sine_values = jnp.sin(angles)[:, None, :]
    front = features[..., :half_width]
    back = features[..., half_width:]
    return jnp.concatenate(
        [front * cosine - back * sine_values, back * cosine + front * sine_values], axis=-1
    )


def modal_chunk(signal, mode_rates, mode_residues, hyena_state, device_index, devices):
    length, channels = signal.shape
    mode_count = mode_rates.shape[0]
    mode_gain = jnp.sqrt(1.0 - jnp.exp(-2.0 * mode_rates))
    offsets = jnp.arange(length, dtype=jnp.float32)[:, None, None]
    rising = jnp.exp(mode_rates[None] * offsets)
    lower_ones = (jnp.arange(length)[:, None] >= jnp.arange(length)[None, :]).astype(jnp.float32)
    scaled_terms = (rising * signal[:, None, :]).reshape(length, mode_count * channels)
    prefix_sums = jnp.dot(lower_ones, scaled_terms, precision=lax.Precision.HIGH).reshape(
        length, mode_count, channels
    )
    falling = jnp.exp(-mode_rates[None] * offsets)
    local_out = jnp.sum((mode_residues * mode_gain)[None] * falling * prefix_sums, axis=1)
    final_local = mode_gain * jnp.exp(-mode_rates * (length - 1)) * prefix_sums[-1]
    finals = lax.all_gather(final_local, "context", axis=0, tiled=False)
    source = jnp.arange(devices, dtype=jnp.int32)
    steps = (device_index - 1 - source).astype(jnp.float32)
    carry_weight = jnp.where(
        (source < device_index)[:, None, None],
        jnp.exp(-mode_rates[None] * (length * jnp.maximum(steps, 0.0))[:, None, None]),
        0.0,
    )
    incoming = jnp.exp(-mode_rates * (length * device_index.astype(jnp.float32))) * hyena_state
    incoming = incoming + jnp.sum(carry_weight * finals, axis=0)
    carried = jnp.sum(
        (mode_residues * incoming)[None] * jnp.exp(-mode_rates[None] * (offsets + 1.0)), axis=1
    )
    return local_out + carried


def shards(
    streams,
    stream_tail,
    short_taps,
    decay_rates,
    residues,
    hyena_state,
    skip_weight,
    residual,
    norm_gain,
    qkv_weight,
    start_offset,
    cache_keys,
    cache_values,
):
    row_count = streams.shape[0]
    tap_count = short_taps.shape[0]
    devices = lax.axis_size("context")
    device_index = lax.axis_index("context")
    head_width = qkv_weight.shape[2]
    heads_here = head_width // HEAD
    half_rows = row_count // 2

    def by_head(block):
        per_head = block.reshape(row_count, heads_here, HEAD).transpose(1, 0, 2)
        return jnp.repeat(per_head, devices // heads_here, axis=0)

    cache_k = lax.all_to_all(by_head(cache_keys), "context", 0, 0, tiled=True)
    cache_v = lax.all_to_all(by_head(cache_values), "context", 0, 0, tiled=True)

    before = shifted(streams[row_count - (tap_count - 1) :], "context", 1)
    before = jnp.where(device_index == 0, stream_tail, before)
    extended = jnp.concatenate([before, streams], axis=0).astype(jnp.float32)
    filtered = jnp.zeros(streams.shape, jnp.float32)
    for step_back in range(tap_count):
        begin = tap_count - 1 - step_back
        filtered = filtered + short_taps[step_back][None] * extended[begin : begin + row_count]
    product = (filtered[:, 0] * filtered[:, 2]).astype(jnp.bfloat16)
    long_out = modal_chunk(
        product.astype(jnp.float32), decay_rates, residues, hyena_state, device_index, devices
    ).astype(jnp.bfloat16)
    hidden = (
        residual.astype(jnp.float32)
        + filtered[:, 1]
        * (long_out.astype(jnp.float32) + skip_weight[None, :] * product.astype(jnp.float32))
    ).astype(jnp.bfloat16)
    gathered = lax.all_gather(hidden, "tensor", axis=1, tiled=True)
    hidden_float = gathered.astype(jnp.float32)
    mean_square = jnp.mean(hidden_float * hidden_float, axis=1, keepdims=True)
    normed = (hidden_float * lax.rsqrt(mean_square + NORM_EPSILON) * norm_gain[None, :]).astype(
        jnp.bfloat16
    )
    projected = jnp.einsum(
        "pk,kgn->pgn", normed, qkv_weight, preferred_element_type=jnp.float32
    ).reshape(row_count, 3, heads_here, HEAD)
    query_index = device_index * row_count + jnp.arange(row_count, dtype=jnp.int32)
    positions = (start_offset[0] + query_index).astype(jnp.float32)
    queries = rotate(projected[:, 0], positions).astype(jnp.bfloat16)
    new_keys = rotate(projected[:, 1], positions).astype(jnp.bfloat16)
    new_values = projected[:, 2].astype(jnp.bfloat16)

    new_k = lax.all_to_all(by_head(new_keys), "context", 0, 0, tiled=True)
    new_v = lax.all_to_all(by_head(new_values), "context", 0, 0, tiled=True)
    query_parts = (
        queries.reshape(2, half_rows, heads_here, HEAD)
        .transpose(2, 0, 1, 3)
        .reshape(devices, half_rows, HEAD)
    )
    my_queries = lax.all_to_all(query_parts, "context", 0, 0, tiled=True)

    hist_rows = cache_k.shape[0] * cache_k.shape[1]
    all_k = jnp.concatenate([cache_k.reshape(-1, HEAD), new_k.reshape(-1, HEAD)], axis=0)
    all_v = jnp.concatenate([cache_v.reshape(-1, HEAD), new_v.reshape(-1, HEAD)], axis=0)
    q_flat = my_queries.reshape(-1, HEAD)
    key_index = jnp.arange(all_k.shape[0], dtype=jnp.int32)
    key_pos = jnp.where(key_index < hist_rows, -1, key_index - hist_rows)
    src = jnp.arange(devices, dtype=jnp.int32)[:, None]
    row = jnp.arange(half_rows, dtype=jnp.int32)[None, :]
    query_pos = (src * row_count + (device_index % 2) * half_rows + row).reshape(-1)
    visible = key_pos[None, :] <= query_pos[:, None]
    score_scale = 1.0 / math.sqrt(HEAD)
    scores = (
        jnp.einsum("qd,kd->qk", q_flat, all_k, preferred_element_type=jnp.float32) * score_scale
    )
    row_max = jnp.max(jnp.where(visible, scores, -jnp.inf), axis=1, keepdims=True)
    weights = jnp.where(visible, jnp.exp(scores - row_max), 0.0).astype(jnp.bfloat16)
    weight_sum = jnp.sum(weights.astype(jnp.float32), axis=1, keepdims=True)
    numerator = jnp.dot(weights, all_v, preferred_element_type=jnp.float32)
    mine = (numerator / weight_sum).astype(jnp.bfloat16).reshape(devices, half_rows, HEAD)
    back = lax.all_to_all(mine, "context", 0, 0, tiled=True)
    attended = (
        back.reshape(heads_here, 2, half_rows, HEAD)
        .transpose(1, 2, 0, 3)
        .reshape(row_count, head_width)
    )
    return attended


def solution(mesh):
    placed = (
        P(("dp", "context"), None, "tensor"),
        P("dp", None, "tensor"),
        P(None, None, "tensor"),
        P(None, "tensor"),
        P(None, "tensor"),
        P("dp", "tensor"),
        P("tensor"),
        P(("dp", "context"), "tensor"),
        P(),
        P(None, None, "tensor"),
        P("dp"),
        P(("dp", "context"), "tensor"),
        P(("dp", "context"), "tensor"),
    )
    return jax.shard_map(
        shards,
        mesh=mesh,
        in_specs=placed,
        out_specs=P(("dp", "context"), "tensor"),
        check_vma=False,
    )
```

```python
import math

import jax
import jax.numpy as jnp
from jax import lax
from jax.sharding import PartitionSpec as P

HEAD = 128


ROTARY_BASE = 1000000.0
NORM_EPSILON = 1e-06


def shifted(x, axis, by):
    devices = lax.axis_size(axis)
    pairs = [(i, i + by) for i in range(devices) if 0 <= i + by < devices]
    return lax.ppermute(x, axis, pairs)


def rotate(features, positions):
    half_width = features.shape[-1] // 2
    exponents = jnp.arange(half_width, dtype=jnp.float32) * (2.0 / features.shape[-1])
    frequency = jnp.exp(-math.log(ROTARY_BASE) * exponents)
    angles = positions[:, None] * frequency[None, :]
    cosine = jnp.cos(angles)[:, None, :]
    sine_values = jnp.sin(angles)[:, None, :]
    front = features[..., :half_width]
    back = features[..., half_width:]
    return jnp.concatenate(
        [front * cosine - back * sine_values, back * cosine + front * sine_values], axis=-1
    )


def modal_chunk(signal, mode_rates, mode_residues, hyena_state, device_index, devices):
    length, channels = signal.shape
    mode_count = mode_rates.shape[0]
    mode_gain = jnp.sqrt(1.0 - jnp.exp(-2.0 * mode_rates))
    offsets = jnp.arange(length, dtype=jnp.float32)[:, None, None]
    rising = jnp.exp(mode_rates[None] * offsets)
    lower_ones = (jnp.arange(length)[:, None] >= jnp.arange(length)[None, :]).astype(jnp.float32)
    scaled_terms = (rising * signal[:, None, :]).reshape(length, mode_count * channels)
    prefix_sums = jnp.dot(lower_ones, scaled_terms, precision=lax.Precision.HIGH).reshape(
        length, mode_count, channels
    )
    falling = jnp.exp(-mode_rates[None] * offsets)
    local_out = jnp.sum((mode_residues * mode_gain)[None] * falling * prefix_sums, axis=1)
    final_local = mode_gain * jnp.exp(-mode_rates * (length - 1)) * prefix_sums[-1]
    carried_in = shifted(final_local, "context", 1)
    carried_in = jnp.where(device_index == 0, hyena_state, carried_in)
    span = 1
    while span < devices:
        carried_in = carried_in + jnp.exp(-mode_rates * (length * span)) * shifted(
            carried_in, "context", span
        )
        span *= 2
    incoming = carried_in
    carried = jnp.sum(
        (mode_residues * incoming)[None] * jnp.exp(-mode_rates[None] * (offsets + 1.0)), axis=1
    )
    return local_out + carried


def shards(
    streams,
    stream_tail,
    short_taps,
    decay_rates,
    residues,
    hyena_state,
    skip_weight,
    residual,
    norm_gain,
    qkv_weight,
    start_offset,
    cache_keys,
    cache_values,
):
    row_count = streams.shape[0]
    tap_count = short_taps.shape[0]
    devices = lax.axis_size("context")
    device_index = lax.axis_index("context")
    head_width = qkv_weight.shape[2]
    heads_here = head_width // HEAD
    half_rows = row_count // 2

    def by_head(block):
        per_head = block.reshape(row_count, heads_here, HEAD).transpose(1, 0, 2)
        return jnp.repeat(per_head, devices // heads_here, axis=0)

    cache_kv = lax.all_to_all(
        jnp.concatenate([by_head(cache_keys), by_head(cache_values)], axis=1),
        "context", 0, 0, tiled=True,
    )
    cache_k, cache_v = cache_kv[:, :row_count], cache_kv[:, row_count:]

    before = shifted(streams[row_count - (tap_count - 1) :], "context", 1)
    before = jnp.where(device_index == 0, stream_tail, before)
    extended = jnp.concatenate([before, streams], axis=0).astype(jnp.float32)
    filtered = jnp.zeros(streams.shape, jnp.float32)
    for step_back in range(tap_count):
        begin = tap_count - 1 - step_back
        filtered = filtered + short_taps[step_back][None] * extended[begin : begin + row_count]
    product = (filtered[:, 0] * filtered[:, 2]).astype(jnp.bfloat16)
    long_out = modal_chunk(
        product.astype(jnp.float32), decay_rates, residues, hyena_state, device_index, devices
    ).astype(jnp.bfloat16)
    hidden = (
        residual.astype(jnp.float32)
        + filtered[:, 1]
        * (long_out.astype(jnp.float32) + skip_weight[None, :] * product.astype(jnp.float32))
    ).astype(jnp.bfloat16)
    ways = lax.axis_size("tensor")
    pieces = [hidden] + [
        lax.ppermute(hidden, "tensor", [(i, (i - k) % ways) for i in range(ways)])
        for k in range(1, ways)
    ]
    gathered = jnp.roll(jnp.stack(pieces), lax.axis_index("tensor"), axis=0)
    gathered = gathered.transpose(1, 0, 2).reshape(row_count, ways * hidden.shape[1])
    hidden_float = gathered.astype(jnp.float32)
    mean_square = jnp.mean(hidden_float * hidden_float, axis=1, keepdims=True)
    normed = (hidden_float * lax.rsqrt(mean_square + NORM_EPSILON) * norm_gain[None, :]).astype(
        jnp.bfloat16
    )
    projected = jnp.einsum(
        "pk,kgn->pgn", normed, qkv_weight, preferred_element_type=jnp.float32
    ).reshape(row_count, 3, heads_here, HEAD)
    query_index = device_index * row_count + jnp.arange(row_count, dtype=jnp.int32)
    positions = (start_offset[0] + query_index).astype(jnp.float32)
    queries = rotate(projected[:, 0], positions).astype(jnp.bfloat16)
    new_keys = rotate(projected[:, 1], positions).astype(jnp.bfloat16)
    new_values = projected[:, 2].astype(jnp.bfloat16)

    query_parts = (
        queries.reshape(2, half_rows, heads_here, HEAD)
        .transpose(2, 0, 1, 3)
        .reshape(devices, half_rows, HEAD)
    )
    sent = lax.all_to_all(
        jnp.concatenate([query_parts, by_head(new_keys), by_head(new_values)], axis=1),
        "context", 0, 0, tiled=True,
    )
    my_queries = sent[:, :half_rows]
    new_k = sent[:, half_rows : half_rows + row_count]
    new_v = sent[:, half_rows + row_count :]

    hist_rows = cache_k.shape[0] * cache_k.shape[1]
    all_k = jnp.concatenate([cache_k.reshape(-1, HEAD), new_k.reshape(-1, HEAD)], axis=0)
    all_v = jnp.concatenate([cache_v.reshape(-1, HEAD), new_v.reshape(-1, HEAD)], axis=0)
    q_flat = my_queries.reshape(-1, HEAD)
    key_index = jnp.arange(all_k.shape[0], dtype=jnp.int32)
    key_pos = jnp.where(key_index < hist_rows, -1, key_index - hist_rows)
    src = jnp.arange(devices, dtype=jnp.int32)[:, None]
    row = jnp.arange(half_rows, dtype=jnp.int32)[None, :]
    query_pos = (src * row_count + (device_index % 2) * half_rows + row).reshape(-1)
    visible = key_pos[None, :] <= query_pos[:, None]
    score_scale = 1.0 / math.sqrt(HEAD)
    scores = (
        jnp.einsum("qd,kd->qk", q_flat, all_k, preferred_element_type=jnp.float32) * score_scale
    )
    row_max = jnp.max(jnp.where(visible, scores, -jnp.inf), axis=1, keepdims=True)
    weights = jnp.where(visible, jnp.exp(scores - row_max), 0.0).astype(jnp.bfloat16)
    weight_sum = jnp.sum(weights.astype(jnp.float32), axis=1, keepdims=True)
    numerator = jnp.dot(weights, all_v, preferred_element_type=jnp.float32)
    mine = (numerator / weight_sum).astype(jnp.bfloat16).reshape(devices, half_rows, HEAD)
    back = lax.all_to_all(mine, "context", 0, 0, tiled=True)
    attended = (
        back.reshape(heads_here, 2, half_rows, HEAD)
        .transpose(1, 2, 0, 3)
        .reshape(row_count, head_width)
    )
    return attended


def solution(mesh):
    placed = (
        P(("dp", "context"), None, "tensor"),
        P("dp", None, "tensor"),
        P(None, None, "tensor"),
        P(None, "tensor"),
        P(None, "tensor"),
        P("dp", "tensor"),
        P("tensor"),
        P(("dp", "context"), "tensor"),
        P(),
        P(None, None, "tensor"),
        P("dp"),
        P(("dp", "context"), "tensor"),
        P(("dp", "context"), "tensor"),
    )
    return jax.shard_map(
        shards,
        mesh=mesh,
        in_specs=placed,
        out_specs=P(("dp", "context"), "tensor"),
        check_vma=False,
    )
```

```python
import functools
import math

import jax
import jax.numpy as jnp
from jax import lax
from jax.experimental import pallas as pl
from jax.experimental.pallas import tpu as pltpu
from jax.sharding import PartitionSpec as P

HEAD = 128


ROTARY_BASE = 1000000.0
NORM_EPSILON = 1e-06


def shifted(x, axis, by):
    devices = lax.axis_size(axis)
    pairs = [(i, i + by) for i in range(devices) if 0 <= i + by < devices]
    return lax.ppermute(x, axis, pairs)


def rotate(features, positions):
    half_width = features.shape[-1] // 2
    exponents = jnp.arange(half_width, dtype=jnp.float32) * (2.0 / features.shape[-1])
    frequency = jnp.exp(-math.log(ROTARY_BASE) * exponents)
    angles = positions[:, None] * frequency[None, :]
    cosine = jnp.cos(angles)[:, None, :]
    sine_values = jnp.sin(angles)[:, None, :]
    front = features[..., :half_width]
    back = features[..., half_width:]
    return jnp.concatenate(
        [front * cosine - back * sine_values, back * cosine + front * sine_values], axis=-1
    )


def local_modes_kernel(x_ref, rate_ref, rg_ref, g_ref, out_ref, final_ref):
    length = x_ref.shape[0]
    mode_count = rate_ref.shape[0]
    x = x_ref[...]
    rows = lax.broadcasted_iota(jnp.int32, (length, length), 0)
    cols = lax.broadcasted_iota(jnp.int32, (length, length), 1)
    lower = (rows >= cols).astype(jnp.bfloat16)
    offsets = lax.broadcasted_iota(jnp.int32, (length, 1), 0).astype(jnp.float32)
    total = jnp.zeros(x.shape, jnp.float32)
    for m in range(mode_count):
        rate = rate_ref[m : m + 1, :]
        terms = jnp.exp(rate * offsets) * x
        high = terms.astype(jnp.bfloat16)
        low = (terms - high.astype(jnp.float32)).astype(jnp.bfloat16)
        prefix = jnp.dot(lower, high, preferred_element_type=jnp.float32) + jnp.dot(
            lower, low, preferred_element_type=jnp.float32
        )
        total = total + rg_ref[m : m + 1, :] * jnp.exp(-rate * offsets) * prefix
        final_ref[m : m + 1, :] = (
            g_ref[m : m + 1, :] * jnp.exp(-rate * (length - 1.0)) * prefix[length - 1 : length, :]
        )
    out_ref[...] = total


def carried_kernel(local_ref, rate_ref, weight_ref, out_ref):
    length = local_ref.shape[0]
    mode_count = rate_ref.shape[0]
    steps = lax.broadcasted_iota(jnp.int32, (length, 1), 0).astype(jnp.float32) + 1.0
    total = local_ref[...]
    for m in range(mode_count):
        total = total + weight_ref[m : m + 1, :] * jnp.exp(-rate_ref[m : m + 1, :] * steps)
    out_ref[...] = total.astype(out_ref.dtype)


def channel_blocks(kernel, inputs, outputs, block):
    channels = inputs[0].shape[1]
    specs = [pl.BlockSpec((a.shape[0], block), lambda j: (0, j)) for a in inputs]
    out_specs = [pl.BlockSpec((o.shape[0], block), lambda j: (0, j)) for o in outputs]
    return pl.pallas_call(
        kernel,
        grid=(channels // block,),
        in_specs=specs,
        out_specs=out_specs,
        out_shape=outputs,
    )(*inputs)


def modal_chunk(signal, mode_rates, mode_residues, hyena_state, device_index, devices):
    length, channels = signal.shape
    mode_gain = jnp.sqrt(1.0 - jnp.exp(-2.0 * mode_rates))
    local_out, final_local = channel_blocks(
        local_modes_kernel,
        [signal, mode_rates, mode_residues * mode_gain, mode_gain],
        [
            jax.ShapeDtypeStruct((length, channels), jnp.float32),
            jax.ShapeDtypeStruct(mode_rates.shape, jnp.float32),
        ],
        256,
    )
    finals = lax.all_gather(final_local, "context", axis=0, tiled=False)
    source = jnp.arange(devices, dtype=jnp.int32)
    steps = (device_index - 1 - source).astype(jnp.float32)
    carry_weight = jnp.where(
        (source < device_index)[:, None, None],
        jnp.exp(-mode_rates[None] * (length * jnp.maximum(steps, 0.0))[:, None, None]),
        0.0,
    )
    incoming = jnp.exp(-mode_rates * (length * device_index.astype(jnp.float32))) * hyena_state
    incoming = incoming + jnp.sum(carry_weight * finals, axis=0)
    (long_out,) = channel_blocks(
        carried_kernel,
        [local_out, mode_rates, mode_residues * incoming],
        [jax.ShapeDtypeStruct((length, channels), jnp.bfloat16)],
        256,
    )
    return long_out


def attention_kernel(scale, q_ref, k_ref, v_ref, qpos_ref, kpos_ref, out_ref):
    scores = (
        lax.dot_general(
            q_ref[...], k_ref[...], (((1,), (1,)), ((), ())), preferred_element_type=jnp.float32
        )
        * scale
    )
    visible = kpos_ref[...] <= qpos_ref[...]
    row_max = jnp.max(jnp.where(visible, scores, -jnp.inf), axis=1, keepdims=True)
    weights = jnp.where(visible, jnp.exp(scores - row_max), 0.0).astype(jnp.bfloat16)
    weight_sum = jnp.sum(weights.astype(jnp.float32), axis=1, keepdims=True)
    numerator = jnp.dot(weights, v_ref[...], preferred_element_type=jnp.float32)
    out_ref[...] = (numerator / weight_sum).astype(out_ref.dtype)


def attend(queries, keys, values, query_pos, key_pos, block=256):
    rows, width = queries.shape
    key_rows = keys.shape[0]
    return pl.pallas_call(
        functools.partial(attention_kernel, 1.0 / math.sqrt(width)),
        grid=(rows // block,),
        in_specs=[
            pl.BlockSpec((block, width), lambda i: (i, 0)),
            pl.BlockSpec((key_rows, width), lambda i: (0, 0)),
            pl.BlockSpec((key_rows, width), lambda i: (0, 0)),
            pl.BlockSpec((block, 1), lambda i: (i, 0)),
            pl.BlockSpec((1, key_rows), lambda i: (0, 0)),
        ],
        out_specs=pl.BlockSpec((block, width), lambda i: (i, 0)),
        out_shape=jax.ShapeDtypeStruct((rows, width), jnp.bfloat16),
        compiler_params=pltpu.CompilerParams(vmem_limit_bytes=48 * 1024 * 1024),
    )(queries, keys, values, query_pos.reshape(rows, 1), key_pos.reshape(1, key_rows))


def shards(
    streams,
    stream_tail,
    short_taps,
    decay_rates,
    residues,
    hyena_state,
    skip_weight,
    residual,
    norm_gain,
    qkv_weight,
    start_offset,
    cache_keys,
    cache_values,
):
    row_count = streams.shape[0]
    tap_count = short_taps.shape[0]
    devices = lax.axis_size("context")
    device_index = lax.axis_index("context")
    head_width = qkv_weight.shape[2]
    heads_here = head_width // HEAD
    half_rows = row_count // 2

    def by_head(block):
        per_head = block.reshape(row_count, heads_here, HEAD).transpose(1, 0, 2)
        return jnp.repeat(per_head, devices // heads_here, axis=0)

    cache_kv = lax.all_to_all(
        jnp.concatenate([by_head(cache_keys), by_head(cache_values)], axis=1),
        "context", 0, 0, tiled=True,
    )
    cache_k, cache_v = cache_kv[:, :row_count], cache_kv[:, row_count:]

    before = shifted(streams[row_count - (tap_count - 1) :], "context", 1)
    before = jnp.where(device_index == 0, stream_tail, before)
    extended = jnp.concatenate([before, streams], axis=0).astype(jnp.float32)
    filtered = jnp.zeros(streams.shape, jnp.float32)
    for step_back in range(tap_count):
        begin = tap_count - 1 - step_back
        filtered = filtered + short_taps[step_back][None] * extended[begin : begin + row_count]
    product = (filtered[:, 0] * filtered[:, 2]).astype(jnp.bfloat16)
    long_out = modal_chunk(
        product.astype(jnp.float32), decay_rates, residues, hyena_state, device_index, devices
    )
    hidden = (
        residual.astype(jnp.float32)
        + filtered[:, 1]
        * (long_out.astype(jnp.float32) + skip_weight[None, :] * product.astype(jnp.float32))
    ).astype(jnp.bfloat16)
    gathered = lax.all_gather(hidden, "tensor", axis=1, tiled=True)
    hidden_float = gathered.astype(jnp.float32)
    mean_square = jnp.mean(hidden_float * hidden_float, axis=1, keepdims=True)
    normed = (hidden_float * lax.rsqrt(mean_square + NORM_EPSILON) * norm_gain[None, :]).astype(
        jnp.bfloat16
    )
    projected = jnp.einsum(
        "pk,kgn->pgn", normed, qkv_weight, preferred_element_type=jnp.float32
    ).reshape(row_count, 3, heads_here, HEAD)
    query_index = device_index * row_count + jnp.arange(row_count, dtype=jnp.int32)
    positions = (start_offset[0] + query_index).astype(jnp.float32)
    queries = rotate(projected[:, 0], positions).astype(jnp.bfloat16)
    new_keys = rotate(projected[:, 1], positions).astype(jnp.bfloat16)
    new_values = projected[:, 2].astype(jnp.bfloat16)

    query_parts = (
        queries.reshape(2, half_rows, heads_here, HEAD)
        .transpose(2, 0, 1, 3)
        .reshape(devices, half_rows, HEAD)
    )
    sent = lax.all_to_all(
        jnp.concatenate([query_parts, by_head(new_keys), by_head(new_values)], axis=1),
        "context", 0, 0, tiled=True,
    )
    my_queries = sent[:, :half_rows]
    new_k = sent[:, half_rows : half_rows + row_count]
    new_v = sent[:, half_rows + row_count :]

    hist_rows = cache_k.shape[0] * cache_k.shape[1]
    all_k = jnp.concatenate([cache_k.reshape(-1, HEAD), new_k.reshape(-1, HEAD)], axis=0)
    all_v = jnp.concatenate([cache_v.reshape(-1, HEAD), new_v.reshape(-1, HEAD)], axis=0)
    q_flat = my_queries.reshape(-1, HEAD)
    key_index = jnp.arange(all_k.shape[0], dtype=jnp.int32)
    key_pos = jnp.where(key_index < hist_rows, -1, key_index - hist_rows)
    src = jnp.arange(devices, dtype=jnp.int32)[:, None]
    row = jnp.arange(half_rows, dtype=jnp.int32)[None, :]
    query_pos = (src * row_count + (device_index % 2) * half_rows + row).reshape(-1)
    mine = attend(q_flat, all_k, all_v, query_pos, key_pos).reshape(devices, half_rows, HEAD)
    back = lax.all_to_all(mine, "context", 0, 0, tiled=True)
    attended = (
        back.reshape(heads_here, 2, half_rows, HEAD)
        .transpose(1, 2, 0, 3)
        .reshape(row_count, head_width)
    )
    return attended


def solution(mesh):
    placed = (
        P(("dp", "context"), None, "tensor"),
        P("dp", None, "tensor"),
        P(None, None, "tensor"),
        P(None, "tensor"),
        P(None, "tensor"),
        P("dp", "tensor"),
        P("tensor"),
        P(("dp", "context"), "tensor"),
        P(),
        P(None, None, "tensor"),
        P("dp"),
        P(("dp", "context"), "tensor"),
        P(("dp", "context"), "tensor"),
    )
    return jax.shard_map(
        shards,
        mesh=mesh,
        in_specs=placed,
        out_specs=P(("dp", "context"), "tensor"),
        check_vma=False,
    )
```

```python
import functools
import math

import jax
import jax.numpy as jnp
from jax import lax
from jax.experimental import pallas as pl
from jax.experimental.pallas import tpu as pltpu
from jax.sharding import PartitionSpec as P

HEAD = 128


ROTARY_BASE = 1000000.0
NORM_EPSILON = 1e-06


def shifted(x, axis, by):
    devices = lax.axis_size(axis)
    pairs = [(i, i + by) for i in range(devices) if 0 <= i + by < devices]
    return lax.ppermute(x, axis, pairs)


def rotate(features, positions):
    half_width = features.shape[-1] // 2
    exponents = jnp.arange(half_width, dtype=jnp.float32) * (2.0 / features.shape[-1])
    frequency = jnp.exp(-math.log(ROTARY_BASE) * exponents)
    angles = positions[:, None] * frequency[None, :]
    cosine = jnp.cos(angles)[:, None, :]
    sine_values = jnp.sin(angles)[:, None, :]
    front = features[..., :half_width]
    back = features[..., half_width:]
    return jnp.concatenate(
        [front * cosine - back * sine_values, back * cosine + front * sine_values], axis=-1
    )


def local_modes_kernel(x_ref, rate_ref, rg_ref, g_ref, out_ref, final_ref):
    length = x_ref.shape[0]
    mode_count = rate_ref.shape[0]
    x = x_ref[...]
    rows = lax.broadcasted_iota(jnp.int32, (length, length), 0)
    cols = lax.broadcasted_iota(jnp.int32, (length, length), 1)
    lower = (rows >= cols).astype(jnp.bfloat16)
    offsets = lax.broadcasted_iota(jnp.int32, (length, 1), 0).astype(jnp.float32)
    total = jnp.zeros(x.shape, jnp.float32)
    for m in range(mode_count):
        rate = rate_ref[m : m + 1, :]
        terms = jnp.exp(rate * offsets) * x
        high = terms.astype(jnp.bfloat16)
        low = (terms - high.astype(jnp.float32)).astype(jnp.bfloat16)
        prefix = jnp.dot(lower, high, preferred_element_type=jnp.float32) + jnp.dot(
            lower, low, preferred_element_type=jnp.float32
        )
        total = total + rg_ref[m : m + 1, :] * jnp.exp(-rate * offsets) * prefix
        final_ref[m : m + 1, :] = (
            g_ref[m : m + 1, :] * jnp.exp(-rate * (length - 1.0)) * prefix[length - 1 : length, :]
        )
    out_ref[...] = total


def carried_kernel(local_ref, rate_ref, weight_ref, out_ref):
    length = local_ref.shape[0]
    mode_count = rate_ref.shape[0]
    steps = lax.broadcasted_iota(jnp.int32, (length, 1), 0).astype(jnp.float32) + 1.0
    total = local_ref[...]
    for m in range(mode_count):
        total = total + weight_ref[m : m + 1, :] * jnp.exp(-rate_ref[m : m + 1, :] * steps)
    out_ref[...] = total.astype(out_ref.dtype)


def channel_blocks(kernel, inputs, outputs, block):
    channels = inputs[0].shape[1]
    specs = [pl.BlockSpec((a.shape[0], block), lambda j: (0, j)) for a in inputs]
    out_specs = [pl.BlockSpec((o.shape[0], block), lambda j: (0, j)) for o in outputs]
    return pl.pallas_call(
        kernel,
        grid=(channels // block,),
        in_specs=specs,
        out_specs=out_specs,
        out_shape=outputs,
    )(*inputs)


def modal_chunk(signal, mode_rates, mode_residues, hyena_state, device_index, devices):
    length, channels = signal.shape
    mode_gain = jnp.sqrt(1.0 - jnp.exp(-2.0 * mode_rates))
    local_out, final_local = channel_blocks(
        local_modes_kernel,
        [signal, mode_rates, mode_residues * mode_gain, mode_gain],
        [
            jax.ShapeDtypeStruct((length, channels), jnp.float32),
            jax.ShapeDtypeStruct(mode_rates.shape, jnp.float32),
        ],
        256,
    )
    finals = lax.all_to_all(
        jnp.broadcast_to(final_local[None], (devices,) + final_local.shape),
        "context", 0, 0, tiled=True,
    )
    source = jnp.arange(devices, dtype=jnp.int32)
    steps = (device_index - 1 - source).astype(jnp.float32)
    carry_weight = jnp.where(
        (source < device_index)[:, None, None],
        jnp.exp(-mode_rates[None] * (length * jnp.maximum(steps, 0.0))[:, None, None]),
        0.0,
    )
    incoming = jnp.exp(-mode_rates * (length * device_index.astype(jnp.float32))) * hyena_state
    incoming = incoming + jnp.sum(carry_weight * finals, axis=0)
    (long_out,) = channel_blocks(
        carried_kernel,
        [local_out, mode_rates, mode_residues * incoming],
        [jax.ShapeDtypeStruct((length, channels), jnp.bfloat16)],
        256,
    )
    return long_out


def attention_kernel(scale, q_ref, k_ref, v_ref, qpos_ref, kpos_ref, out_ref):
    scores = (
        lax.dot_general(
            q_ref[...], k_ref[...], (((1,), (1,)), ((), ())), preferred_element_type=jnp.float32
        )
        * scale
    )
    visible = kpos_ref[...] <= qpos_ref[...]
    row_max = jnp.max(jnp.where(visible, scores, -jnp.inf), axis=1, keepdims=True)
    weights = jnp.where(visible, jnp.exp(scores - row_max), 0.0).astype(jnp.bfloat16)
    weight_sum = jnp.sum(weights.astype(jnp.float32), axis=1, keepdims=True)
    numerator = jnp.dot(weights, v_ref[...], preferred_element_type=jnp.float32)
    out_ref[...] = (numerator / weight_sum).astype(out_ref.dtype)


def attend(queries, keys, values, query_pos, key_pos, block=256):
    rows, width = queries.shape
    key_rows = keys.shape[0]
    return pl.pallas_call(
        functools.partial(attention_kernel, 1.0 / math.sqrt(width)),
        grid=(rows // block,),
        in_specs=[
            pl.BlockSpec((block, width), lambda i: (i, 0)),
            pl.BlockSpec((key_rows, width), lambda i: (0, 0)),
            pl.BlockSpec((key_rows, width), lambda i: (0, 0)),
            pl.BlockSpec((block, 1), lambda i: (i, 0)),
            pl.BlockSpec((1, key_rows), lambda i: (0, 0)),
        ],
        out_specs=pl.BlockSpec((block, width), lambda i: (i, 0)),
        out_shape=jax.ShapeDtypeStruct((rows, width), jnp.bfloat16),
        compiler_params=pltpu.CompilerParams(vmem_limit_bytes=48 * 1024 * 1024),
    )(queries, keys, values, query_pos.reshape(rows, 1), key_pos.reshape(1, key_rows))


def project_kernel(x_ref, w_ref, out_ref):
    out_ref[...] = jnp.dot(x_ref[...], w_ref[...], preferred_element_type=jnp.float32)


def project(x, w, block=512):
    rows, depth = x.shape
    groups, _, width = w.shape
    return pl.pallas_call(
        project_kernel,
        grid=(groups, width // block),
        in_specs=[
            pl.BlockSpec((rows, depth), lambda g, j: (0, 0)),
            pl.BlockSpec((None, depth, block), lambda g, j: (g, 0, j)),
        ],
        out_specs=pl.BlockSpec((None, rows, block), lambda g, j: (g, 0, j)),
        out_shape=jax.ShapeDtypeStruct((groups, rows, width), jnp.float32),
        compiler_params=pltpu.CompilerParams(vmem_limit_bytes=48 * 1024 * 1024),
        cost_estimate=pl.CostEstimate(
            flops=2 * rows * depth * width * groups,
            bytes_accessed=2 * (rows * depth + groups * depth * width) + 4 * groups * rows * width,
            transcendentals=0,
        ),
    )(x, w)


def shards(
    streams,
    stream_tail,
    short_taps,
    decay_rates,
    residues,
    hyena_state,
    skip_weight,
    residual,
    norm_gain,
    qkv_weight,
    start_offset,
    cache_keys,
    cache_values,
):
    row_count = streams.shape[0]
    tap_count = short_taps.shape[0]
    devices = lax.axis_size("context")
    device_index = lax.axis_index("context")
    head_width = qkv_weight.shape[2]
    heads_here = head_width // HEAD
    half_rows = row_count // 2

    def by_head(block):
        per_head = block.reshape(row_count, heads_here, HEAD).transpose(1, 0, 2)
        return jnp.repeat(per_head, devices // heads_here, axis=0)

    cache_kv = lax.all_to_all(
        jnp.concatenate([by_head(cache_keys), by_head(cache_values)], axis=1),
        "context", 0, 0, tiled=True,
    )
    cache_k, cache_v = cache_kv[:, :row_count], cache_kv[:, row_count:]

    before = shifted(streams[row_count - (tap_count - 1) :], "context", 1)
    before = jnp.where(device_index == 0, stream_tail, before)
    extended = jnp.concatenate([before, streams], axis=0).astype(jnp.float32)
    filtered = jnp.zeros(streams.shape, jnp.float32)
    for step_back in range(tap_count):
        begin = tap_count - 1 - step_back
        filtered = filtered + short_taps[step_back][None] * extended[begin : begin + row_count]
    product = (filtered[:, 0] * filtered[:, 2]).astype(jnp.bfloat16)
    long_out = modal_chunk(
        product.astype(jnp.float32), decay_rates, residues, hyena_state, device_index, devices
    )
    hidden = (
        residual.astype(jnp.float32)
        + filtered[:, 1]
        * (long_out.astype(jnp.float32) + skip_weight[None, :] * product.astype(jnp.float32))
    ).astype(jnp.bfloat16)
    ways = lax.axis_size("tensor")
    gathered = lax.all_to_all(
        jnp.broadcast_to(hidden[None], (ways,) + hidden.shape), "tensor", 0, 0, tiled=True
    )
    gathered = gathered.transpose(1, 0, 2).reshape(row_count, ways * hidden.shape[1])
    hidden_float = gathered.astype(jnp.float32)
    mean_square = jnp.mean(hidden_float * hidden_float, axis=1, keepdims=True)
    normed = (hidden_float * lax.rsqrt(mean_square + NORM_EPSILON) * norm_gain[None, :]).astype(
        jnp.bfloat16
    )
    projected = (
        project(normed, qkv_weight.transpose(1, 0, 2))
        .transpose(1, 0, 2)
        .reshape(row_count, 3, heads_here, HEAD)
    )
    query_index = device_index * row_count + jnp.arange(row_count, dtype=jnp.int32)
    positions = (start_offset[0] + query_index).astype(jnp.float32)
    queries = rotate(projected[:, 0], positions).astype(jnp.bfloat16)
    new_keys = rotate(projected[:, 1], positions).astype(jnp.bfloat16)
    new_values = projected[:, 2].astype(jnp.bfloat16)

    query_parts = (
        queries.reshape(2, half_rows, heads_here, HEAD)
        .transpose(2, 0, 1, 3)
        .reshape(devices, half_rows, HEAD)
    )
    sent = lax.all_to_all(
        jnp.concatenate([query_parts, by_head(new_keys), by_head(new_values)], axis=1),
        "context", 0, 0, tiled=True,
    )
    my_queries = sent[:, :half_rows]
    new_k = sent[:, half_rows : half_rows + row_count]
    new_v = sent[:, half_rows + row_count :]

    hist_rows = cache_k.shape[0] * cache_k.shape[1]
    all_k = jnp.concatenate([cache_k.reshape(-1, HEAD), new_k.reshape(-1, HEAD)], axis=0)
    all_v = jnp.concatenate([cache_v.reshape(-1, HEAD), new_v.reshape(-1, HEAD)], axis=0)
    q_flat = my_queries.reshape(-1, HEAD)
    key_index = jnp.arange(all_k.shape[0], dtype=jnp.int32)
    key_pos = jnp.where(key_index < hist_rows, -1, key_index - hist_rows)
    src = jnp.arange(devices, dtype=jnp.int32)[:, None]
    row = jnp.arange(half_rows, dtype=jnp.int32)[None, :]
    query_pos = (src * row_count + (device_index % 2) * half_rows + row).reshape(-1)
    mine = attend(q_flat, all_k, all_v, query_pos, key_pos).reshape(devices, half_rows, HEAD)
    back = lax.all_to_all(mine, "context", 0, 0, tiled=True)
    attended = (
        back.reshape(heads_here, 2, half_rows, HEAD)
        .transpose(1, 2, 0, 3)
        .reshape(row_count, head_width)
    )
    return attended


def solution(mesh):
    placed = (
        P(("dp", "context"), None, "tensor"),
        P("dp", None, "tensor"),
        P(None, None, "tensor"),
        P(None, "tensor"),
        P(None, "tensor"),
        P("dp", "tensor"),
        P("tensor"),
        P(("dp", "context"), "tensor"),
        P(),
        P(None, None, "tensor"),
        P("dp"),
        P(("dp", "context"), "tensor"),
        P(("dp", "context"), "tensor"),
    )
    return jax.shard_map(
        shards,
        mesh=mesh,
        in_specs=placed,
        out_specs=P(("dp", "context"), "tensor"),
        check_vma=False,
    )
```

```python
import functools
import math

import jax
import jax.numpy as jnp
from jax import lax
from jax.experimental import pallas as pl
from jax.experimental.pallas import tpu as pltpu
from jax.sharding import PartitionSpec as P

HEAD = 128


ROTARY_BASE = 1000000.0
NORM_EPSILON = 1e-06


def shifted(x, axis, by):
    devices = lax.axis_size(axis)
    pairs = [(i, i + by) for i in range(devices) if 0 <= i + by < devices]
    return lax.ppermute(x, axis, pairs)


def rotate(features, positions):
    half_width = features.shape[-1] // 2
    exponents = jnp.arange(half_width, dtype=jnp.float32) * (2.0 / features.shape[-1])
    frequency = jnp.exp(-math.log(ROTARY_BASE) * exponents)
    angles = positions[:, None] * frequency[None, :]
    cosine = jnp.cos(angles)[:, None, :]
    sine_values = jnp.sin(angles)[:, None, :]
    front = features[..., :half_width]
    back = features[..., half_width:]
    return jnp.concatenate(
        [front * cosine - back * sine_values, back * cosine + front * sine_values], axis=-1
    )


def local_modes_kernel(x_ref, rate_ref, rg_ref, g_ref, out_ref, final_ref):
    length = x_ref.shape[0]
    mode_count = rate_ref.shape[0]
    x = x_ref[...]
    rows = lax.broadcasted_iota(jnp.int32, (length, length), 0)
    cols = lax.broadcasted_iota(jnp.int32, (length, length), 1)
    lower = (rows >= cols).astype(jnp.bfloat16)
    offsets = lax.broadcasted_iota(jnp.int32, (length, 1), 0).astype(jnp.float32)
    total = jnp.zeros(x.shape, jnp.float32)
    for m in range(mode_count):
        rate = rate_ref[m : m + 1, :]
        terms = jnp.exp(rate * offsets) * x
        high = terms.astype(jnp.bfloat16)
        low = (terms - high.astype(jnp.float32)).astype(jnp.bfloat16)
        prefix = jnp.dot(lower, high, preferred_element_type=jnp.float32) + jnp.dot(
            lower, low, preferred_element_type=jnp.float32
        )
        total = total + rg_ref[m : m + 1, :] * jnp.exp(-rate * offsets) * prefix
        final_ref[m : m + 1, :] = (
            g_ref[m : m + 1, :] * jnp.exp(-rate * (length - 1.0)) * prefix[length - 1 : length, :]
        )
    out_ref[...] = total


def carried_kernel(local_ref, rate_ref, weight_ref, out_ref):
    length = local_ref.shape[0]
    mode_count = rate_ref.shape[0]
    steps = lax.broadcasted_iota(jnp.int32, (length, 1), 0).astype(jnp.float32) + 1.0
    total = local_ref[...]
    for m in range(mode_count):
        total = total + weight_ref[m : m + 1, :] * jnp.exp(-rate_ref[m : m + 1, :] * steps)
    out_ref[...] = total.astype(out_ref.dtype)


def channel_blocks(kernel, inputs, outputs, block):
    channels = inputs[0].shape[1]
    specs = [pl.BlockSpec((a.shape[0], block), lambda j: (0, j)) for a in inputs]
    out_specs = [pl.BlockSpec((o.shape[0], block), lambda j: (0, j)) for o in outputs]
    return pl.pallas_call(
        kernel,
        grid=(channels // block,),
        in_specs=specs,
        out_specs=out_specs,
        out_shape=outputs,
    )(*inputs)


def modal_chunk(signal, mode_rates, mode_residues, hyena_state, device_index, devices):
    length, channels = signal.shape
    mode_gain = jnp.sqrt(1.0 - jnp.exp(-2.0 * mode_rates))
    local_out, final_local = channel_blocks(
        local_modes_kernel,
        [signal, mode_rates, mode_residues * mode_gain, mode_gain],
        [
            jax.ShapeDtypeStruct((length, channels), jnp.float32),
            jax.ShapeDtypeStruct(mode_rates.shape, jnp.float32),
        ],
        256,
    )
    finals = lax.all_to_all(
        jnp.broadcast_to(final_local.astype(jnp.bfloat16)[None], (devices,) + final_local.shape),
        "context", 0, 0, tiled=True,
    ).astype(jnp.float32)
    source = jnp.arange(devices, dtype=jnp.int32)
    steps = (device_index - 1 - source).astype(jnp.float32)
    carry_weight = jnp.where(
        (source < device_index)[:, None, None],
        jnp.exp(-mode_rates[None] * (length * jnp.maximum(steps, 0.0))[:, None, None]),
        0.0,
    )
    incoming = jnp.exp(-mode_rates * (length * device_index.astype(jnp.float32))) * hyena_state
    incoming = incoming + jnp.sum(carry_weight * finals, axis=0)
    (long_out,) = channel_blocks(
        carried_kernel,
        [local_out, mode_rates, mode_residues * incoming],
        [jax.ShapeDtypeStruct((length, channels), jnp.bfloat16)],
        256,
    )
    return long_out


def attention_kernel(scale, q_ref, k_ref, v_ref, qpos_ref, kpos_ref, out_ref):
    scores = (
        lax.dot_general(
            q_ref[...], k_ref[...], (((1,), (1,)), ((), ())), preferred_element_type=jnp.float32
        )
        * scale
    )
    visible = kpos_ref[...] <= qpos_ref[...]
    row_max = jnp.max(jnp.where(visible, scores, -jnp.inf), axis=1, keepdims=True)
    weights = jnp.where(visible, jnp.exp(scores - row_max), 0.0).astype(jnp.bfloat16)
    weight_sum = jnp.sum(weights.astype(jnp.float32), axis=1, keepdims=True)
    numerator = jnp.dot(weights, v_ref[...], preferred_element_type=jnp.float32)
    out_ref[...] = (numerator / weight_sum).astype(out_ref.dtype)


def attend(queries, keys, values, query_pos, key_pos, block=256):
    rows, width = queries.shape
    key_rows = keys.shape[0]
    return pl.pallas_call(
        functools.partial(attention_kernel, 1.0 / math.sqrt(width)),
        grid=(rows // block,),
        in_specs=[
            pl.BlockSpec((block, width), lambda i: (i, 0)),
            pl.BlockSpec((key_rows, width), lambda i: (0, 0)),
            pl.BlockSpec((key_rows, width), lambda i: (0, 0)),
            pl.BlockSpec((block, 1), lambda i: (i, 0)),
            pl.BlockSpec((1, key_rows), lambda i: (0, 0)),
        ],
        out_specs=pl.BlockSpec((block, width), lambda i: (i, 0)),
        out_shape=jax.ShapeDtypeStruct((rows, width), jnp.bfloat16),
        compiler_params=pltpu.CompilerParams(vmem_limit_bytes=48 * 1024 * 1024),
    )(queries, keys, values, query_pos.reshape(rows, 1), key_pos.reshape(1, key_rows))


def project_kernel(x_ref, w_ref, out_ref):
    out_ref[...] = jnp.dot(x_ref[...], w_ref[...], preferred_element_type=jnp.float32)


def project(x, w, block=512):
    rows, depth = x.shape
    groups, _, width = w.shape
    return pl.pallas_call(
        project_kernel,
        grid=(groups, width // block),
        in_specs=[
            pl.BlockSpec((rows, depth), lambda g, j: (0, 0)),
            pl.BlockSpec((None, depth, block), lambda g, j: (g, 0, j)),
        ],
        out_specs=pl.BlockSpec((None, rows, block), lambda g, j: (g, 0, j)),
        out_shape=jax.ShapeDtypeStruct((groups, rows, width), jnp.float32),
        compiler_params=pltpu.CompilerParams(vmem_limit_bytes=48 * 1024 * 1024),
        cost_estimate=pl.CostEstimate(
            flops=2 * rows * depth * width * groups,
            bytes_accessed=2 * (rows * depth + groups * depth * width) + 4 * groups * rows * width,
            transcendentals=0,
        ),
    )(x, w)


def shards(
    streams,
    stream_tail,
    short_taps,
    decay_rates,
    residues,
    hyena_state,
    skip_weight,
    residual,
    norm_gain,
    qkv_weight,
    start_offset,
    cache_keys,
    cache_values,
):
    row_count = streams.shape[0]
    tap_count = short_taps.shape[0]
    devices = lax.axis_size("context")
    device_index = lax.axis_index("context")
    head_width = qkv_weight.shape[2]
    heads_here = head_width // HEAD
    half_rows = row_count // 2

    def by_head(block):
        per_head = block.reshape(row_count, heads_here, HEAD).transpose(1, 0, 2)
        return jnp.repeat(per_head, devices // heads_here, axis=0)

    cache_kv = lax.all_to_all(
        jnp.concatenate([by_head(cache_keys), by_head(cache_values)], axis=1),
        "context", 0, 0, tiled=True,
    )
    cache_k, cache_v = cache_kv[:, :row_count], cache_kv[:, row_count:]

    before = shifted(streams[row_count - (tap_count - 1) :], "context", 1)
    before = jnp.where(device_index == 0, stream_tail, before)
    extended = jnp.concatenate([before, streams], axis=0).astype(jnp.float32)
    filtered = jnp.zeros(streams.shape, jnp.float32)
    for step_back in range(tap_count):
        begin = tap_count - 1 - step_back
        filtered = filtered + short_taps[step_back][None] * extended[begin : begin + row_count]
    product = (filtered[:, 0] * filtered[:, 2]).astype(jnp.bfloat16)
    long_out = modal_chunk(
        product.astype(jnp.float32), decay_rates, residues, hyena_state, device_index, devices
    )
    hidden = (
        residual.astype(jnp.float32)
        + filtered[:, 1]
        * (long_out.astype(jnp.float32) + skip_weight[None, :] * product.astype(jnp.float32))
    ).astype(jnp.bfloat16)
    ways = lax.axis_size("tensor")
    gathered = lax.all_to_all(
        jnp.broadcast_to(hidden[None], (ways,) + hidden.shape), "tensor", 0, 0, tiled=True
    )
    gathered = gathered.transpose(1, 0, 2).reshape(row_count, ways * hidden.shape[1])
    hidden_float = gathered.astype(jnp.float32)
    mean_square = jnp.mean(hidden_float * hidden_float, axis=1, keepdims=True)
    normed = (hidden_float * lax.rsqrt(mean_square + NORM_EPSILON) * norm_gain[None, :]).astype(
        jnp.bfloat16
    )
    projected = (
        project(normed, qkv_weight.transpose(1, 0, 2))
        .transpose(1, 0, 2)
        .reshape(row_count, 3, heads_here, HEAD)
    )
    query_index = device_index * row_count + jnp.arange(row_count, dtype=jnp.int32)
    positions = (start_offset[0] + query_index).astype(jnp.float32)
    queries = rotate(projected[:, 0], positions).astype(jnp.bfloat16)
    new_keys = rotate(projected[:, 1], positions).astype(jnp.bfloat16)
    new_values = projected[:, 2].astype(jnp.bfloat16)

    query_parts = (
        queries.reshape(2, half_rows, heads_here, HEAD)
        .transpose(2, 0, 1, 3)
        .reshape(devices, half_rows, HEAD)
    )
    sent = lax.all_to_all(
        jnp.concatenate([query_parts, by_head(new_keys), by_head(new_values)], axis=1),
        "context", 0, 0, tiled=True,
    )
    my_queries = sent[:, :half_rows]
    new_k = sent[:, half_rows : half_rows + row_count]
    new_v = sent[:, half_rows + row_count :]

    hist_rows = cache_k.shape[0] * cache_k.shape[1]
    all_k = jnp.concatenate([cache_k.reshape(-1, HEAD), new_k.reshape(-1, HEAD)], axis=0)
    all_v = jnp.concatenate([cache_v.reshape(-1, HEAD), new_v.reshape(-1, HEAD)], axis=0)
    q_flat = my_queries.reshape(-1, HEAD)
    key_index = jnp.arange(all_k.shape[0], dtype=jnp.int32)
    key_pos = jnp.where(key_index < hist_rows, -1, key_index - hist_rows)
    src = jnp.arange(devices, dtype=jnp.int32)[:, None]
    row = jnp.arange(half_rows, dtype=jnp.int32)[None, :]
    query_pos = (src * row_count + (device_index % 2) * half_rows + row).reshape(-1)
    quarter = half_rows // 2
    q_split = q_flat.reshape(devices, 2, quarter, HEAD)
    pos_split = query_pos.reshape(devices, 2, quarter)
    halves = []
    for h in range(2):
        mine = attend(
            q_split[:, h].reshape(-1, HEAD), all_k, all_v, pos_split[:, h].reshape(-1), key_pos
        ).reshape(devices, quarter, HEAD)
        halves.append(lax.all_to_all(mine, "context", 0, 0, tiled=True))
    back = jnp.stack(halves, axis=1).reshape(devices, half_rows, HEAD)
    attended = (
        back.reshape(heads_here, 2, half_rows, HEAD)
        .transpose(1, 2, 0, 3)
        .reshape(row_count, head_width)
    )
    return attended


def solution(mesh):
    placed = (
        P(("dp", "context"), None, "tensor"),
        P("dp", None, "tensor"),
        P(None, None, "tensor"),
        P(None, "tensor"),
        P(None, "tensor"),
        P("dp", "tensor"),
        P("tensor"),
        P(("dp", "context"), "tensor"),
        P(),
        P(None, None, "tensor"),
        P("dp"),
        P(("dp", "context"), "tensor"),
        P(("dp", "context"), "tensor"),
    )
    return jax.shard_map(
        shards,
        mesh=mesh,
        in_specs=placed,
        out_specs=P(("dp", "context"), "tensor"),
        check_vma=False,
    )
```

```python
import functools
import math

import jax
import jax.numpy as jnp
from jax import lax
from jax.experimental import pallas as pl
from jax.experimental.pallas import tpu as pltpu
from jax.sharding import PartitionSpec as P

HEAD = 128


ROTARY_BASE = 1000000.0
NORM_EPSILON = 1e-06


def shifted(x, axis, by):
    devices = lax.axis_size(axis)
    pairs = [(i, i + by) for i in range(devices) if 0 <= i + by < devices]
    return lax.ppermute(x, axis, pairs)


def rotate(features, positions):
    half_width = features.shape[-1] // 2
    exponents = jnp.arange(half_width, dtype=jnp.float32) * (2.0 / features.shape[-1])
    frequency = jnp.exp(-math.log(ROTARY_BASE) * exponents)
    angles = positions[:, None] * frequency[None, :]
    cosine = jnp.cos(angles)[:, None, :]
    sine_values = jnp.sin(angles)[:, None, :]
    front = features[..., :half_width]
    back = features[..., half_width:]
    return jnp.concatenate(
        [front * cosine - back * sine_values, back * cosine + front * sine_values], axis=-1
    )


def local_modes_kernel(x_ref, rate_ref, rg_ref, g_ref, out_ref, final_ref):
    length = x_ref.shape[0]
    mode_count = rate_ref.shape[0]
    x = x_ref[...]
    rows = lax.broadcasted_iota(jnp.int32, (length, length), 0)
    cols = lax.broadcasted_iota(jnp.int32, (length, length), 1)
    lower = (rows >= cols).astype(jnp.bfloat16)
    offsets = lax.broadcasted_iota(jnp.int32, (length, 1), 0).astype(jnp.float32)
    total = jnp.zeros(x.shape, jnp.float32)
    for m in range(mode_count):
        rate = rate_ref[m : m + 1, :]
        terms = jnp.exp(rate * offsets) * x
        high = terms.astype(jnp.bfloat16)
        low = (terms - high.astype(jnp.float32)).astype(jnp.bfloat16)
        prefix = jnp.dot(lower, high, preferred_element_type=jnp.float32) + jnp.dot(
            lower, low, preferred_element_type=jnp.float32
        )
        total = total + rg_ref[m : m + 1, :] * jnp.exp(-rate * offsets) * prefix
        final_ref[m : m + 1, :] = (
            g_ref[m : m + 1, :] * jnp.exp(-rate * (length - 1.0)) * prefix[length - 1 : length, :]
        )
    out_ref[...] = total


def carried_kernel(local_ref, rate_ref, weight_ref, out_ref):
    length = local_ref.shape[0]
    mode_count = rate_ref.shape[0]
    steps = lax.broadcasted_iota(jnp.int32, (length, 1), 0).astype(jnp.float32) + 1.0
    total = local_ref[...]
    for m in range(mode_count):
        total = total + weight_ref[m : m + 1, :] * jnp.exp(-rate_ref[m : m + 1, :] * steps)
    out_ref[...] = total.astype(out_ref.dtype)


def channel_blocks(kernel, inputs, outputs, block):
    channels = inputs[0].shape[1]
    specs = [pl.BlockSpec((a.shape[0], block), lambda j: (0, j)) for a in inputs]
    out_specs = [pl.BlockSpec((o.shape[0], block), lambda j: (0, j)) for o in outputs]
    return pl.pallas_call(
        kernel,
        grid=(channels // block,),
        in_specs=specs,
        out_specs=out_specs,
        out_shape=outputs,
    )(*inputs)


def modal_chunk(signal, mode_rates, mode_residues, hyena_state, device_index, devices):
    length, channels = signal.shape
    mode_gain = jnp.sqrt(1.0 - jnp.exp(-2.0 * mode_rates))
    local_out, final_local = channel_blocks(
        local_modes_kernel,
        [signal, mode_rates, mode_residues * mode_gain, mode_gain],
        [
            jax.ShapeDtypeStruct((length, channels), jnp.float32),
            jax.ShapeDtypeStruct(mode_rates.shape, jnp.float32),
        ],
        256,
    )
    finals = lax.all_to_all(
        jnp.broadcast_to(final_local.astype(jnp.bfloat16)[None], (devices,) + final_local.shape),
        "context", 0, 0, tiled=True,
    ).astype(jnp.float32)
    source = jnp.arange(devices, dtype=jnp.int32)
    steps = (device_index - 1 - source).astype(jnp.float32)
    carry_weight = jnp.where(
        (source < device_index)[:, None, None],
        jnp.exp(-mode_rates[None] * (length * jnp.maximum(steps, 0.0))[:, None, None]),
        0.0,
    )
    incoming = jnp.exp(-mode_rates * (length * device_index.astype(jnp.float32))) * hyena_state
    incoming = incoming + jnp.sum(carry_weight * finals, axis=0)
    (long_out,) = channel_blocks(
        carried_kernel,
        [local_out, mode_rates, mode_residues * incoming],
        [jax.ShapeDtypeStruct((length, channels), jnp.bfloat16)],
        256,
    )
    return long_out


def attention_kernel(scale, q_ref, k_ref, v_ref, qpos_ref, kpos_ref, out_ref):
    scores = (
        lax.dot_general(
            q_ref[...], k_ref[...], (((1,), (1,)), ((), ())), preferred_element_type=jnp.float32
        )
        * scale
    )
    visible = kpos_ref[...] <= qpos_ref[...]
    row_max = jnp.max(jnp.where(visible, scores, -jnp.inf), axis=1, keepdims=True)
    weights = jnp.where(visible, jnp.exp(scores - row_max), 0.0).astype(jnp.bfloat16)
    weight_sum = jnp.sum(weights.astype(jnp.float32), axis=1, keepdims=True)
    numerator = jnp.dot(weights, v_ref[...], preferred_element_type=jnp.float32)
    out_ref[...] = (numerator / weight_sum).astype(out_ref.dtype)


def attend(queries, keys, values, query_pos, key_pos, block=256):
    rows, width = queries.shape
    key_rows = keys.shape[0]
    return pl.pallas_call(
        functools.partial(attention_kernel, 1.0 / math.sqrt(width)),
        grid=(rows // block,),
        in_specs=[
            pl.BlockSpec((block, width), lambda i: (i, 0)),
            pl.BlockSpec((key_rows, width), lambda i: (0, 0)),
            pl.BlockSpec((key_rows, width), lambda i: (0, 0)),
            pl.BlockSpec((block, 1), lambda i: (i, 0)),
            pl.BlockSpec((1, key_rows), lambda i: (0, 0)),
        ],
        out_specs=pl.BlockSpec((block, width), lambda i: (i, 0)),
        out_shape=jax.ShapeDtypeStruct((rows, width), jnp.bfloat16),
        compiler_params=pltpu.CompilerParams(vmem_limit_bytes=48 * 1024 * 1024),
    )(queries, keys, values, query_pos.reshape(rows, 1), key_pos.reshape(1, key_rows))


def project_kernel(x_ref, w_ref, out_ref):
    out_ref[...] = jnp.dot(x_ref[...], w_ref[...], preferred_element_type=jnp.float32)


def project(x, w, block=512):
    rows, depth = x.shape
    groups, _, width = w.shape
    return pl.pallas_call(
        project_kernel,
        grid=(groups, width // block),
        in_specs=[
            pl.BlockSpec((rows, depth), lambda g, j: (0, 0)),
            pl.BlockSpec((None, depth, block), lambda g, j: (g, 0, j)),
        ],
        out_specs=pl.BlockSpec((None, rows, block), lambda g, j: (g, 0, j)),
        out_shape=jax.ShapeDtypeStruct((groups, rows, width), jnp.float32),
        compiler_params=pltpu.CompilerParams(vmem_limit_bytes=48 * 1024 * 1024),
        cost_estimate=pl.CostEstimate(
            flops=2 * rows * depth * width * groups,
            bytes_accessed=2 * (rows * depth + groups * depth * width) + 4 * groups * rows * width,
            transcendentals=0,
        ),
    )(x, w)


def shards(
    streams,
    stream_tail,
    short_taps,
    decay_rates,
    residues,
    hyena_state,
    skip_weight,
    residual,
    norm_gain,
    qkv_weight,
    start_offset,
    cache_keys,
    cache_values,
):
    row_count = streams.shape[0]
    tap_count = short_taps.shape[0]
    devices = lax.axis_size("context")
    device_index = lax.axis_index("context")
    head_width = qkv_weight.shape[2]
    heads_here = head_width // HEAD
    half_rows = row_count // 2

    def by_head(block):
        per_head = block.reshape(row_count, heads_here, HEAD).transpose(1, 0, 2)
        return jnp.repeat(per_head, devices // heads_here, axis=0)

    cache_kv = lax.all_to_all(
        jnp.concatenate([by_head(cache_keys), by_head(cache_values)], axis=1),
        "context", 0, 0, tiled=True,
    )
    cache_k, cache_v = cache_kv[:, :row_count], cache_kv[:, row_count:]

    before = shifted(streams[row_count - (tap_count - 1) :], "context", 1)
    before = jnp.where(device_index == 0, stream_tail, before)
    extended = jnp.concatenate([before, streams], axis=0).astype(jnp.float32)
    filtered = jnp.zeros(streams.shape, jnp.float32)
    for step_back in range(tap_count):
        begin = tap_count - 1 - step_back
        filtered = filtered + short_taps[step_back][None] * extended[begin : begin + row_count]
    product = (filtered[:, 0] * filtered[:, 2]).astype(jnp.bfloat16)
    long_out = modal_chunk(
        product.astype(jnp.float32), decay_rates, residues, hyena_state, device_index, devices
    )
    hidden = (
        residual.astype(jnp.float32)
        + filtered[:, 1]
        * (long_out.astype(jnp.float32) + skip_weight[None, :] * product.astype(jnp.float32))
    ).astype(jnp.bfloat16)
    ways = lax.axis_size("tensor")
    pieces = [hidden] + [
        lax.ppermute(hidden, "tensor", [(i, (i - k) % ways) for i in range(ways)])
        for k in range(1, ways)
    ]
    gathered = jnp.roll(jnp.stack(pieces), lax.axis_index("tensor"), axis=0)
    gathered = gathered.transpose(1, 0, 2).reshape(row_count, ways * hidden.shape[1])
    hidden_float = gathered.astype(jnp.float32)
    mean_square = jnp.mean(hidden_float * hidden_float, axis=1, keepdims=True)
    normed = (hidden_float * lax.rsqrt(mean_square + NORM_EPSILON) * norm_gain[None, :]).astype(
        jnp.bfloat16
    )
    projected = (
        project(normed, qkv_weight.transpose(1, 0, 2))
        .transpose(1, 0, 2)
        .reshape(row_count, 3, heads_here, HEAD)
    )
    query_index = device_index * row_count + jnp.arange(row_count, dtype=jnp.int32)
    positions = (start_offset[0] + query_index).astype(jnp.float32)
    queries = rotate(projected[:, 0], positions).astype(jnp.bfloat16)
    new_keys = rotate(projected[:, 1], positions).astype(jnp.bfloat16)
    new_values = projected[:, 2].astype(jnp.bfloat16)

    query_parts = (
        queries.reshape(2, half_rows, heads_here, HEAD)
        .transpose(2, 0, 1, 3)
        .reshape(devices, half_rows, HEAD)
    )
    sent = lax.all_to_all(
        jnp.concatenate([query_parts, by_head(new_keys), by_head(new_values)], axis=1),
        "context", 0, 0, tiled=True,
    )
    my_queries = sent[:, :half_rows]
    new_k = sent[:, half_rows : half_rows + row_count]
    new_v = sent[:, half_rows + row_count :]

    hist_rows = cache_k.shape[0] * cache_k.shape[1]
    all_k = jnp.concatenate([cache_k.reshape(-1, HEAD), new_k.reshape(-1, HEAD)], axis=0)
    all_v = jnp.concatenate([cache_v.reshape(-1, HEAD), new_v.reshape(-1, HEAD)], axis=0)
    q_flat = my_queries.reshape(-1, HEAD)
    key_index = jnp.arange(all_k.shape[0], dtype=jnp.int32)
    key_pos = jnp.where(key_index < hist_rows, -1, key_index - hist_rows)
    src = jnp.arange(devices, dtype=jnp.int32)[:, None]
    row = jnp.arange(half_rows, dtype=jnp.int32)[None, :]
    query_pos = (src * row_count + (device_index % 2) * half_rows + row).reshape(-1)
    mine = attend(q_flat, all_k, all_v, query_pos, key_pos).reshape(devices, half_rows, HEAD)
    back = lax.all_to_all(mine, "context", 0, 0, tiled=True)
    attended = (
        back.reshape(heads_here, 2, half_rows, HEAD)
        .transpose(1, 2, 0, 3)
        .reshape(row_count, head_width)
    )
    return attended


def solution(mesh):
    placed = (
        P(("dp", "context"), None, "tensor"),
        P("dp", None, "tensor"),
        P(None, None, "tensor"),
        P(None, "tensor"),
        P(None, "tensor"),
        P("dp", "tensor"),
        P("tensor"),
        P(("dp", "context"), "tensor"),
        P(),
        P(None, None, "tensor"),
        P("dp"),
        P(("dp", "context"), "tensor"),
        P(("dp", "context"), "tensor"),
    )
    return jax.shard_map(
        shards,
        mesh=mesh,
        in_specs=placed,
        out_specs=P(("dp", "context"), "tensor"),
        check_vma=False,
    )
```

```python
import functools
import math

import jax
import jax.numpy as jnp
from jax import lax
from jax.experimental import pallas as pl
from jax.experimental.pallas import tpu as pltpu
from jax.sharding import PartitionSpec as P

HEAD = 128


ROTARY_BASE = 1000000.0
NORM_EPSILON = 1e-06


def shifted(x, axis, by):
    devices = lax.axis_size(axis)
    pairs = [(i, i + by) for i in range(devices) if 0 <= i + by < devices]
    return lax.ppermute(x, axis, pairs)


def rotate(features, positions):
    half_width = features.shape[-1] // 2
    exponents = jnp.arange(half_width, dtype=jnp.float32) * (2.0 / features.shape[-1])
    frequency = jnp.exp(-math.log(ROTARY_BASE) * exponents)
    angles = positions[:, None] * frequency[None, :]
    cosine = jnp.cos(angles)[:, None, :]
    sine_values = jnp.sin(angles)[:, None, :]
    front = features[..., :half_width]
    back = features[..., half_width:]
    return jnp.concatenate(
        [front * cosine - back * sine_values, back * cosine + front * sine_values], axis=-1
    )


def local_modes_kernel(x_ref, rate_ref, rg_ref, g_ref, out_ref, final_ref):
    length = x_ref.shape[0]
    mode_count = rate_ref.shape[0]
    x = x_ref[...]
    rows = lax.broadcasted_iota(jnp.int32, (length, length), 0)
    cols = lax.broadcasted_iota(jnp.int32, (length, length), 1)
    lower = (rows >= cols).astype(jnp.bfloat16)
    offsets = lax.broadcasted_iota(jnp.int32, (length, 1), 0).astype(jnp.float32)
    total = jnp.zeros(x.shape, jnp.float32)
    for m in range(mode_count):
        rate = rate_ref[m : m + 1, :]
        terms = jnp.exp(rate * offsets) * x
        high = terms.astype(jnp.bfloat16)
        low = (terms - high.astype(jnp.float32)).astype(jnp.bfloat16)
        prefix = jnp.dot(lower, high, preferred_element_type=jnp.float32) + jnp.dot(
            lower, low, preferred_element_type=jnp.float32
        )
        total = total + rg_ref[m : m + 1, :] * jnp.exp(-rate * offsets) * prefix
        final_ref[m : m + 1, :] = (
            g_ref[m : m + 1, :] * jnp.exp(-rate * (length - 1.0)) * prefix[length - 1 : length, :]
        )
    out_ref[...] = total


def carried_kernel(local_ref, rate_ref, weight_ref, out_ref):
    length = local_ref.shape[0]
    mode_count = rate_ref.shape[0]
    steps = lax.broadcasted_iota(jnp.int32, (length, 1), 0).astype(jnp.float32) + 1.0
    total = local_ref[...]
    for m in range(mode_count):
        total = total + weight_ref[m : m + 1, :] * jnp.exp(-rate_ref[m : m + 1, :] * steps)
    out_ref[...] = total.astype(out_ref.dtype)


def channel_blocks(kernel, inputs, outputs, block):
    channels = inputs[0].shape[1]
    specs = [pl.BlockSpec((a.shape[0], block), lambda j: (0, j)) for a in inputs]
    out_specs = [pl.BlockSpec((o.shape[0], block), lambda j: (0, j)) for o in outputs]
    return pl.pallas_call(
        kernel,
        grid=(channels // block,),
        in_specs=specs,
        out_specs=out_specs,
        out_shape=outputs,
    )(*inputs)


def modal_chunk(signal, mode_rates, mode_residues, hyena_state, device_index, devices):
    length, channels = signal.shape
    mode_gain = jnp.sqrt(1.0 - jnp.exp(-2.0 * mode_rates))
    local_out, final_local = channel_blocks(
        local_modes_kernel,
        [signal, mode_rates, mode_residues * mode_gain, mode_gain],
        [
            jax.ShapeDtypeStruct((length, channels), jnp.float32),
            jax.ShapeDtypeStruct(mode_rates.shape, jnp.float32),
        ],
        256,
    )
    finals = lax.all_to_all(
        jnp.broadcast_to(final_local.astype(jnp.bfloat16)[None], (devices,) + final_local.shape),
        "context", 0, 0, tiled=True,
    ).astype(jnp.float32)
    source = jnp.arange(devices, dtype=jnp.int32)
    steps = (device_index - 1 - source).astype(jnp.float32)
    carry_weight = jnp.where(
        (source < device_index)[:, None, None],
        jnp.exp(-mode_rates[None] * (length * jnp.maximum(steps, 0.0))[:, None, None]),
        0.0,
    )
    incoming = jnp.exp(-mode_rates * (length * device_index.astype(jnp.float32))) * hyena_state
    incoming = incoming + jnp.sum(carry_weight * finals, axis=0)
    (long_out,) = channel_blocks(
        carried_kernel,
        [local_out, mode_rates, mode_residues * incoming],
        [jax.ShapeDtypeStruct((length, channels), jnp.bfloat16)],
        256,
    )
    return long_out


def attention_kernel(scale, history, q_ref, k_ref, v_ref, qpos_ref, out_ref):
    q = q_ref[...]
    contract = (((1,), (1,)), ((), ()))
    old_scores = (
        lax.dot_general(q, k_ref[:history], contract, preferred_element_type=jnp.float32) * scale
    )
    new_scores = (
        lax.dot_general(q, k_ref[history:], contract, preferred_element_type=jnp.float32) * scale
    )
    new_pos = lax.broadcasted_iota(jnp.int32, (1, new_scores.shape[1]), 1)
    new_scores = jnp.where(new_pos <= qpos_ref[...], new_scores, -jnp.inf)
    row_max = jnp.maximum(
        jnp.max(old_scores, axis=1, keepdims=True), jnp.max(new_scores, axis=1, keepdims=True)
    )
    old_w = jnp.exp(old_scores - row_max).astype(jnp.bfloat16)
    new_w = jnp.exp(new_scores - row_max).astype(jnp.bfloat16)
    ones = jnp.ones((history, 128), jnp.bfloat16)
    weight_sum = jnp.dot(old_w, ones, preferred_element_type=jnp.float32) + jnp.dot(
        new_w, ones[: new_w.shape[1]], preferred_element_type=jnp.float32
    )
    numerator = jnp.dot(old_w, v_ref[:history], preferred_element_type=jnp.float32) + jnp.dot(
        new_w, v_ref[history:], preferred_element_type=jnp.float32
    )
    out_ref[...] = (numerator / weight_sum[:, :1]).astype(out_ref.dtype)


def attend(queries, keys, values, query_pos, history, block=256):
    rows, width = queries.shape
    key_rows = keys.shape[0]
    return pl.pallas_call(
        functools.partial(attention_kernel, 1.0 / math.sqrt(width), history),
        grid=(rows // block,),
        in_specs=[
            pl.BlockSpec((block, width), lambda i: (i, 0)),
            pl.BlockSpec((key_rows, width), lambda i: (0, 0)),
            pl.BlockSpec((key_rows, width), lambda i: (0, 0)),
            pl.BlockSpec((block, 1), lambda i: (i, 0)),
        ],
        out_specs=pl.BlockSpec((block, width), lambda i: (i, 0)),
        out_shape=jax.ShapeDtypeStruct((rows, width), jnp.bfloat16),
        compiler_params=pltpu.CompilerParams(vmem_limit_bytes=48 * 1024 * 1024),
    )(queries, keys, values, query_pos.reshape(rows, 1))


def project_kernel(x_ref, w_ref, out_ref):
    out_ref[...] = jnp.dot(x_ref[...], w_ref[...], preferred_element_type=jnp.float32)


def project(x, w, block=512):
    rows, depth = x.shape
    groups, _, width = w.shape
    return pl.pallas_call(
        project_kernel,
        grid=(groups, width // block),
        in_specs=[
            pl.BlockSpec((rows, depth), lambda g, j: (0, 0)),
            pl.BlockSpec((None, depth, block), lambda g, j: (g, 0, j)),
        ],
        out_specs=pl.BlockSpec((None, rows, block), lambda g, j: (g, 0, j)),
        out_shape=jax.ShapeDtypeStruct((groups, rows, width), jnp.float32),
        compiler_params=pltpu.CompilerParams(vmem_limit_bytes=48 * 1024 * 1024),
        cost_estimate=pl.CostEstimate(
            flops=2 * rows * depth * width * groups,
            bytes_accessed=2 * (rows * depth + groups * depth * width) + 4 * groups * rows * width,
            transcendentals=0,
        ),
    )(x, w)


def shards(
    streams,
    stream_tail,
    short_taps,
    decay_rates,
    residues,
    hyena_state,
    skip_weight,
    residual,
    norm_gain,
    qkv_weight,
    start_offset,
    cache_keys,
    cache_values,
):
    row_count = streams.shape[0]
    tap_count = short_taps.shape[0]
    devices = lax.axis_size("context")
    device_index = lax.axis_index("context")
    head_width = qkv_weight.shape[2]
    heads_here = head_width // HEAD
    half_rows = row_count // 2

    def by_head(block):
        per_head = block.reshape(row_count, heads_here, HEAD).transpose(1, 0, 2)
        return jnp.repeat(per_head, devices // heads_here, axis=0)

    cache_kv = lax.all_to_all(
        jnp.concatenate([by_head(cache_keys), by_head(cache_values)], axis=1),
        "context", 0, 0, tiled=True,
    )
    cache_k, cache_v = cache_kv[:, :row_count], cache_kv[:, row_count:]

    before = shifted(streams[row_count - (tap_count - 1) :], "context", 1)
    before = jnp.where(device_index == 0, stream_tail, before)
    extended = jnp.concatenate([before, streams], axis=0).astype(jnp.float32)
    filtered = jnp.zeros(streams.shape, jnp.float32)
    for step_back in range(tap_count):
        begin = tap_count - 1 - step_back
        filtered = filtered + short_taps[step_back][None] * extended[begin : begin + row_count]
    product = (filtered[:, 0] * filtered[:, 2]).astype(jnp.bfloat16)
    long_out = modal_chunk(
        product.astype(jnp.float32), decay_rates, residues, hyena_state, device_index, devices
    )
    hidden = (
        residual.astype(jnp.float32)
        + filtered[:, 1]
        * (long_out.astype(jnp.float32) + skip_weight[None, :] * product.astype(jnp.float32))
    ).astype(jnp.bfloat16)
    ways = lax.axis_size("tensor")
    gathered = lax.all_to_all(
        jnp.broadcast_to(hidden[None], (ways,) + hidden.shape), "tensor", 0, 0, tiled=True
    )
    gathered = gathered.transpose(1, 0, 2).reshape(row_count, ways * hidden.shape[1])
    hidden_float = gathered.astype(jnp.float32)
    mean_square = jnp.mean(hidden_float * hidden_float, axis=1, keepdims=True)
    normed = (hidden_float * lax.rsqrt(mean_square + NORM_EPSILON) * norm_gain[None, :]).astype(
        jnp.bfloat16
    )
    projected = (
        project(normed, qkv_weight.transpose(1, 0, 2))
        .transpose(1, 0, 2)
        .reshape(row_count, 3, heads_here, HEAD)
    )
    query_index = device_index * row_count + jnp.arange(row_count, dtype=jnp.int32)
    positions = (start_offset[0] + query_index).astype(jnp.float32)
    queries = rotate(projected[:, 0], positions).astype(jnp.bfloat16)
    new_keys = rotate(projected[:, 1], positions).astype(jnp.bfloat16)
    new_values = projected[:, 2].astype(jnp.bfloat16)

    query_parts = (
        queries.reshape(2, half_rows, heads_here, HEAD)
        .transpose(2, 0, 1, 3)
        .reshape(devices, half_rows, HEAD)
    )
    sent = lax.all_to_all(
        jnp.concatenate([query_parts, by_head(new_keys), by_head(new_values)], axis=1),
        "context", 0, 0, tiled=True,
    )
    my_queries = sent[:, :half_rows]
    new_k = sent[:, half_rows : half_rows + row_count]
    new_v = sent[:, half_rows + row_count :]

    hist_rows = cache_k.shape[0] * cache_k.shape[1]
    all_k = jnp.concatenate([cache_k.reshape(-1, HEAD), new_k.reshape(-1, HEAD)], axis=0)
    all_v = jnp.concatenate([cache_v.reshape(-1, HEAD), new_v.reshape(-1, HEAD)], axis=0)
    q_flat = my_queries.reshape(-1, HEAD)
    src = jnp.arange(devices, dtype=jnp.int32)[:, None]
    row = jnp.arange(half_rows, dtype=jnp.int32)[None, :]
    query_pos = (src * row_count + (device_index % 2) * half_rows + row).reshape(-1)
    mine = attend(q_flat, all_k, all_v, query_pos, hist_rows).reshape(devices, half_rows, HEAD)
    back = lax.all_to_all(mine, "context", 0, 0, tiled=True)
    attended = (
        back.reshape(heads_here, 2, half_rows, HEAD)
        .transpose(1, 2, 0, 3)
        .reshape(row_count, head_width)
    )
    return attended


def solution(mesh):
    placed = (
        P(("dp", "context"), None, "tensor"),
        P("dp", None, "tensor"),
        P(None, None, "tensor"),
        P(None, "tensor"),
        P(None, "tensor"),
        P("dp", "tensor"),
        P("tensor"),
        P(("dp", "context"), "tensor"),
        P(),
        P(None, None, "tensor"),
        P("dp"),
        P(("dp", "context"), "tensor"),
        P(("dp", "context"), "tensor"),
    )
    return jax.shard_map(
        shards,
        mesh=mesh,
        in_specs=placed,
        out_specs=P(("dp", "context"), "tensor"),
        check_vma=False,
    )
```

```python
import functools
import math

import jax
import jax.numpy as jnp
from jax import lax
from jax.experimental import pallas as pl
from jax.experimental.pallas import tpu as pltpu
from jax.sharding import PartitionSpec as P

HEAD = 128


ROTARY_BASE = 1000000.0
NORM_EPSILON = 1e-06


def shifted(x, axis, by):
    devices = lax.axis_size(axis)
    pairs = [(i, i + by) for i in range(devices) if 0 <= i + by < devices]
    return lax.ppermute(x, axis, pairs)


def rotate(features, positions):
    half_width = features.shape[-1] // 2
    exponents = jnp.arange(half_width, dtype=jnp.float32) * (2.0 / features.shape[-1])
    frequency = jnp.exp(-math.log(ROTARY_BASE) * exponents)
    angles = positions[:, None] * frequency[None, :]
    cosine = jnp.cos(angles)[:, None, :]
    sine_values = jnp.sin(angles)[:, None, :]
    front = features[..., :half_width]
    back = features[..., half_width:]
    return jnp.concatenate(
        [front * cosine - back * sine_values, back * cosine + front * sine_values], axis=-1
    )


def front_kernel(
    s_ref, b_ref, tap_ref, rate_ref, rg_ref, g_ref, prod_ref, f1_ref, out_ref, fin_ref, fin_scr
):
    length = s_ref.shape[1]
    mode_count = rate_ref.shape[0]
    row = lax.broadcasted_iota(jnp.int32, (length, s_ref.shape[2]), 0)
    filtered = []
    for i in range(3):
        now = s_ref[i].astype(jnp.float32)
        before = b_ref[i].astype(jnp.float32)
        back1 = jnp.where(row == 0, before[1:2], pltpu.roll(now, 1, 0))
        back2 = jnp.where(
            row == 0, before[0:1], jnp.where(row == 1, before[1:2], pltpu.roll(now, 2, 0))
        )
        taps = tap_ref[:, i, :]
        filtered.append(taps[0:1] * now + taps[1:2] * back1 + taps[2:3] * back2)
    product = (filtered[0] * filtered[2]).astype(jnp.bfloat16)
    prod_ref[...] = product
    f1_ref[...] = filtered[1]
    x = product.astype(jnp.float32)
    rows = lax.broadcasted_iota(jnp.int32, (length, length), 0)
    cols = lax.broadcasted_iota(jnp.int32, (length, length), 1)
    lower = (rows >= cols).astype(jnp.bfloat16)
    offsets = lax.broadcasted_iota(jnp.int32, (length, 1), 0).astype(jnp.float32)
    total = jnp.zeros(x.shape, jnp.float32)
    for m in range(mode_count):
        rate = rate_ref[m : m + 1, :]
        terms = jnp.exp(rate * offsets) * x
        high = terms.astype(jnp.bfloat16)
        low = (terms - high.astype(jnp.float32)).astype(jnp.bfloat16)
        prefix = jnp.dot(lower, high, preferred_element_type=jnp.float32) + jnp.dot(
            lower, low, preferred_element_type=jnp.float32
        )
        total = total + rg_ref[m : m + 1, :] * jnp.exp(-rate * offsets) * prefix
        fin_scr[m : m + 1, :] = (
            g_ref[m : m + 1, :] * jnp.exp(-rate * (length - 1.0)) * prefix[length - 1 : length, :]
        )
    out_ref[...] = total
    fin_ref[...] = jnp.broadcast_to(fin_scr[...][None], fin_ref.shape).astype(fin_ref.dtype)


def back_kernel(
    local_ref, rate_ref, res_ref, fin_ref, hs_ref, steps_ref, mask_ref, first_ref,
    f1_ref, prod_ref, resid_ref, skip_ref, out_ref,
):
    length = local_ref.shape[0]
    mode_count = rate_ref.shape[0]
    rates = rate_ref[...]
    incoming = jnp.exp(-rates * first_ref[...]) * hs_ref[...]
    for src in range(fin_ref.shape[0]):
        incoming = incoming + mask_ref[src : src + 1, :] * jnp.exp(
            -rates * steps_ref[src : src + 1, :]
        ) * fin_ref[src].astype(jnp.float32)
    weight = res_ref[...] * incoming
    steps = lax.broadcasted_iota(jnp.int32, (length, 1), 0).astype(jnp.float32) + 1.0
    total = local_ref[...]
    for m in range(mode_count):
        total = total + weight[m : m + 1, :] * jnp.exp(-rates[m : m + 1, :] * steps)
    long_out = total.astype(jnp.bfloat16).astype(jnp.float32)
    hidden = (
        resid_ref[...].astype(jnp.float32)
        + f1_ref[...] * (long_out + skip_ref[...] * prod_ref[...].astype(jnp.float32))
    ).astype(out_ref.dtype)
    out_ref[...] = jnp.broadcast_to(hidden[None], out_ref.shape)


def channel_blocks(kernel, inputs, outputs, block, scratch=()):
    def spec(shape):
        lead = tuple(0 for _ in shape[:-1])
        return pl.BlockSpec(tuple(shape[:-1]) + (block,), lambda j: lead + (j,))

    return pl.pallas_call(
        kernel,
        grid=(outputs[0].shape[-1] // block,),
        in_specs=[spec(a.shape) for a in inputs],
        out_specs=[spec(o.shape) for o in outputs],
        out_shape=outputs,
        scratch_shapes=list(scratch),
    )(*inputs)


def attention_kernel(scale, history, q_ref, k_ref, v_ref, qpos_ref, out_ref):
    q = q_ref[...]
    contract = (((1,), (1,)), ((), ()))
    old_scores = (
        lax.dot_general(q, k_ref[:history], contract, preferred_element_type=jnp.float32) * scale
    )
    new_scores = (
        lax.dot_general(q, k_ref[history:], contract, preferred_element_type=jnp.float32) * scale
    )
    new_pos = lax.broadcasted_iota(jnp.int32, (1, new_scores.shape[1]), 1)
    new_scores = jnp.where(new_pos <= qpos_ref[...], new_scores, -jnp.inf)
    row_max = jnp.maximum(
        jnp.max(old_scores, axis=1, keepdims=True), jnp.max(new_scores, axis=1, keepdims=True)
    )
    old_w = jnp.exp(old_scores - row_max).astype(jnp.bfloat16)
    new_w = jnp.exp(new_scores - row_max).astype(jnp.bfloat16)
    ones = jnp.ones((history, 128), jnp.bfloat16)
    weight_sum = jnp.dot(old_w, ones, preferred_element_type=jnp.float32) + jnp.dot(
        new_w, ones[: new_w.shape[1]], preferred_element_type=jnp.float32
    )
    numerator = jnp.dot(old_w, v_ref[:history], preferred_element_type=jnp.float32) + jnp.dot(
        new_w, v_ref[history:], preferred_element_type=jnp.float32
    )
    out_ref[...] = (numerator / weight_sum[:, :1]).astype(out_ref.dtype)


def attend(queries, keys, values, query_pos, history, block=256):
    rows, width = queries.shape
    key_rows = keys.shape[0]
    return pl.pallas_call(
        functools.partial(attention_kernel, 1.0 / math.sqrt(width), history),
        grid=(rows // block,),
        in_specs=[
            pl.BlockSpec((block, width), lambda i: (i, 0)),
            pl.BlockSpec((key_rows, width), lambda i: (0, 0)),
            pl.BlockSpec((key_rows, width), lambda i: (0, 0)),
            pl.BlockSpec((block, 1), lambda i: (i, 0)),
        ],
        out_specs=pl.BlockSpec((block, width), lambda i: (i, 0)),
        out_shape=jax.ShapeDtypeStruct((rows, width), jnp.bfloat16),
        compiler_params=pltpu.CompilerParams(vmem_limit_bytes=48 * 1024 * 1024),
    )(queries, keys, values, query_pos.reshape(rows, 1))


def project_kernel(x_ref, w_ref, out_ref):
    out_ref[...] = jnp.dot(x_ref[...], w_ref[...], preferred_element_type=jnp.float32)


def project(x, w, block=512):
    rows, depth = x.shape
    groups, _, width = w.shape
    return pl.pallas_call(
        project_kernel,
        grid=(groups, width // block),
        in_specs=[
            pl.BlockSpec((rows, depth), lambda g, j: (0, 0)),
            pl.BlockSpec((None, depth, block), lambda g, j: (g, 0, j)),
        ],
        out_specs=pl.BlockSpec((None, rows, block), lambda g, j: (g, 0, j)),
        out_shape=jax.ShapeDtypeStruct((groups, rows, width), jnp.float32),
        compiler_params=pltpu.CompilerParams(vmem_limit_bytes=48 * 1024 * 1024),
        cost_estimate=pl.CostEstimate(
            flops=2 * rows * depth * width * groups,
            bytes_accessed=2 * (rows * depth + groups * depth * width) + 4 * groups * rows * width,
            transcendentals=0,
        ),
    )(x, w)


def shards(
    streams,
    stream_tail,
    short_taps,
    decay_rates,
    residues,
    hyena_state,
    skip_weight,
    residual,
    norm_gain,
    qkv_weight,
    start_offset,
    cache_keys,
    cache_values,
):
    row_count = streams.shape[0]
    tap_count = short_taps.shape[0]
    devices = lax.axis_size("context")
    device_index = lax.axis_index("context")
    head_width = qkv_weight.shape[2]
    heads_here = head_width // HEAD
    half_rows = row_count // 2

    def by_head(block):
        per_head = block.reshape(row_count, heads_here, HEAD).transpose(1, 0, 2)
        return jnp.repeat(per_head, devices // heads_here, axis=0)

    cache_kv = lax.all_to_all(
        jnp.concatenate([by_head(cache_keys), by_head(cache_values)], axis=1),
        "context", 0, 0, tiled=True,
    )
    cache_k, cache_v = cache_kv[:, :row_count], cache_kv[:, row_count:]

    before = shifted(streams[row_count - (tap_count - 1) :], "context", 1)
    before = jnp.where(device_index == 0, stream_tail, before)
    channels = streams.shape[2]
    mode_count = decay_rates.shape[0]
    ways = lax.axis_size("tensor")
    mode_gain = jnp.sqrt(1.0 - jnp.exp(-2.0 * decay_rates))
    block = 256
    product, filtered1, local_out, finals_out = channel_blocks(
        front_kernel,
        [
            streams.transpose(1, 0, 2),
            before.transpose(1, 0, 2),
            short_taps,
            decay_rates,
            residues * mode_gain,
            mode_gain,
        ],
        [
            jax.ShapeDtypeStruct((row_count, channels), jnp.bfloat16),
            jax.ShapeDtypeStruct((row_count, channels), jnp.float32),
            jax.ShapeDtypeStruct((row_count, channels), jnp.float32),
            jax.ShapeDtypeStruct((devices, mode_count, channels), jnp.bfloat16),
        ],
        block,
        [pltpu.VMEM((mode_count, block), jnp.float32)],
    )
    finals = lax.all_to_all(finals_out, "context", 0, 0, tiled=True)
    source = jnp.arange(devices, dtype=jnp.int32)
    earlier = source < device_index
    steps = jnp.where(earlier, (device_index - 1 - source) * row_count, 0).astype(jnp.float32)
    ones_row = jnp.ones((1, channels), jnp.float32)
    (hidden_out,) = channel_blocks(
        back_kernel,
        [
            local_out,
            decay_rates,
            residues,
            finals,
            hyena_state,
            steps[:, None] * ones_row,
            earlier.astype(jnp.float32)[:, None] * ones_row,
            (device_index * row_count).astype(jnp.float32) * ones_row,
            filtered1,
            product,
            residual,
            skip_weight[None, :],
        ],
        [jax.ShapeDtypeStruct((ways, row_count, channels), jnp.bfloat16)],
        block,
    )
    gathered = lax.all_to_all(hidden_out, "tensor", 0, 0, tiled=True)
    gathered = gathered.transpose(1, 0, 2).reshape(row_count, ways * channels)
    hidden_float = gathered.astype(jnp.float32)
    mean_square = jnp.mean(hidden_float * hidden_float, axis=1, keepdims=True)
    normed = (hidden_float * lax.rsqrt(mean_square + NORM_EPSILON) * norm_gain[None, :]).astype(
        jnp.bfloat16
    )
    projected = (
        project(normed, qkv_weight.transpose(1, 0, 2))
        .transpose(1, 0, 2)
        .reshape(row_count, 3, heads_here, HEAD)
    )
    query_index = device_index * row_count + jnp.arange(row_count, dtype=jnp.int32)
    positions = (start_offset[0] + query_index).astype(jnp.float32)
    queries = rotate(projected[:, 0], positions).astype(jnp.bfloat16)
    new_keys = rotate(projected[:, 1], positions).astype(jnp.bfloat16)
    new_values = projected[:, 2].astype(jnp.bfloat16)

    query_parts = (
        queries.reshape(2, half_rows, heads_here, HEAD)
        .transpose(2, 0, 1, 3)
        .reshape(devices, half_rows, HEAD)
    )
    sent = lax.all_to_all(
        jnp.concatenate([query_parts, by_head(new_keys), by_head(new_values)], axis=1),
        "context", 0, 0, tiled=True,
    )
    my_queries = sent[:, :half_rows]
    new_k = sent[:, half_rows : half_rows + row_count]
    new_v = sent[:, half_rows + row_count :]

    hist_rows = cache_k.shape[0] * cache_k.shape[1]
    all_k = jnp.concatenate([cache_k.reshape(-1, HEAD), new_k.reshape(-1, HEAD)], axis=0)
    all_v = jnp.concatenate([cache_v.reshape(-1, HEAD), new_v.reshape(-1, HEAD)], axis=0)
    q_flat = my_queries.reshape(-1, HEAD)
    src = jnp.arange(devices, dtype=jnp.int32)[:, None]
    row = jnp.arange(half_rows, dtype=jnp.int32)[None, :]
    query_pos = (src * row_count + (device_index % 2) * half_rows + row).reshape(-1)
    mine = attend(q_flat, all_k, all_v, query_pos, hist_rows).reshape(devices, half_rows, HEAD)
    back = lax.all_to_all(mine, "context", 0, 0, tiled=True)
    attended = (
        back.reshape(heads_here, 2, half_rows, HEAD)
        .transpose(1, 2, 0, 3)
        .reshape(row_count, head_width)
    )
    return attended


def solution(mesh):
    placed = (
        P(("dp", "context"), None, "tensor"),
        P("dp", None, "tensor"),
        P(None, None, "tensor"),
        P(None, "tensor"),
        P(None, "tensor"),
        P("dp", "tensor"),
        P("tensor"),
        P(("dp", "context"), "tensor"),
        P(),
        P(None, None, "tensor"),
        P("dp"),
        P(("dp", "context"), "tensor"),
        P(("dp", "context"), "tensor"),
    )
    return jax.shard_map(
        shards,
        mesh=mesh,
        in_specs=placed,
        out_specs=P(("dp", "context"), "tensor"),
        check_vma=False,
    )
```

```python
import functools
import math

import jax
import jax.numpy as jnp
from jax import lax
from jax.experimental import pallas as pl
from jax.experimental.pallas import tpu as pltpu
from jax.sharding import PartitionSpec as P

HEAD = 128


ROTARY_BASE = 1000000.0
NORM_EPSILON = 1e-06


def shifted(x, axis, by):
    devices = lax.axis_size(axis)
    pairs = [(i, i + by) for i in range(devices) if 0 <= i + by < devices]
    return lax.ppermute(x, axis, pairs)


def rotate(features, positions):
    half_width = features.shape[-1] // 2
    exponents = jnp.arange(half_width, dtype=jnp.float32) * (2.0 / features.shape[-1])
    frequency = jnp.exp(-math.log(ROTARY_BASE) * exponents)
    angles = positions[:, None] * frequency[None, :]
    cosine = jnp.cos(angles)[:, None, :]
    sine_values = jnp.sin(angles)[:, None, :]
    front = features[..., :half_width]
    back = features[..., half_width:]
    return jnp.concatenate(
        [front * cosine - back * sine_values, back * cosine + front * sine_values], axis=-1
    )


def front_kernel(
    idx_ref, s_ref, recv_ref, tail_ref, tap_ref, rate_ref, res_ref,
    prod_ref, f1_ref, out_ref, fin_ref, fin_scr,
):
    length = s_ref.shape[1]
    mode_count = rate_ref.shape[0]
    row = lax.broadcasted_iota(jnp.int32, (length, s_ref.shape[2]), 0)
    filtered = []
    for i in range(3):
        now = s_ref[i].astype(jnp.float32)
        before = jnp.where(
            idx_ref[0] == 0, tail_ref[i].astype(jnp.float32), recv_ref[i].astype(jnp.float32)
        )
        back1 = jnp.where(row == 0, before[1:2], pltpu.roll(now, 1, 0))
        back2 = jnp.where(
            row == 0, before[0:1], jnp.where(row == 1, before[1:2], pltpu.roll(now, 2, 0))
        )
        taps = tap_ref[:, i, :]
        filtered.append(taps[0:1] * now + taps[1:2] * back1 + taps[2:3] * back2)
    product = (filtered[0] * filtered[2]).astype(jnp.bfloat16)
    prod_ref[...] = product
    f1_ref[...] = filtered[1]
    x = product.astype(jnp.float32)
    rows = lax.broadcasted_iota(jnp.int32, (length, length), 0)
    cols = lax.broadcasted_iota(jnp.int32, (length, length), 1)
    lower = (rows >= cols).astype(jnp.bfloat16)
    offsets = lax.broadcasted_iota(jnp.int32, (length, 1), 0).astype(jnp.float32)
    gains = jnp.sqrt(1.0 - jnp.exp(-2.0 * rate_ref[...]))
    rgains = res_ref[...] * gains
    total = jnp.zeros(x.shape, jnp.float32)
    for m in range(mode_count):
        rate = rate_ref[m : m + 1, :]
        terms = jnp.exp(rate * offsets) * x
        high = terms.astype(jnp.bfloat16)
        low = (terms - high.astype(jnp.float32)).astype(jnp.bfloat16)
        prefix = jnp.dot(lower, high, preferred_element_type=jnp.float32) + jnp.dot(
            lower, low, preferred_element_type=jnp.float32
        )
        total = total + rgains[m : m + 1, :] * jnp.exp(-rate * offsets) * prefix
        fin_scr[m : m + 1, :] = (
            gains[m : m + 1, :] * jnp.exp(-rate * (length - 1.0)) * prefix[length - 1 : length, :]
        )
    out_ref[...] = total
    fin_ref[...] = jnp.broadcast_to(fin_scr[...][None], fin_ref.shape).astype(fin_ref.dtype)


def back_kernel(
    idx_ref, local_ref, rate_ref, res_ref, fin_ref, hs_ref,
    f1_ref, prod_ref, resid_ref, skip_ref, out_ref,
):
    length = local_ref.shape[0]
    mode_count = rate_ref.shape[0]
    rates = rate_ref[...]
    me = idx_ref[0]
    incoming = jnp.exp(-rates * (me * length).astype(jnp.float32)) * hs_ref[...]
    for src in range(fin_ref.shape[0]):
        steps_back = (jnp.maximum(me - 1 - src, 0) * length).astype(jnp.float32)
        weight_src = jnp.where(src < me, jnp.exp(-rates * steps_back), 0.0)
        incoming = incoming + weight_src * fin_ref[src].astype(jnp.float32)
    weight = res_ref[...] * incoming
    steps = lax.broadcasted_iota(jnp.int32, (length, 1), 0).astype(jnp.float32) + 1.0
    total = local_ref[...]
    for m in range(mode_count):
        total = total + weight[m : m + 1, :] * jnp.exp(-rates[m : m + 1, :] * steps)
    long_out = total.astype(jnp.bfloat16).astype(jnp.float32)
    hidden = (
        resid_ref[...].astype(jnp.float32)
        + f1_ref[...] * (long_out + skip_ref[...] * prod_ref[...].astype(jnp.float32))
    ).astype(out_ref.dtype)
    out_ref[...] = jnp.broadcast_to(hidden[None], out_ref.shape)


def channel_blocks(kernel, index, inputs, outputs, block, scratch=()):
    def spec(shape):
        lead = tuple(0 for _ in shape[:-1])
        return pl.BlockSpec(tuple(shape[:-1]) + (block,), lambda j, idx: lead + (j,))

    grid_spec = pltpu.PrefetchScalarGridSpec(
        num_scalar_prefetch=1,
        grid=(outputs[0].shape[-1] // block,),
        in_specs=[spec(a.shape) for a in inputs],
        out_specs=[spec(o.shape) for o in outputs],
        scratch_shapes=list(scratch),
    )
    return pl.pallas_call(kernel, grid_spec=grid_spec, out_shape=outputs)(index, *inputs)


def attention_kernel(scale, history, q_ref, k_ref, v_ref, qpos_ref, out_ref):
    q = q_ref[...]
    contract = (((1,), (1,)), ((), ()))
    old_scores = (
        lax.dot_general(q, k_ref[:history], contract, preferred_element_type=jnp.float32) * scale
    )
    new_scores = (
        lax.dot_general(q, k_ref[history:], contract, preferred_element_type=jnp.float32) * scale
    )
    new_pos = lax.broadcasted_iota(jnp.int32, (1, new_scores.shape[1]), 1)
    new_scores = jnp.where(new_pos <= qpos_ref[...], new_scores, -jnp.inf)
    row_max = jnp.maximum(
        jnp.max(old_scores, axis=1, keepdims=True), jnp.max(new_scores, axis=1, keepdims=True)
    )
    old_w = jnp.exp(old_scores - row_max).astype(jnp.bfloat16)
    new_w = jnp.exp(new_scores - row_max).astype(jnp.bfloat16)
    ones = jnp.ones((history, 128), jnp.bfloat16)
    weight_sum = jnp.dot(old_w, ones, preferred_element_type=jnp.float32) + jnp.dot(
        new_w, ones[: new_w.shape[1]], preferred_element_type=jnp.float32
    )
    numerator = jnp.dot(old_w, v_ref[:history], preferred_element_type=jnp.float32) + jnp.dot(
        new_w, v_ref[history:], preferred_element_type=jnp.float32
    )
    out_ref[...] = (numerator / weight_sum[:, :1]).astype(out_ref.dtype)


def attend(queries, keys, values, query_pos, history, block=256):
    rows, width = queries.shape
    key_rows = keys.shape[0]
    return pl.pallas_call(
        functools.partial(attention_kernel, 1.0 / math.sqrt(width), history),
        grid=(rows // block,),
        in_specs=[
            pl.BlockSpec((block, width), lambda i: (i, 0)),
            pl.BlockSpec((key_rows, width), lambda i: (0, 0)),
            pl.BlockSpec((key_rows, width), lambda i: (0, 0)),
            pl.BlockSpec((block, 1), lambda i: (i, 0)),
        ],
        out_specs=pl.BlockSpec((block, width), lambda i: (i, 0)),
        out_shape=jax.ShapeDtypeStruct((rows, width), jnp.bfloat16),
        compiler_params=pltpu.CompilerParams(vmem_limit_bytes=48 * 1024 * 1024),
    )(queries, keys, values, query_pos.reshape(rows, 1))


def project_kernel(x_ref, w_ref, out_ref):
    out_ref[...] = jnp.dot(x_ref[...], w_ref[...], preferred_element_type=jnp.float32)


def project(x, w, block=512):
    rows, depth = x.shape
    groups, _, width = w.shape
    return pl.pallas_call(
        project_kernel,
        grid=(groups, width // block),
        in_specs=[
            pl.BlockSpec((rows, depth), lambda g, j: (0, 0)),
            pl.BlockSpec((None, depth, block), lambda g, j: (g, 0, j)),
        ],
        out_specs=pl.BlockSpec((None, rows, block), lambda g, j: (g, 0, j)),
        out_shape=jax.ShapeDtypeStruct((groups, rows, width), jnp.float32),
        compiler_params=pltpu.CompilerParams(vmem_limit_bytes=48 * 1024 * 1024),
        cost_estimate=pl.CostEstimate(
            flops=2 * rows * depth * width * groups,
            bytes_accessed=2 * (rows * depth + groups * depth * width) + 4 * groups * rows * width,
            transcendentals=0,
        ),
    )(x, w)


def shards(
    streams,
    stream_tail,
    short_taps,
    decay_rates,
    residues,
    hyena_state,
    skip_weight,
    residual,
    norm_gain,
    qkv_weight,
    start_offset,
    cache_keys,
    cache_values,
):
    row_count = streams.shape[0]
    tap_count = short_taps.shape[0]
    devices = lax.axis_size("context")
    device_index = lax.axis_index("context")
    head_width = qkv_weight.shape[2]
    heads_here = head_width // HEAD
    half_rows = row_count // 2

    def by_head(block):
        per_head = block.reshape(row_count, heads_here, HEAD).transpose(1, 0, 2)
        return jnp.repeat(per_head, devices // heads_here, axis=0)

    cache_kv = lax.all_to_all(
        jnp.concatenate([by_head(cache_keys), by_head(cache_values)], axis=1),
        "context", 0, 0, tiled=True,
    )
    cache_k, cache_v = cache_kv[:, :row_count], cache_kv[:, row_count:]

    received = shifted(streams[row_count - (tap_count - 1) :], "context", 1)
    channels = streams.shape[2]
    mode_count = decay_rates.shape[0]
    ways = lax.axis_size("tensor")
    index = device_index.astype(jnp.int32).reshape(1)
    block = 256
    product, filtered1, local_out, finals_out = channel_blocks(
        front_kernel,
        index,
        [
            streams.transpose(1, 0, 2),
            received.transpose(1, 0, 2),
            stream_tail.transpose(1, 0, 2),
            short_taps,
            decay_rates,
            residues,
        ],
        [
            jax.ShapeDtypeStruct((row_count, channels), jnp.bfloat16),
            jax.ShapeDtypeStruct((row_count, channels), jnp.float32),
            jax.ShapeDtypeStruct((row_count, channels), jnp.float32),
            jax.ShapeDtypeStruct((devices, mode_count, channels), jnp.bfloat16),
        ],
        block,
        [pltpu.VMEM((mode_count, block), jnp.float32)],
    )
    finals = lax.all_to_all(finals_out, "context", 0, 0, tiled=True)
    (hidden_out,) = channel_blocks(
        back_kernel,
        index,
        [
            local_out,
            decay_rates,
            residues,
            finals,
            hyena_state,
            filtered1,
            product,
            residual,
            skip_weight[None, :],
        ],
        [jax.ShapeDtypeStruct((ways, row_count, channels), jnp.bfloat16)],
        block,
    )
    gathered = lax.all_to_all(hidden_out, "tensor", 0, 0, tiled=True)
    gathered = gathered.transpose(1, 0, 2).reshape(row_count, ways * channels)
    hidden_float = gathered.astype(jnp.float32)
    mean_square = jnp.mean(hidden_float * hidden_float, axis=1, keepdims=True)
    normed = (hidden_float * lax.rsqrt(mean_square + NORM_EPSILON) * norm_gain[None, :]).astype(
        jnp.bfloat16
    )
    projected = (
        project(normed, qkv_weight.transpose(1, 0, 2))
        .transpose(1, 0, 2)
        .reshape(row_count, 3, heads_here, HEAD)
    )
    query_index = device_index * row_count + jnp.arange(row_count, dtype=jnp.int32)
    positions = (start_offset[0] + query_index).astype(jnp.float32)
    queries = rotate(projected[:, 0], positions).astype(jnp.bfloat16)
    new_keys = rotate(projected[:, 1], positions).astype(jnp.bfloat16)
    new_values = projected[:, 2].astype(jnp.bfloat16)

    query_parts = (
        queries.reshape(2, half_rows, heads_here, HEAD)
        .transpose(2, 0, 1, 3)
        .reshape(devices, half_rows, HEAD)
    )
    sent = lax.all_to_all(
        jnp.concatenate([query_parts, by_head(new_keys), by_head(new_values)], axis=1),
        "context", 0, 0, tiled=True,
    )
    my_queries = sent[:, :half_rows]
    new_k = sent[:, half_rows : half_rows + row_count]
    new_v = sent[:, half_rows + row_count :]

    hist_rows = cache_k.shape[0] * cache_k.shape[1]
    all_k = jnp.concatenate([cache_k.reshape(-1, HEAD), new_k.reshape(-1, HEAD)], axis=0)
    all_v = jnp.concatenate([cache_v.reshape(-1, HEAD), new_v.reshape(-1, HEAD)], axis=0)
    q_flat = my_queries.reshape(-1, HEAD)
    src = jnp.arange(devices, dtype=jnp.int32)[:, None]
    row = jnp.arange(half_rows, dtype=jnp.int32)[None, :]
    query_pos = (src * row_count + (device_index % 2) * half_rows + row).reshape(-1)
    mine = attend(q_flat, all_k, all_v, query_pos, hist_rows).reshape(devices, half_rows, HEAD)
    back = lax.all_to_all(mine, "context", 0, 0, tiled=True)
    attended = (
        back.reshape(heads_here, 2, half_rows, HEAD)
        .transpose(1, 2, 0, 3)
        .reshape(row_count, head_width)
    )
    return attended


def solution(mesh):
    placed = (
        P(("dp", "context"), None, "tensor"),
        P("dp", None, "tensor"),
        P(None, None, "tensor"),
        P(None, "tensor"),
        P(None, "tensor"),
        P("dp", "tensor"),
        P("tensor"),
        P(("dp", "context"), "tensor"),
        P(),
        P(None, None, "tensor"),
        P("dp"),
        P(("dp", "context"), "tensor"),
        P(("dp", "context"), "tensor"),
    )
    return jax.shard_map(
        shards,
        mesh=mesh,
        in_specs=placed,
        out_specs=P(("dp", "context"), "tensor"),
        check_vma=False,
    )
```

```python
import functools
import math

import jax
import jax.numpy as jnp
from jax import lax
from jax.experimental import pallas as pl
from jax.experimental.pallas import tpu as pltpu
from jax.sharding import PartitionSpec as P

HEAD = 128


ROTARY_BASE = 1000000.0
NORM_EPSILON = 1e-06


def shifted(x, axis, by):
    devices = lax.axis_size(axis)
    pairs = [(i, i + by) for i in range(devices) if 0 <= i + by < devices]
    return lax.ppermute(x, axis, pairs)


def rotate(features, positions):
    half_width = features.shape[-1] // 2
    exponents = jnp.arange(half_width, dtype=jnp.float32) * (2.0 / features.shape[-1])
    frequency = jnp.exp(-math.log(ROTARY_BASE) * exponents)
    angles = positions[:, None] * frequency[None, :]
    cosine = jnp.cos(angles)[:, None, :]
    sine_values = jnp.sin(angles)[:, None, :]
    front = features[..., :half_width]
    back = features[..., half_width:]
    return jnp.concatenate(
        [front * cosine - back * sine_values, back * cosine + front * sine_values], axis=-1
    )


def front_kernel(
    idx_ref, s_ref, recv_ref, tail_ref, tap_ref, rate_ref, res_ref,
    prod_ref, f1_ref, out_ref, fin_ref, fin_scr,
):
    length = s_ref.shape[1]
    mode_count = rate_ref.shape[0]
    row = lax.broadcasted_iota(jnp.int32, (length, s_ref.shape[2]), 0)
    filtered = []
    for i in range(3):
        now = s_ref[i].astype(jnp.float32)
        before = jnp.where(
            idx_ref[0] == 0, tail_ref[i].astype(jnp.float32), recv_ref[i].astype(jnp.float32)
        )
        back1 = jnp.where(row == 0, before[1:2], pltpu.roll(now, 1, 0))
        back2 = jnp.where(
            row == 0, before[0:1], jnp.where(row == 1, before[1:2], pltpu.roll(now, 2, 0))
        )
        taps = tap_ref[:, i, :]
        filtered.append(taps[0:1] * now + taps[1:2] * back1 + taps[2:3] * back2)
    product = (filtered[0] * filtered[2]).astype(jnp.bfloat16)
    prod_ref[...] = product
    f1_ref[...] = filtered[1]
    x = product.astype(jnp.float32)
    rows = lax.broadcasted_iota(jnp.int32, (length, length), 0)
    cols = lax.broadcasted_iota(jnp.int32, (length, length), 1)
    lower = (rows >= cols).astype(jnp.bfloat16)
    offsets = lax.broadcasted_iota(jnp.int32, (length, 1), 0).astype(jnp.float32)
    gains = jnp.sqrt(1.0 - jnp.exp(-2.0 * rate_ref[...]))
    rgains = res_ref[...] * gains
    total = jnp.zeros(x.shape, jnp.float32)
    for m in range(mode_count):
        rate = rate_ref[m : m + 1, :]
        terms = jnp.exp(rate * offsets) * x
        high = terms.astype(jnp.bfloat16)
        low = (terms - high.astype(jnp.float32)).astype(jnp.bfloat16)
        prefix = jnp.dot(lower, high, preferred_element_type=jnp.float32) + jnp.dot(
            lower, low, preferred_element_type=jnp.float32
        )
        total = total + rgains[m : m + 1, :] * jnp.exp(-rate * offsets) * prefix
        fin_scr[m : m + 1, :] = (
            gains[m : m + 1, :] * jnp.exp(-rate * (length - 1.0)) * prefix[length - 1 : length, :]
        )
    out_ref[...] = total
    fin_ref[...] = jnp.broadcast_to(fin_scr[...][None], fin_ref.shape).astype(fin_ref.dtype)


def back_kernel(
    idx_ref, local_ref, rate_ref, res_ref, fin_ref, hs_ref,
    f1_ref, prod_ref, resid_ref, skip_ref, out_ref,
):
    length = local_ref.shape[0]
    mode_count = rate_ref.shape[0]
    rates = rate_ref[...]
    me = idx_ref[0]
    incoming = jnp.exp(-rates * (me * length).astype(jnp.float32)) * hs_ref[...]
    for src in range(fin_ref.shape[0]):
        steps_back = (jnp.maximum(me - 1 - src, 0) * length).astype(jnp.float32)
        weight_src = jnp.where(src < me, jnp.exp(-rates * steps_back), 0.0)
        incoming = incoming + weight_src * fin_ref[src].astype(jnp.float32)
    weight = res_ref[...] * incoming
    steps = lax.broadcasted_iota(jnp.int32, (length, 1), 0).astype(jnp.float32) + 1.0
    total = local_ref[...]
    for m in range(mode_count):
        total = total + weight[m : m + 1, :] * jnp.exp(-rates[m : m + 1, :] * steps)
    long_out = total.astype(jnp.bfloat16).astype(jnp.float32)
    hidden = (
        resid_ref[...].astype(jnp.float32)
        + f1_ref[...] * (long_out + skip_ref[...] * prod_ref[...].astype(jnp.float32))
    ).astype(out_ref.dtype)
    out_ref[...] = jnp.broadcast_to(hidden[None], out_ref.shape)


def channel_blocks(kernel, index, inputs, outputs, block, scratch=()):
    def spec(shape):
        lead = tuple(0 for _ in shape[:-1])
        return pl.BlockSpec(tuple(shape[:-1]) + (block,), lambda j, idx: lead + (j,))

    grid_spec = pltpu.PrefetchScalarGridSpec(
        num_scalar_prefetch=1,
        grid=(outputs[0].shape[-1] // block,),
        in_specs=[spec(a.shape) for a in inputs],
        out_specs=[spec(o.shape) for o in outputs],
        scratch_shapes=list(scratch),
    )
    return pl.pallas_call(kernel, grid_spec=grid_spec, out_shape=outputs)(index, *inputs)


def attention_kernel(scale, history, q_ref, k_ref, v_ref, qpos_ref, out_ref):
    q = q_ref[...]
    contract = (((1,), (1,)), ((), ()))
    old_scores = (
        lax.dot_general(q, k_ref[:history], contract, preferred_element_type=jnp.float32) * scale
    )
    new_scores = (
        lax.dot_general(q, k_ref[history:], contract, preferred_element_type=jnp.float32) * scale
    )
    new_pos = lax.broadcasted_iota(jnp.int32, (1, new_scores.shape[1]), 1)
    new_scores = jnp.where(new_pos <= qpos_ref[...], new_scores, -jnp.inf)
    row_max = jnp.maximum(
        jnp.max(old_scores, axis=1, keepdims=True), jnp.max(new_scores, axis=1, keepdims=True)
    )
    old_w = jnp.exp(old_scores - row_max).astype(jnp.bfloat16)
    new_w = jnp.exp(new_scores - row_max).astype(jnp.bfloat16)
    ones = jnp.ones((history, 128), jnp.bfloat16)
    weight_sum = jnp.dot(old_w, ones, preferred_element_type=jnp.float32) + jnp.dot(
        new_w, ones[: new_w.shape[1]], preferred_element_type=jnp.float32
    )
    numerator = jnp.dot(old_w, v_ref[:history], preferred_element_type=jnp.float32) + jnp.dot(
        new_w, v_ref[history:], preferred_element_type=jnp.float32
    )
    out_ref[...] = (numerator / weight_sum[:, :1]).astype(out_ref.dtype)


def attend(queries, keys, values, query_pos, history, block=256):
    rows, width = queries.shape
    key_rows = keys.shape[0]
    return pl.pallas_call(
        functools.partial(attention_kernel, 1.0 / math.sqrt(width), history),
        grid=(rows // block,),
        in_specs=[
            pl.BlockSpec((block, width), lambda i: (i, 0)),
            pl.BlockSpec((key_rows, width), lambda i: (0, 0)),
            pl.BlockSpec((key_rows, width), lambda i: (0, 0)),
            pl.BlockSpec((block, 1), lambda i: (i, 0)),
        ],
        out_specs=pl.BlockSpec((block, width), lambda i: (i, 0)),
        out_shape=jax.ShapeDtypeStruct((rows, width), jnp.bfloat16),
        compiler_params=pltpu.CompilerParams(vmem_limit_bytes=48 * 1024 * 1024),
    )(queries, keys, values, query_pos.reshape(rows, 1))


def local_project_kernel(idx_ref, x_ref, w_ref, out_ref):
    out_ref[...] = jnp.dot(x_ref[...], w_ref[...], preferred_element_type=jnp.float32)


def rest_project_kernel(idx_ref, x_ref, w_ref, part_ref, out_ref):
    @pl.when(pl.program_id(2) == 0)
    def _():
        out_ref[...] = part_ref[...]

    out_ref[...] += jnp.dot(x_ref[...], w_ref[...], preferred_element_type=jnp.float32)


def project_own(index, x, w, block=512):
    rows, depth = x.shape
    groups, _, width = w.shape
    grid_spec = pltpu.PrefetchScalarGridSpec(
        num_scalar_prefetch=1,
        grid=(groups, width // block),
        in_specs=[
            pl.BlockSpec((rows, depth), lambda g, j, idx: (0, 0)),
            pl.BlockSpec((None, depth, block), lambda g, j, idx: (g, idx[0], j)),
        ],
        out_specs=pl.BlockSpec((None, rows, block), lambda g, j, idx: (g, 0, j)),
    )
    return pl.pallas_call(
        local_project_kernel,
        grid_spec=grid_spec,
        out_shape=jax.ShapeDtypeStruct((groups, rows, width), jnp.float32),
        compiler_params=pltpu.CompilerParams(vmem_limit_bytes=48 * 1024 * 1024),
        cost_estimate=pl.CostEstimate(
            flops=2 * rows * depth * width * groups,
            bytes_accessed=2 * (rows * depth + groups * depth * width) + 4 * groups * rows * width,
            transcendentals=0,
        ),
    )(index, x, w)


def project_rest(index, xs, w, part, block=512):
    ways, rows, depth = xs.shape
    groups, _, width = w.shape

    def other(k, idx):
        return (idx[0] + 1 + k) % ways

    grid_spec = pltpu.PrefetchScalarGridSpec(
        num_scalar_prefetch=1,
        grid=(groups, width // block, ways - 1),
        in_specs=[
            pl.BlockSpec((None, rows, depth), lambda g, j, k, idx: (other(k, idx), 0, 0)),
            pl.BlockSpec((None, depth, block), lambda g, j, k, idx: (g, other(k, idx), j)),
            pl.BlockSpec((None, rows, block), lambda g, j, k, idx: (g, 0, j)),
        ],
        out_specs=pl.BlockSpec((None, rows, block), lambda g, j, k, idx: (g, 0, j)),
    )
    return pl.pallas_call(
        rest_project_kernel,
        grid_spec=grid_spec,
        out_shape=jax.ShapeDtypeStruct((groups, rows, width), jnp.float32),
        compiler_params=pltpu.CompilerParams(vmem_limit_bytes=48 * 1024 * 1024),
        cost_estimate=pl.CostEstimate(
            flops=2 * rows * depth * width * groups * (ways - 1),
            bytes_accessed=2 * (ways - 1) * (rows * depth + groups * depth * width)
            + 8 * groups * rows * width,
            transcendentals=0,
        ),
    )(index, xs, w, part)


def shards(
    streams,
    stream_tail,
    short_taps,
    decay_rates,
    residues,
    hyena_state,
    skip_weight,
    residual,
    norm_gain,
    qkv_weight,
    start_offset,
    cache_keys,
    cache_values,
):
    row_count = streams.shape[0]
    tap_count = short_taps.shape[0]
    devices = lax.axis_size("context")
    device_index = lax.axis_index("context")
    head_width = qkv_weight.shape[2]
    heads_here = head_width // HEAD
    half_rows = row_count // 2

    def by_head(block):
        per_head = block.reshape(row_count, heads_here, HEAD).transpose(1, 0, 2)
        return jnp.repeat(per_head, devices // heads_here, axis=0)

    cache_kv = lax.all_to_all(
        jnp.concatenate([by_head(cache_keys), by_head(cache_values)], axis=1),
        "context", 0, 0, tiled=True,
    )
    cache_k, cache_v = cache_kv[:, :row_count], cache_kv[:, row_count:]

    received = shifted(streams[row_count - (tap_count - 1) :], "context", 1)
    channels = streams.shape[2]
    mode_count = decay_rates.shape[0]
    ways = lax.axis_size("tensor")
    index = device_index.astype(jnp.int32).reshape(1)
    block = 256
    product, filtered1, local_out, finals_out = channel_blocks(
        front_kernel,
        index,
        [
            streams.transpose(1, 0, 2),
            received.transpose(1, 0, 2),
            stream_tail.transpose(1, 0, 2),
            short_taps,
            decay_rates,
            residues,
        ],
        [
            jax.ShapeDtypeStruct((row_count, channels), jnp.bfloat16),
            jax.ShapeDtypeStruct((row_count, channels), jnp.float32),
            jax.ShapeDtypeStruct((row_count, channels), jnp.float32),
            jax.ShapeDtypeStruct((devices, mode_count, channels), jnp.bfloat16),
        ],
        block,
        [pltpu.VMEM((mode_count, block), jnp.float32)],
    )
    finals = lax.all_to_all(finals_out, "context", 0, 0, tiled=True)
    (hidden_out,) = channel_blocks(
        back_kernel,
        index,
        [
            local_out,
            decay_rates,
            residues,
            finals,
            hyena_state,
            filtered1,
            product,
            residual,
            skip_weight[None, :],
        ],
        [jax.ShapeDtypeStruct((ways, row_count, channels), jnp.bfloat16)],
        block,
    )
    tensor_index = lax.axis_index("tensor").astype(jnp.int32).reshape(1)
    gains = norm_gain.reshape(ways, 1, channels)
    weights3 = qkv_weight.transpose(1, 0, 2)
    own_gain = lax.dynamic_index_in_dim(gains, tensor_index[0], 0, keepdims=False)
    own = (hidden_out[0].astype(jnp.float32) * own_gain).astype(jnp.bfloat16)
    part = project_own(tensor_index, own, weights3)
    gathered = lax.all_to_all(hidden_out, "tensor", 0, 0, tiled=True)
    hidden_float = gathered.astype(jnp.float32)
    mean_square = jnp.sum(hidden_float * hidden_float, axis=(0, 2)) / (ways * channels)
    scaled = (hidden_float * gains).astype(jnp.bfloat16)
    total = project_rest(tensor_index, scaled, weights3, part)
    row_scale = lax.rsqrt(mean_square + NORM_EPSILON)
    projected = (
        (total * row_scale[None, :, None])
        .transpose(1, 0, 2)
        .reshape(row_count, 3, heads_here, HEAD)
    )
    query_index = device_index * row_count + jnp.arange(row_count, dtype=jnp.int32)
    positions = (start_offset[0] + query_index).astype(jnp.float32)
    queries = rotate(projected[:, 0], positions).astype(jnp.bfloat16)
    new_keys = rotate(projected[:, 1], positions).astype(jnp.bfloat16)
    new_values = projected[:, 2].astype(jnp.bfloat16)

    query_parts = (
        queries.reshape(2, half_rows, heads_here, HEAD)
        .transpose(2, 0, 1, 3)
        .reshape(devices, half_rows, HEAD)
    )
    sent = lax.all_to_all(
        jnp.concatenate([query_parts, by_head(new_keys), by_head(new_values)], axis=1),
        "context", 0, 0, tiled=True,
    )
    my_queries = sent[:, :half_rows]
    new_k = sent[:, half_rows : half_rows + row_count]
    new_v = sent[:, half_rows + row_count :]

    hist_rows = cache_k.shape[0] * cache_k.shape[1]
    all_k = jnp.concatenate([cache_k.reshape(-1, HEAD), new_k.reshape(-1, HEAD)], axis=0)
    all_v = jnp.concatenate([cache_v.reshape(-1, HEAD), new_v.reshape(-1, HEAD)], axis=0)
    q_flat = my_queries.reshape(-1, HEAD)
    src = jnp.arange(devices, dtype=jnp.int32)[:, None]
    row = jnp.arange(half_rows, dtype=jnp.int32)[None, :]
    query_pos = (src * row_count + (device_index % 2) * half_rows + row).reshape(-1)
    mine = attend(q_flat, all_k, all_v, query_pos, hist_rows).reshape(devices, half_rows, HEAD)
    back = lax.all_to_all(mine, "context", 0, 0, tiled=True)
    attended = (
        back.reshape(heads_here, 2, half_rows, HEAD)
        .transpose(1, 2, 0, 3)
        .reshape(row_count, head_width)
    )
    return attended


def solution(mesh):
    placed = (
        P(("dp", "context"), None, "tensor"),
        P("dp", None, "tensor"),
        P(None, None, "tensor"),
        P(None, "tensor"),
        P(None, "tensor"),
        P("dp", "tensor"),
        P("tensor"),
        P(("dp", "context"), "tensor"),
        P(),
        P(None, None, "tensor"),
        P("dp"),
        P(("dp", "context"), "tensor"),
        P(("dp", "context"), "tensor"),
    )
    return jax.shard_map(
        shards,
        mesh=mesh,
        in_specs=placed,
        out_specs=P(("dp", "context"), "tensor"),
        check_vma=False,
    )
```

```python
import functools
import math

import jax
import jax.numpy as jnp
from jax import lax
from jax.experimental import pallas as pl
from jax.experimental.pallas import tpu as pltpu
from jax.sharding import PartitionSpec as P

HEAD = 128


ROTARY_BASE = 1000000.0
NORM_EPSILON = 1e-06


def shifted(x, axis, by):
    devices = lax.axis_size(axis)
    pairs = [(i, i + by) for i in range(devices) if 0 <= i + by < devices]
    return lax.ppermute(x, axis, pairs)


def rotate(features, positions):
    half_width = features.shape[-1] // 2
    exponents = jnp.arange(half_width, dtype=jnp.float32) * (2.0 / features.shape[-1])
    frequency = jnp.exp(-math.log(ROTARY_BASE) * exponents)
    angles = positions[:, None] * frequency[None, :]
    cosine = jnp.cos(angles)[:, None, :]
    sine_values = jnp.sin(angles)[:, None, :]
    front = features[..., :half_width]
    back = features[..., half_width:]
    return jnp.concatenate(
        [front * cosine - back * sine_values, back * cosine + front * sine_values], axis=-1
    )


def front_kernel(
    idx_ref, s_ref, recv_ref, tail_ref, tap_ref, rate_ref, res_ref,
    prod_ref, f1_ref, out_ref, fin_ref, fin_scr,
):
    length = s_ref.shape[1]
    mode_count = rate_ref.shape[0]
    row = lax.broadcasted_iota(jnp.int32, (length, s_ref.shape[2]), 0)
    filtered = []
    for i in range(3):
        now = s_ref[i].astype(jnp.float32)
        before = jnp.where(
            idx_ref[0] == 0, tail_ref[i].astype(jnp.float32), recv_ref[i].astype(jnp.float32)
        )
        back1 = jnp.where(row == 0, before[1:2], pltpu.roll(now, 1, 0))
        back2 = jnp.where(
            row == 0, before[0:1], jnp.where(row == 1, before[1:2], pltpu.roll(now, 2, 0))
        )
        taps = tap_ref[:, i, :]
        filtered.append(taps[0:1] * now + taps[1:2] * back1 + taps[2:3] * back2)
    product = (filtered[0] * filtered[2]).astype(jnp.bfloat16)
    prod_ref[...] = product
    f1_ref[...] = filtered[1]
    x = product.astype(jnp.float32)
    rows = lax.broadcasted_iota(jnp.int32, (length, length), 0)
    cols = lax.broadcasted_iota(jnp.int32, (length, length), 1)
    lower = (rows >= cols).astype(jnp.bfloat16)
    offsets = lax.broadcasted_iota(jnp.int32, (length, 1), 0).astype(jnp.float32)
    gains = jnp.sqrt(1.0 - jnp.exp(-2.0 * rate_ref[...]))
    rgains = res_ref[...] * gains
    total = jnp.zeros(x.shape, jnp.float32)
    for m in range(mode_count):
        rate = rate_ref[m : m + 1, :]
        terms = jnp.exp(rate * offsets) * x
        high = terms.astype(jnp.bfloat16)
        low = (terms - high.astype(jnp.float32)).astype(jnp.bfloat16)
        prefix = jnp.dot(lower, high, preferred_element_type=jnp.float32) + jnp.dot(
            lower, low, preferred_element_type=jnp.float32
        )
        total = total + rgains[m : m + 1, :] * jnp.exp(-rate * offsets) * prefix
        fin_scr[m : m + 1, :] = (
            gains[m : m + 1, :] * jnp.exp(-rate * (length - 1.0)) * prefix[length - 1 : length, :]
        )
    out_ref[...] = total
    fin_ref[...] = jnp.broadcast_to(fin_scr[...][None], fin_ref.shape).astype(fin_ref.dtype)


def back_kernel(
    idx_ref, local_ref, rate_ref, res_ref, fin_ref, hs_ref,
    f1_ref, prod_ref, resid_ref, skip_ref, out_ref,
):
    length = local_ref.shape[0]
    mode_count = rate_ref.shape[0]
    rates = rate_ref[...]
    me = idx_ref[0]
    incoming = jnp.exp(-rates * (me * length).astype(jnp.float32)) * hs_ref[...]
    for src in range(fin_ref.shape[0]):
        steps_back = (jnp.maximum(me - 1 - src, 0) * length).astype(jnp.float32)
        weight_src = jnp.where(src < me, jnp.exp(-rates * steps_back), 0.0)
        incoming = incoming + weight_src * fin_ref[src].astype(jnp.float32)
    weight = res_ref[...] * incoming
    steps = lax.broadcasted_iota(jnp.int32, (length, 1), 0).astype(jnp.float32) + 1.0
    total = local_ref[...]
    for m in range(mode_count):
        total = total + weight[m : m + 1, :] * jnp.exp(-rates[m : m + 1, :] * steps)
    long_out = total.astype(jnp.bfloat16).astype(jnp.float32)
    hidden = (
        resid_ref[...].astype(jnp.float32)
        + f1_ref[...] * (long_out + skip_ref[...] * prod_ref[...].astype(jnp.float32))
    ).astype(out_ref.dtype)
    out_ref[...] = jnp.broadcast_to(hidden[None], out_ref.shape)


def channel_blocks(kernel, index, inputs, outputs, block, scratch=()):
    def spec(shape):
        lead = tuple(0 for _ in shape[:-1])
        return pl.BlockSpec(tuple(shape[:-1]) + (block,), lambda j, idx: lead + (j,))

    grid_spec = pltpu.PrefetchScalarGridSpec(
        num_scalar_prefetch=1,
        grid=(outputs[0].shape[-1] // block,),
        in_specs=[spec(a.shape) for a in inputs],
        out_specs=[spec(o.shape) for o in outputs],
        scratch_shapes=list(scratch),
    )
    return pl.pallas_call(kernel, grid_spec=grid_spec, out_shape=outputs)(index, *inputs)


def attention_kernel(scale, history, q_ref, k_ref, v_ref, qpos_ref, out_ref):
    q = q_ref[...]
    contract = (((1,), (1,)), ((), ()))
    old_scores = (
        lax.dot_general(q, k_ref[:history], contract, preferred_element_type=jnp.float32) * scale
    )
    new_scores = (
        lax.dot_general(q, k_ref[history:], contract, preferred_element_type=jnp.float32) * scale
    )
    new_pos = lax.broadcasted_iota(jnp.int32, (1, new_scores.shape[1]), 1)
    new_scores = jnp.where(new_pos <= qpos_ref[...], new_scores, -jnp.inf)
    row_max = jnp.maximum(
        jnp.max(old_scores, axis=1, keepdims=True), jnp.max(new_scores, axis=1, keepdims=True)
    )
    old_w = jnp.exp(old_scores - row_max).astype(jnp.bfloat16)
    new_w = jnp.exp(new_scores - row_max).astype(jnp.bfloat16)
    ones = jnp.ones((history, 128), jnp.bfloat16)
    weight_sum = jnp.dot(old_w, ones, preferred_element_type=jnp.float32) + jnp.dot(
        new_w, ones[: new_w.shape[1]], preferred_element_type=jnp.float32
    )
    numerator = jnp.dot(old_w, v_ref[:history], preferred_element_type=jnp.float32) + jnp.dot(
        new_w, v_ref[history:], preferred_element_type=jnp.float32
    )
    out_ref[...] = (numerator / weight_sum[:, :1]).astype(out_ref.dtype)


def attend(queries, keys, values, query_pos, history, block=512):
    rows, width = queries.shape
    key_rows = keys.shape[0]
    return pl.pallas_call(
        functools.partial(attention_kernel, 1.0 / math.sqrt(width), history),
        grid=(rows // block,),
        in_specs=[
            pl.BlockSpec((block, width), lambda i: (i, 0)),
            pl.BlockSpec((key_rows, width), lambda i: (0, 0)),
            pl.BlockSpec((key_rows, width), lambda i: (0, 0)),
            pl.BlockSpec((block, 1), lambda i: (i, 0)),
        ],
        out_specs=pl.BlockSpec((block, width), lambda i: (i, 0)),
        out_shape=jax.ShapeDtypeStruct((rows, width), jnp.bfloat16),
        compiler_params=pltpu.CompilerParams(vmem_limit_bytes=48 * 1024 * 1024),
    )(queries, keys, values, query_pos.reshape(rows, 1))


def project_kernel(x_ref, w_ref, out_ref):
    out_ref[...] = jnp.dot(x_ref[...], w_ref[...], preferred_element_type=jnp.float32)


def project(x, w, block=1024):
    rows, depth = x.shape
    groups, _, width = w.shape
    return pl.pallas_call(
        project_kernel,
        grid=(groups, width // block),
        in_specs=[
            pl.BlockSpec((rows, depth), lambda g, j: (0, 0)),
            pl.BlockSpec((None, depth, block), lambda g, j: (g, 0, j)),
        ],
        out_specs=pl.BlockSpec((None, rows, block), lambda g, j: (g, 0, j)),
        out_shape=jax.ShapeDtypeStruct((groups, rows, width), jnp.float32),
        compiler_params=pltpu.CompilerParams(vmem_limit_bytes=48 * 1024 * 1024),
        cost_estimate=pl.CostEstimate(
            flops=2 * rows * depth * width * groups,
            bytes_accessed=2 * (rows * depth + groups * depth * width) + 4 * groups * rows * width,
            transcendentals=0,
        ),
    )(x, w)


def shards(
    streams,
    stream_tail,
    short_taps,
    decay_rates,
    residues,
    hyena_state,
    skip_weight,
    residual,
    norm_gain,
    qkv_weight,
    start_offset,
    cache_keys,
    cache_values,
):
    row_count = streams.shape[0]
    tap_count = short_taps.shape[0]
    devices = lax.axis_size("context")
    device_index = lax.axis_index("context")
    head_width = qkv_weight.shape[2]
    heads_here = head_width // HEAD
    half_rows = row_count // 2

    def by_head(block):
        per_head = block.reshape(row_count, heads_here, HEAD).transpose(1, 0, 2)
        return jnp.repeat(per_head, devices // heads_here, axis=0)

    cache_kv = lax.all_to_all(
        jnp.concatenate([by_head(cache_keys), by_head(cache_values)], axis=1),
        "context", 0, 0, tiled=True,
    )
    cache_k, cache_v = cache_kv[:, :row_count], cache_kv[:, row_count:]

    received = shifted(streams[row_count - (tap_count - 1) :], "context", 1)
    channels = streams.shape[2]
    mode_count = decay_rates.shape[0]
    ways = lax.axis_size("tensor")
    index = device_index.astype(jnp.int32).reshape(1)
    block = 256
    product, filtered1, local_out, finals_out = channel_blocks(
        front_kernel,
        index,
        [
            streams.transpose(1, 0, 2),
            received.transpose(1, 0, 2),
            stream_tail.transpose(1, 0, 2),
            short_taps,
            decay_rates,
            residues,
        ],
        [
            jax.ShapeDtypeStruct((row_count, channels), jnp.bfloat16),
            jax.ShapeDtypeStruct((row_count, channels), jnp.float32),
            jax.ShapeDtypeStruct((row_count, channels), jnp.float32),
            jax.ShapeDtypeStruct((devices, mode_count, channels), jnp.bfloat16),
        ],
        block,
        [pltpu.VMEM((mode_count, block), jnp.float32)],
    )
    finals = lax.all_to_all(finals_out, "context", 0, 0, tiled=True)
    (hidden_out,) = channel_blocks(
        back_kernel,
        index,
        [
            local_out,
            decay_rates,
            residues,
            finals,
            hyena_state,
            filtered1,
            product,
            residual,
            skip_weight[None, :],
        ],
        [jax.ShapeDtypeStruct((ways, row_count, channels), jnp.bfloat16)],
        block,
    )
    gathered = lax.all_to_all(hidden_out, "tensor", 0, 0, tiled=True)
    gathered = gathered.transpose(1, 0, 2).reshape(row_count, ways * channels)
    hidden_float = gathered.astype(jnp.float32)
    mean_square = jnp.mean(hidden_float * hidden_float, axis=1, keepdims=True)
    normed = (hidden_float * lax.rsqrt(mean_square + NORM_EPSILON) * norm_gain[None, :]).astype(
        jnp.bfloat16
    )
    projected = (
        project(normed, qkv_weight.transpose(1, 0, 2))
        .transpose(1, 0, 2)
        .reshape(row_count, 3, heads_here, HEAD)
    )
    query_index = device_index * row_count + jnp.arange(row_count, dtype=jnp.int32)
    positions = (start_offset[0] + query_index).astype(jnp.float32)
    queries = rotate(projected[:, 0], positions).astype(jnp.bfloat16)
    new_keys = rotate(projected[:, 1], positions).astype(jnp.bfloat16)
    new_values = projected[:, 2].astype(jnp.bfloat16)

    query_parts = (
        queries.reshape(2, half_rows, heads_here, HEAD)
        .transpose(2, 0, 1, 3)
        .reshape(devices, half_rows, HEAD)
    )
    sent = lax.all_to_all(
        jnp.concatenate([query_parts, by_head(new_keys), by_head(new_values)], axis=1),
        "context", 0, 0, tiled=True,
    )
    my_queries = sent[:, :half_rows]
    new_k = sent[:, half_rows : half_rows + row_count]
    new_v = sent[:, half_rows + row_count :]

    hist_rows = cache_k.shape[0] * cache_k.shape[1]
    all_k = jnp.concatenate([cache_k.reshape(-1, HEAD), new_k.reshape(-1, HEAD)], axis=0)
    all_v = jnp.concatenate([cache_v.reshape(-1, HEAD), new_v.reshape(-1, HEAD)], axis=0)
    q_flat = my_queries.reshape(-1, HEAD)
    src = jnp.arange(devices, dtype=jnp.int32)[:, None]
    row = jnp.arange(half_rows, dtype=jnp.int32)[None, :]
    query_pos = (src * row_count + (device_index % 2) * half_rows + row).reshape(-1)
    mine = attend(q_flat, all_k, all_v, query_pos, hist_rows).reshape(devices, half_rows, HEAD)
    back = lax.all_to_all(mine, "context", 0, 0, tiled=True)
    attended = (
        back.reshape(heads_here, 2, half_rows, HEAD)
        .transpose(1, 2, 0, 3)
        .reshape(row_count, head_width)
    )
    return attended


def solution(mesh):
    placed = (
        P(("dp", "context"), None, "tensor"),
        P("dp", None, "tensor"),
        P(None, None, "tensor"),
        P(None, "tensor"),
        P(None, "tensor"),
        P("dp", "tensor"),
        P("tensor"),
        P(("dp", "context"), "tensor"),
        P(),
        P(None, None, "tensor"),
        P("dp"),
        P(("dp", "context"), "tensor"),
        P(("dp", "context"), "tensor"),
    )
    return jax.shard_map(
        shards,
        mesh=mesh,
        in_specs=placed,
        out_specs=P(("dp", "context"), "tensor"),
        check_vma=False,
    )
```

```python
import functools
import math

import jax
import jax.numpy as jnp
from jax import lax
from jax.experimental import pallas as pl
from jax.experimental.pallas import tpu as pltpu
from jax.sharding import PartitionSpec as P

HEAD = 128


ROTARY_BASE = 1000000.0
NORM_EPSILON = 1e-06


def shifted(x, axis, by):
    devices = lax.axis_size(axis)
    pairs = [(i, i + by) for i in range(devices) if 0 <= i + by < devices]
    return lax.ppermute(x, axis, pairs)


def rotate(features, positions):
    half_width = features.shape[-1] // 2
    exponents = jnp.arange(half_width, dtype=jnp.float32) * (2.0 / features.shape[-1])
    frequency = jnp.exp(-math.log(ROTARY_BASE) * exponents)
    angles = positions[:, None] * frequency[None, :]
    cosine = jnp.cos(angles)[:, None, :]
    sine_values = jnp.sin(angles)[:, None, :]
    front = features[..., :half_width]
    back = features[..., half_width:]
    return jnp.concatenate(
        [front * cosine - back * sine_values, back * cosine + front * sine_values], axis=-1
    )


def front_kernel(
    idx_ref, s_ref, recv_ref, tail_ref, tap_ref, rate_ref, res_ref,
    prod_ref, f1_ref, out_ref, fin_ref, fin_scr,
):
    length = s_ref.shape[1]
    mode_count = rate_ref.shape[0]
    row = lax.broadcasted_iota(jnp.int32, (length, s_ref.shape[2]), 0)
    filtered = []
    for i in range(3):
        now = s_ref[i].astype(jnp.float32)
        before = jnp.where(
            idx_ref[0] == 0, tail_ref[i].astype(jnp.float32), recv_ref[i].astype(jnp.float32)
        )
        back1 = jnp.where(row == 0, before[1:2], pltpu.roll(now, 1, 0))
        back2 = jnp.where(
            row == 0, before[0:1], jnp.where(row == 1, before[1:2], pltpu.roll(now, 2, 0))
        )
        taps = tap_ref[:, i, :]
        filtered.append(taps[0:1] * now + taps[1:2] * back1 + taps[2:3] * back2)
    product = (filtered[0] * filtered[2]).astype(jnp.bfloat16)
    prod_ref[...] = product
    f1_ref[...] = filtered[1]
    x = product.astype(jnp.float32)
    rows = lax.broadcasted_iota(jnp.int32, (length, length), 0)
    cols = lax.broadcasted_iota(jnp.int32, (length, length), 1)
    lower = (rows >= cols).astype(jnp.bfloat16)
    offsets = lax.broadcasted_iota(jnp.int32, (length, 1), 0).astype(jnp.float32)
    gains = jnp.sqrt(1.0 - jnp.exp(-2.0 * rate_ref[...]))
    rgains = res_ref[...] * gains
    total = jnp.zeros(x.shape, jnp.float32)
    for m in range(mode_count):
        rate = rate_ref[m : m + 1, :]
        terms = jnp.exp(rate * offsets) * x
        high = terms.astype(jnp.bfloat16)
        low = (terms - high.astype(jnp.float32)).astype(jnp.bfloat16)
        prefix = jnp.dot(lower, high, preferred_element_type=jnp.float32) + jnp.dot(
            lower, low, preferred_element_type=jnp.float32
        )
        total = total + rgains[m : m + 1, :] * jnp.exp(-rate * offsets) * prefix
        fin_scr[m : m + 1, :] = (
            gains[m : m + 1, :] * jnp.exp(-rate * (length - 1.0)) * prefix[length - 1 : length, :]
        )
    out_ref[...] = total
    fin_ref[...] = jnp.broadcast_to(fin_scr[...][None], fin_ref.shape).astype(fin_ref.dtype)


def back_kernel(
    idx_ref, local_ref, rate_ref, res_ref, fin_ref, hs_ref,
    f1_ref, prod_ref, resid_ref, skip_ref, out_ref,
):
    length = local_ref.shape[0]
    mode_count = rate_ref.shape[0]
    rates = rate_ref[...]
    me = idx_ref[0]
    incoming = jnp.exp(-rates * (me * length).astype(jnp.float32)) * hs_ref[...]
    for src in range(fin_ref.shape[0]):
        steps_back = (jnp.maximum(me - 1 - src, 0) * length).astype(jnp.float32)
        weight_src = jnp.where(src < me, jnp.exp(-rates * steps_back), 0.0)
        incoming = incoming + weight_src * fin_ref[src].astype(jnp.float32)
    weight = res_ref[...] * incoming
    steps = lax.broadcasted_iota(jnp.int32, (length, 1), 0).astype(jnp.float32) + 1.0
    total = local_ref[...]
    for m in range(mode_count):
        total = total + weight[m : m + 1, :] * jnp.exp(-rates[m : m + 1, :] * steps)
    long_out = total.astype(jnp.bfloat16).astype(jnp.float32)
    hidden = (
        resid_ref[...].astype(jnp.float32)
        + f1_ref[...] * (long_out + skip_ref[...] * prod_ref[...].astype(jnp.float32))
    ).astype(out_ref.dtype)
    out_ref[...] = jnp.broadcast_to(hidden[None], out_ref.shape)


def channel_blocks(kernel, index, inputs, outputs, block, scratch=()):
    def spec(shape):
        lead = tuple(0 for _ in shape[:-1])
        return pl.BlockSpec(tuple(shape[:-1]) + (block,), lambda j, idx: lead + (j,))

    grid_spec = pltpu.PrefetchScalarGridSpec(
        num_scalar_prefetch=1,
        grid=(outputs[0].shape[-1] // block,),
        in_specs=[spec(a.shape) for a in inputs],
        out_specs=[spec(o.shape) for o in outputs],
        scratch_shapes=list(scratch),
    )
    return pl.pallas_call(kernel, grid_spec=grid_spec, out_shape=outputs)(index, *inputs)


def cache_attention_kernel(scale, q_ref, k_ref, v_ref, max_ref, sum_ref, num_ref):
    scores = (
        lax.dot_general(
            q_ref[...], k_ref[...], (((1,), (1,)), ((), ())), preferred_element_type=jnp.float32
        )
        * scale
    )
    row_max = jnp.max(scores, axis=1, keepdims=True)
    weights = jnp.exp(scores - row_max).astype(jnp.bfloat16)
    ones = jnp.ones((weights.shape[1], 128), jnp.bfloat16)
    max_ref[...] = jnp.broadcast_to(row_max, max_ref.shape)
    sum_ref[...] = jnp.dot(weights, ones, preferred_element_type=jnp.float32)
    num_ref[...] = jnp.dot(weights, v_ref[...], preferred_element_type=jnp.float32)


def new_attention_kernel(scale, q_ref, k_ref, v_ref, qpos_ref, max_ref, sum_ref, num_ref, out_ref):
    scores = (
        lax.dot_general(
            q_ref[...], k_ref[...], (((1,), (1,)), ((), ())), preferred_element_type=jnp.float32
        )
        * scale
    )
    key_pos = lax.broadcasted_iota(jnp.int32, (1, scores.shape[1]), 1)
    scores = jnp.where(key_pos <= qpos_ref[...], scores, -jnp.inf)
    old_max = max_ref[:, :1]
    row_max = jnp.maximum(old_max, jnp.max(scores, axis=1, keepdims=True))
    rescale = jnp.exp(old_max - row_max)
    weights = jnp.exp(scores - row_max).astype(jnp.bfloat16)
    ones = jnp.ones((weights.shape[1], 128), jnp.bfloat16)
    weight_sum = sum_ref[:, :1] * rescale + jnp.dot(
        weights, ones, preferred_element_type=jnp.float32
    )[:, :1]
    numerator = num_ref[...] * rescale + jnp.dot(
        weights, v_ref[...], preferred_element_type=jnp.float32
    )
    out_ref[...] = (numerator / weight_sum).astype(out_ref.dtype)


def attend_cache(queries, keys, values, block=512):
    rows, width = queries.shape
    key_rows = keys.shape[0]
    piece = jax.ShapeDtypeStruct((rows, width), jnp.float32)
    row_spec = pl.BlockSpec((block, width), lambda i: (i, 0))
    return pl.pallas_call(
        functools.partial(cache_attention_kernel, 1.0 / math.sqrt(width)),
        grid=(rows // block,),
        in_specs=[
            row_spec,
            pl.BlockSpec((key_rows, width), lambda i: (0, 0)),
            pl.BlockSpec((key_rows, width), lambda i: (0, 0)),
        ],
        out_specs=[row_spec, row_spec, row_spec],
        out_shape=[piece, piece, piece],
        compiler_params=pltpu.CompilerParams(vmem_limit_bytes=48 * 1024 * 1024),
        cost_estimate=pl.CostEstimate(
            flops=6 * rows * key_rows * width,
            bytes_accessed=2 * rows * width + 4 * key_rows * width + 12 * rows * width,
            transcendentals=rows * key_rows,
        ),
    )(queries, keys, values)


def attend_new(queries, keys, values, query_pos, pieces, block=512):
    rows, width = queries.shape
    key_rows = keys.shape[0]
    row_spec = pl.BlockSpec((block, width), lambda i: (i, 0))
    return pl.pallas_call(
        functools.partial(new_attention_kernel, 1.0 / math.sqrt(width)),
        grid=(rows // block,),
        in_specs=[
            row_spec,
            pl.BlockSpec((key_rows, width), lambda i: (0, 0)),
            pl.BlockSpec((key_rows, width), lambda i: (0, 0)),
            pl.BlockSpec((block, 1), lambda i: (i, 0)),
            row_spec,
            row_spec,
            row_spec,
        ],
        out_specs=row_spec,
        out_shape=jax.ShapeDtypeStruct((rows, width), jnp.bfloat16),
        compiler_params=pltpu.CompilerParams(vmem_limit_bytes=48 * 1024 * 1024),
    )(queries, keys, values, query_pos.reshape(rows, 1), *pieces)


def project_kernel(x_ref, w_ref, out_ref):
    out_ref[...] = jnp.dot(x_ref[...], w_ref[...], preferred_element_type=jnp.float32)


def project(x, w, first, groups, block=1024):
    rows, depth = x.shape
    width = w.shape[2]
    return pl.pallas_call(
        project_kernel,
        grid=(groups, width // block),
        in_specs=[
            pl.BlockSpec((rows, depth), lambda g, j: (0, 0)),
            pl.BlockSpec((None, depth, block), lambda g, j: (g + first, 0, j)),
        ],
        out_specs=pl.BlockSpec((None, rows, block), lambda g, j: (g, 0, j)),
        out_shape=jax.ShapeDtypeStruct((groups, rows, width), jnp.float32),
        compiler_params=pltpu.CompilerParams(vmem_limit_bytes=48 * 1024 * 1024),
        cost_estimate=pl.CostEstimate(
            flops=2 * rows * depth * width * groups,
            bytes_accessed=2 * (rows * depth + groups * depth * width) + 4 * groups * rows * width,
            transcendentals=0,
        ),
    )(x, w)


def shards(
    streams,
    stream_tail,
    short_taps,
    decay_rates,
    residues,
    hyena_state,
    skip_weight,
    residual,
    norm_gain,
    qkv_weight,
    start_offset,
    cache_keys,
    cache_values,
):
    row_count = streams.shape[0]
    tap_count = short_taps.shape[0]
    devices = lax.axis_size("context")
    device_index = lax.axis_index("context")
    head_width = qkv_weight.shape[2]
    heads_here = head_width // HEAD
    half_rows = row_count // 2

    def by_head(block):
        per_head = block.reshape(row_count, heads_here, HEAD).transpose(1, 0, 2)
        return jnp.repeat(per_head, devices // heads_here, axis=0)

    cache_kv = lax.all_to_all(
        jnp.concatenate([by_head(cache_keys), by_head(cache_values)], axis=1),
        "context", 0, 0, tiled=True,
    )
    cache_k, cache_v = cache_kv[:, :row_count], cache_kv[:, row_count:]

    received = shifted(streams[row_count - (tap_count - 1) :], "context", 1)
    channels = streams.shape[2]
    mode_count = decay_rates.shape[0]
    ways = lax.axis_size("tensor")
    index = device_index.astype(jnp.int32).reshape(1)
    block = 256
    product, filtered1, local_out, finals_out = channel_blocks(
        front_kernel,
        index,
        [
            streams.transpose(1, 0, 2),
            received.transpose(1, 0, 2),
            stream_tail.transpose(1, 0, 2),
            short_taps,
            decay_rates,
            residues,
        ],
        [
            jax.ShapeDtypeStruct((row_count, channels), jnp.bfloat16),
            jax.ShapeDtypeStruct((row_count, channels), jnp.float32),
            jax.ShapeDtypeStruct((row_count, channels), jnp.float32),
            jax.ShapeDtypeStruct((devices, mode_count, channels), jnp.bfloat16),
        ],
        block,
        [pltpu.VMEM((mode_count, block), jnp.float32)],
    )
    finals = lax.all_to_all(finals_out, "context", 0, 0, tiled=True)
    (hidden_out,) = channel_blocks(
        back_kernel,
        index,
        [
            local_out,
            decay_rates,
            residues,
            finals,
            hyena_state,
            filtered1,
            product,
            residual,
            skip_weight[None, :],
        ],
        [jax.ShapeDtypeStruct((ways, row_count, channels), jnp.bfloat16)],
        block,
    )
    gathered = lax.all_to_all(hidden_out, "tensor", 0, 0, tiled=True)
    gathered = gathered.transpose(1, 0, 2).reshape(row_count, ways * channels)
    hidden_float = gathered.astype(jnp.float32)
    mean_square = jnp.mean(hidden_float * hidden_float, axis=1, keepdims=True)
    normed = (hidden_float * lax.rsqrt(mean_square + NORM_EPSILON) * norm_gain[None, :]).astype(
        jnp.bfloat16
    )
    weights3 = qkv_weight.transpose(1, 0, 2)
    query_index = device_index * row_count + jnp.arange(row_count, dtype=jnp.int32)
    positions = (start_offset[0] + query_index).astype(jnp.float32)
    query_proj = project(normed, weights3, 0, 1)[0].reshape(row_count, heads_here, HEAD)
    queries = rotate(query_proj, positions).astype(jnp.bfloat16)
    query_parts = (
        queries.reshape(2, half_rows, heads_here, HEAD)
        .transpose(2, 0, 1, 3)
        .reshape(devices, half_rows, HEAD)
    )
    my_queries = lax.all_to_all(query_parts, "context", 0, 0, tiled=True)
    kv_proj = project(normed, weights3, 1, 2).reshape(2, row_count, heads_here, HEAD)
    new_keys = rotate(kv_proj[0], positions).astype(jnp.bfloat16)
    new_values = kv_proj[1].astype(jnp.bfloat16)
    new_kv = lax.all_to_all(
        jnp.concatenate([by_head(new_keys), by_head(new_values)], axis=1),
        "context", 0, 0, tiled=True,
    )
    q_flat = my_queries.reshape(-1, HEAD)
    pieces = attend_cache(q_flat, cache_k.reshape(-1, HEAD), cache_v.reshape(-1, HEAD))
    src = jnp.arange(devices, dtype=jnp.int32)[:, None]
    row = jnp.arange(half_rows, dtype=jnp.int32)[None, :]
    query_pos = (src * row_count + (device_index % 2) * half_rows + row).reshape(-1)
    mine = attend_new(
        q_flat,
        new_kv[:, :row_count].reshape(-1, HEAD),
        new_kv[:, row_count:].reshape(-1, HEAD),
        query_pos,
        pieces,
    ).reshape(devices, half_rows, HEAD)
    back = lax.all_to_all(mine, "context", 0, 0, tiled=True)
    attended = (
        back.reshape(heads_here, 2, half_rows, HEAD)
        .transpose(1, 2, 0, 3)
        .reshape(row_count, head_width)
    )
    return attended


def solution(mesh):
    placed = (
        P(("dp", "context"), None, "tensor"),
        P("dp", None, "tensor"),
        P(None, None, "tensor"),
        P(None, "tensor"),
        P(None, "tensor"),
        P("dp", "tensor"),
        P("tensor"),
        P(("dp", "context"), "tensor"),
        P(),
        P(None, None, "tensor"),
        P("dp"),
        P(("dp", "context"), "tensor"),
        P(("dp", "context"), "tensor"),
    )
    return jax.shard_map(
        shards,
        mesh=mesh,
        in_specs=placed,
        out_specs=P(("dp", "context"), "tensor"),
        check_vma=False,
    )
```

```python
import functools
import math

import jax
import jax.numpy as jnp
from jax import lax
from jax.experimental import pallas as pl
from jax.experimental.pallas import tpu as pltpu
from jax.sharding import PartitionSpec as P

HEAD = 128


ROTARY_BASE = 1000000.0
NORM_EPSILON = 1e-06


def shifted(x, axis, by):
    devices = lax.axis_size(axis)
    pairs = [(i, i + by) for i in range(devices) if 0 <= i + by < devices]
    return lax.ppermute(x, axis, pairs)


def rotate(features, positions):
    half_width = features.shape[-1] // 2
    exponents = jnp.arange(half_width, dtype=jnp.float32) * (2.0 / features.shape[-1])
    frequency = jnp.exp(-math.log(ROTARY_BASE) * exponents)
    angles = positions[:, None] * frequency[None, :]
    cosine = jnp.cos(angles)[:, None, :]
    sine_values = jnp.sin(angles)[:, None, :]
    front = features[..., :half_width]
    back = features[..., half_width:]
    return jnp.concatenate(
        [front * cosine - back * sine_values, back * cosine + front * sine_values], axis=-1
    )


def front_kernel(
    idx_ref, s_ref, recv_ref, tail_ref, tap_ref, rate_ref, res_ref,
    prod_ref, f1_ref, out_ref, fin_ref, fin_scr,
):
    length = s_ref.shape[1]
    mode_count = rate_ref.shape[0]
    row = lax.broadcasted_iota(jnp.int32, (length, s_ref.shape[2]), 0)
    filtered = []
    for i in range(3):
        now = s_ref[i].astype(jnp.float32)
        before = jnp.where(
            idx_ref[0] == 0, tail_ref[i].astype(jnp.float32), recv_ref[i].astype(jnp.float32)
        )
        back1 = jnp.where(row == 0, before[1:2], pltpu.roll(now, 1, 0))
        back2 = jnp.where(
            row == 0, before[0:1], jnp.where(row == 1, before[1:2], pltpu.roll(now, 2, 0))
        )
        taps = tap_ref[:, i, :]
        filtered.append(taps[0:1] * now + taps[1:2] * back1 + taps[2:3] * back2)
    product = (filtered[0] * filtered[2]).astype(jnp.bfloat16)
    prod_ref[...] = product
    f1_ref[...] = filtered[1]
    x = product.astype(jnp.float32)
    rows = lax.broadcasted_iota(jnp.int32, (length, length), 0)
    cols = lax.broadcasted_iota(jnp.int32, (length, length), 1)
    lower = (rows >= cols).astype(jnp.bfloat16)
    offsets = lax.broadcasted_iota(jnp.int32, (length, 1), 0).astype(jnp.float32)
    gains = jnp.sqrt(1.0 - jnp.exp(-2.0 * rate_ref[...]))
    rgains = res_ref[...] * gains
    total = jnp.zeros(x.shape, jnp.float32)
    for m in range(mode_count):
        rate = rate_ref[m : m + 1, :]
        terms = jnp.exp(rate * offsets) * x
        high = terms.astype(jnp.bfloat16)
        low = (terms - high.astype(jnp.float32)).astype(jnp.bfloat16)
        prefix = jnp.dot(lower, high, preferred_element_type=jnp.float32) + jnp.dot(
            lower, low, preferred_element_type=jnp.float32
        )
        total = total + rgains[m : m + 1, :] * jnp.exp(-rate * offsets) * prefix
        fin_scr[m : m + 1, :] = (
            gains[m : m + 1, :] * jnp.exp(-rate * (length - 1.0)) * prefix[length - 1 : length, :]
        )
    out_ref[...] = total
    fin_ref[...] = jnp.broadcast_to(fin_scr[...][None], fin_ref.shape).astype(fin_ref.dtype)


def back_kernel(
    idx_ref, local_ref, rate_ref, res_ref, fin_ref, hs_ref,
    f1_ref, prod_ref, resid_ref, skip_ref, out_ref,
):
    length = local_ref.shape[0]
    mode_count = rate_ref.shape[0]
    rates = rate_ref[...]
    me = idx_ref[0]
    incoming = jnp.exp(-rates * (me * length).astype(jnp.float32)) * hs_ref[...]
    for src in range(fin_ref.shape[0]):
        steps_back = (jnp.maximum(me - 1 - src, 0) * length).astype(jnp.float32)
        weight_src = jnp.where(src < me, jnp.exp(-rates * steps_back), 0.0)
        incoming = incoming + weight_src * fin_ref[src].astype(jnp.float32)
    weight = res_ref[...] * incoming
    steps = lax.broadcasted_iota(jnp.int32, (length, 1), 0).astype(jnp.float32) + 1.0
    total = local_ref[...]
    for m in range(mode_count):
        total = total + weight[m : m + 1, :] * jnp.exp(-rates[m : m + 1, :] * steps)
    long_out = total.astype(jnp.bfloat16).astype(jnp.float32)
    hidden = (
        resid_ref[...].astype(jnp.float32)
        + f1_ref[...] * (long_out + skip_ref[...] * prod_ref[...].astype(jnp.float32))
    ).astype(out_ref.dtype)
    out_ref[...] = jnp.broadcast_to(hidden[None], out_ref.shape)


def channel_blocks(kernel, index, inputs, outputs, block, scratch=()):
    def spec(shape):
        lead = tuple(0 for _ in shape[:-1])
        return pl.BlockSpec(tuple(shape[:-1]) + (block,), lambda j, idx: lead + (j,))

    grid_spec = pltpu.PrefetchScalarGridSpec(
        num_scalar_prefetch=1,
        grid=(outputs[0].shape[-1] // block,),
        in_specs=[spec(a.shape) for a in inputs],
        out_specs=[spec(o.shape) for o in outputs],
        scratch_shapes=list(scratch),
    )
    return pl.pallas_call(kernel, grid_spec=grid_spec, out_shape=outputs)(index, *inputs)


def cache_attention_kernel(scale, q_ref, k_ref, v_ref, max_ref, sum_ref, num_ref):
    scores = (
        lax.dot_general(
            q_ref[...], k_ref[...], (((1,), (1,)), ((), ())), preferred_element_type=jnp.float32
        )
        * scale
    )
    row_max = jnp.max(scores, axis=1, keepdims=True)
    weights = jnp.exp(scores - row_max).astype(jnp.bfloat16)
    ones = jnp.ones((weights.shape[1], 128), jnp.bfloat16)
    max_ref[...] = jnp.broadcast_to(row_max, max_ref.shape)
    sum_ref[...] = jnp.dot(weights, ones, preferred_element_type=jnp.float32)
    num_ref[...] = jnp.dot(weights, v_ref[...], preferred_element_type=jnp.float32)


def new_attention_kernel(scale, q_ref, k_ref, v_ref, qpos_ref, max_ref, sum_ref, num_ref, out_ref):
    scores = (
        lax.dot_general(
            q_ref[...], k_ref[...], (((1,), (1,)), ((), ())), preferred_element_type=jnp.float32
        )
        * scale
    )
    key_pos = lax.broadcasted_iota(jnp.int32, (1, scores.shape[1]), 1)
    scores = jnp.where(key_pos <= qpos_ref[...], scores, -jnp.inf)
    old_max = max_ref[:, :1]
    row_max = jnp.maximum(old_max, jnp.max(scores, axis=1, keepdims=True))
    rescale = jnp.exp(old_max - row_max)
    weights = jnp.exp(scores - row_max).astype(jnp.bfloat16)
    ones = jnp.ones((weights.shape[1], 128), jnp.bfloat16)
    weight_sum = sum_ref[:, :1] * rescale + jnp.dot(
        weights, ones, preferred_element_type=jnp.float32
    )[:, :1]
    numerator = num_ref[...] * rescale + jnp.dot(
        weights, v_ref[...], preferred_element_type=jnp.float32
    )
    out_ref[...] = (numerator / weight_sum).astype(out_ref.dtype)


def attend_cache(queries, keys, values, block=512):
    rows, width = queries.shape
    key_rows = keys.shape[0]
    piece = jax.ShapeDtypeStruct((rows, width), jnp.float32)
    row_spec = pl.BlockSpec((block, width), lambda i: (i, 0))
    return pl.pallas_call(
        functools.partial(cache_attention_kernel, 1.0 / math.sqrt(width)),
        grid=(rows // block,),
        in_specs=[
            row_spec,
            pl.BlockSpec((key_rows, width), lambda i: (0, 0)),
            pl.BlockSpec((key_rows, width), lambda i: (0, 0)),
        ],
        out_specs=[row_spec, row_spec, row_spec],
        out_shape=[piece, piece, piece],
        compiler_params=pltpu.CompilerParams(vmem_limit_bytes=48 * 1024 * 1024),
        cost_estimate=pl.CostEstimate(
            flops=6 * rows * key_rows * width,
            bytes_accessed=2 * rows * width + 4 * key_rows * width + 12 * rows * width,
            transcendentals=rows * key_rows,
        ),
    )(queries, keys, values)


def attend_new(queries, keys, values, query_pos, pieces, block=512):
    rows, width = queries.shape
    key_rows = keys.shape[0]
    row_spec = pl.BlockSpec((block, width), lambda i: (i, 0))
    return pl.pallas_call(
        functools.partial(new_attention_kernel, 1.0 / math.sqrt(width)),
        grid=(rows // block,),
        in_specs=[
            row_spec,
            pl.BlockSpec((key_rows, width), lambda i: (0, 0)),
            pl.BlockSpec((key_rows, width), lambda i: (0, 0)),
            pl.BlockSpec((block, 1), lambda i: (i, 0)),
            row_spec,
            row_spec,
            row_spec,
        ],
        out_specs=row_spec,
        out_shape=jax.ShapeDtypeStruct((rows, width), jnp.bfloat16),
        compiler_params=pltpu.CompilerParams(vmem_limit_bytes=48 * 1024 * 1024),
    )(queries, keys, values, query_pos.reshape(rows, 1), *pieces)


def project_kernel(x_ref, w_ref, out_ref):
    out_ref[...] = jnp.dot(x_ref[...], w_ref[...], preferred_element_type=jnp.float32)


def project_after_kernel(x_ref, w_ref, after_ref, out_ref):
    project_kernel(x_ref, w_ref, out_ref)


def project(x, w, first, groups, block=1024, after=None):
    rows, depth = x.shape
    width = w.shape[2]
    return pl.pallas_call(
        project_kernel if after is None else project_after_kernel,
        grid=(groups, width // block),
        in_specs=[
            pl.BlockSpec((rows, depth), lambda g, j: (0, 0)),
            pl.BlockSpec((None, depth, block), lambda g, j: (g + first, 0, j)),
        ]
        + ([] if after is None else [pl.BlockSpec(after.shape, lambda g, j: (0,) * after.ndim)]),
        out_specs=pl.BlockSpec((None, rows, block), lambda g, j: (g, 0, j)),
        out_shape=jax.ShapeDtypeStruct((groups, rows, width), jnp.float32),
        compiler_params=pltpu.CompilerParams(vmem_limit_bytes=48 * 1024 * 1024),
        cost_estimate=pl.CostEstimate(
            flops=2 * rows * depth * width * groups,
            bytes_accessed=2 * (rows * depth + groups * depth * width) + 4 * groups * rows * width,
            transcendentals=0,
        ),
    )(x, w, *([] if after is None else [after]))


def shards(
    streams,
    stream_tail,
    short_taps,
    decay_rates,
    residues,
    hyena_state,
    skip_weight,
    residual,
    norm_gain,
    qkv_weight,
    start_offset,
    cache_keys,
    cache_values,
):
    row_count = streams.shape[0]
    tap_count = short_taps.shape[0]
    devices = lax.axis_size("context")
    device_index = lax.axis_index("context")
    head_width = qkv_weight.shape[2]
    heads_here = head_width // HEAD
    half_rows = row_count // 2

    def by_head(block):
        per_head = block.reshape(row_count, heads_here, HEAD).transpose(1, 0, 2)
        return jnp.repeat(per_head, devices // heads_here, axis=0)


    received = shifted(streams[row_count - (tap_count - 1) :], "context", 1)
    channels = streams.shape[2]
    mode_count = decay_rates.shape[0]
    ways = lax.axis_size("tensor")
    index = device_index.astype(jnp.int32).reshape(1)
    block = 256
    product, filtered1, local_out, finals_out = channel_blocks(
        front_kernel,
        index,
        [
            streams.transpose(1, 0, 2),
            received.transpose(1, 0, 2),
            stream_tail.transpose(1, 0, 2),
            short_taps,
            decay_rates,
            residues,
        ],
        [
            jax.ShapeDtypeStruct((row_count, channels), jnp.bfloat16),
            jax.ShapeDtypeStruct((row_count, channels), jnp.float32),
            jax.ShapeDtypeStruct((row_count, channels), jnp.float32),
            jax.ShapeDtypeStruct((devices, mode_count, channels), jnp.bfloat16),
        ],
        block,
        [pltpu.VMEM((mode_count, block), jnp.float32)],
    )
    finals = lax.all_to_all(finals_out, "context", 0, 0, tiled=True)
    (hidden_out,) = channel_blocks(
        back_kernel,
        index,
        [
            local_out,
            decay_rates,
            residues,
            finals,
            hyena_state,
            filtered1,
            product,
            residual,
            skip_weight[None, :],
        ],
        [jax.ShapeDtypeStruct((ways, row_count, channels), jnp.bfloat16)],
        block,
    )
    gathered = lax.all_to_all(hidden_out, "tensor", 0, 0, tiled=True)
    gathered = gathered.transpose(1, 0, 2).reshape(row_count, ways * channels)
    hidden_float = gathered.astype(jnp.float32)
    mean_square = jnp.mean(hidden_float * hidden_float, axis=1, keepdims=True)
    normed = (hidden_float * lax.rsqrt(mean_square + NORM_EPSILON) * norm_gain[None, :]).astype(
        jnp.bfloat16
    )
    weights3 = qkv_weight.transpose(1, 0, 2)
    query_index = device_index * row_count + jnp.arange(row_count, dtype=jnp.int32)
    positions = (start_offset[0] + query_index).astype(jnp.float32)
    query_proj = project(normed, weights3, 0, 1)[0].reshape(row_count, heads_here, HEAD)
    queries = rotate(query_proj, positions).astype(jnp.bfloat16)
    query_parts = (
        queries.reshape(2, half_rows, heads_here, HEAD)
        .transpose(2, 0, 1, 3)
        .reshape(devices, half_rows, HEAD)
    )
    first_sent = lax.all_to_all(
        jnp.concatenate([by_head(cache_keys), by_head(cache_values), query_parts], axis=1),
        "context", 0, 0, tiled=True,
    )
    kv_proj = project(normed, weights3, 1, 2, after=query_parts).reshape(
        2, row_count, heads_here, HEAD
    )
    new_keys = rotate(kv_proj[0], positions).astype(jnp.bfloat16)
    new_values = kv_proj[1].astype(jnp.bfloat16)
    new_keys, new_values, first_sent = lax.optimization_barrier(
        (new_keys, new_values, first_sent)
    )
    cache_k = first_sent[:, :row_count]
    cache_v = first_sent[:, row_count : 2 * row_count]
    my_queries = first_sent[:, 2 * row_count :]
    new_kv = lax.all_to_all(
        jnp.concatenate([by_head(new_keys), by_head(new_values)], axis=1),
        "context", 0, 0, tiled=True,
    )
    q_flat = my_queries.reshape(-1, HEAD)
    pieces = attend_cache(q_flat, cache_k.reshape(-1, HEAD), cache_v.reshape(-1, HEAD))
    src = jnp.arange(devices, dtype=jnp.int32)[:, None]
    row = jnp.arange(half_rows, dtype=jnp.int32)[None, :]
    query_pos = (src * row_count + (device_index % 2) * half_rows + row).reshape(-1)
    mine = attend_new(
        q_flat,
        new_kv[:, :row_count].reshape(-1, HEAD),
        new_kv[:, row_count:].reshape(-1, HEAD),
        query_pos,
        pieces,
    ).reshape(devices, half_rows, HEAD)
    back = lax.all_to_all(mine, "context", 0, 0, tiled=True)
    attended = (
        back.reshape(heads_here, 2, half_rows, HEAD)
        .transpose(1, 2, 0, 3)
        .reshape(row_count, head_width)
    )
    return attended


def solution(mesh):
    placed = (
        P(("dp", "context"), None, "tensor"),
        P("dp", None, "tensor"),
        P(None, None, "tensor"),
        P(None, "tensor"),
        P(None, "tensor"),
        P("dp", "tensor"),
        P("tensor"),
        P(("dp", "context"), "tensor"),
        P(),
        P(None, None, "tensor"),
        P("dp"),
        P(("dp", "context"), "tensor"),
        P(("dp", "context"), "tensor"),
    )
    return jax.shard_map(
        shards,
        mesh=mesh,
        in_specs=placed,
        out_specs=P(("dp", "context"), "tensor"),
        check_vma=False,
    )
```

```python
import functools
import math

import jax
import jax.numpy as jnp
from jax import lax
from jax.experimental import pallas as pl
from jax.experimental.pallas import tpu as pltpu
from jax.sharding import PartitionSpec as P

HEAD = 128


ROTARY_BASE = 1000000.0
NORM_EPSILON = 1e-06


def shifted(x, axis, by):
    devices = lax.axis_size(axis)
    pairs = [(i, i + by) for i in range(devices) if 0 <= i + by < devices]
    return lax.ppermute(x, axis, pairs)


def rotate(features, positions):
    half_width = features.shape[-1] // 2
    exponents = jnp.arange(half_width, dtype=jnp.float32) * (2.0 / features.shape[-1])
    frequency = jnp.exp(-math.log(ROTARY_BASE) * exponents)
    angles = positions[:, None] * frequency[None, :]
    cosine = jnp.cos(angles)[:, None, :]
    sine_values = jnp.sin(angles)[:, None, :]
    front = features[..., :half_width]
    back = features[..., half_width:]
    return jnp.concatenate(
        [front * cosine - back * sine_values, back * cosine + front * sine_values], axis=-1
    )


def front_kernel(
    idx_ref, s_ref, recv_ref, tail_ref, tap_ref, rate_ref, res_ref,
    prod_ref, f1_ref, out_ref, fin_ref, fin_scr,
):
    length = s_ref.shape[1]
    mode_count = rate_ref.shape[0]
    row = lax.broadcasted_iota(jnp.int32, (length, s_ref.shape[2]), 0)
    filtered = []
    for i in range(3):
        now = s_ref[i].astype(jnp.float32)
        before = jnp.where(
            idx_ref[0] == 0, tail_ref[i].astype(jnp.float32), recv_ref[i].astype(jnp.float32)
        )
        back1 = jnp.where(row == 0, before[1:2], pltpu.roll(now, 1, 0))
        back2 = jnp.where(
            row == 0, before[0:1], jnp.where(row == 1, before[1:2], pltpu.roll(now, 2, 0))
        )
        taps = tap_ref[:, i, :]
        filtered.append(taps[0:1] * now + taps[1:2] * back1 + taps[2:3] * back2)
    product = (filtered[0] * filtered[2]).astype(jnp.bfloat16)
    prod_ref[...] = product
    f1_ref[...] = filtered[1]
    x = product.astype(jnp.float32)
    rows = lax.broadcasted_iota(jnp.int32, (length, length), 0)
    cols = lax.broadcasted_iota(jnp.int32, (length, length), 1)
    lower = (rows >= cols).astype(jnp.bfloat16)
    offsets = lax.broadcasted_iota(jnp.int32, (length, 1), 0).astype(jnp.float32)
    gains = jnp.sqrt(1.0 - jnp.exp(-2.0 * rate_ref[...]))
    rgains = res_ref[...] * gains
    total = jnp.zeros(x.shape, jnp.float32)
    for m in range(mode_count):
        rate = rate_ref[m : m + 1, :]
        terms = jnp.exp(rate * offsets) * x
        high = terms.astype(jnp.bfloat16)
        low = (terms - high.astype(jnp.float32)).astype(jnp.bfloat16)
        prefix = jnp.dot(lower, high, preferred_element_type=jnp.float32) + jnp.dot(
            lower, low, preferred_element_type=jnp.float32
        )
        total = total + rgains[m : m + 1, :] * jnp.exp(-rate * offsets) * prefix
        fin_scr[m : m + 1, :] = (
            gains[m : m + 1, :] * jnp.exp(-rate * (length - 1.0)) * prefix[length - 1 : length, :]
        )
    out_ref[...] = total
    fin_ref[...] = jnp.broadcast_to(fin_scr[...][None], fin_ref.shape).astype(fin_ref.dtype)


def back_kernel(
    idx_ref, local_ref, rate_ref, res_ref, fin_ref, hs_ref,
    f1_ref, prod_ref, resid_ref, skip_ref, out_ref,
):
    length = local_ref.shape[0]
    mode_count = rate_ref.shape[0]
    rates = rate_ref[...]
    me = idx_ref[0]
    incoming = jnp.exp(-rates * (me * length).astype(jnp.float32)) * hs_ref[...]
    for src in range(fin_ref.shape[0]):
        steps_back = (jnp.maximum(me - 1 - src, 0) * length).astype(jnp.float32)
        weight_src = jnp.where(src < me, jnp.exp(-rates * steps_back), 0.0)
        incoming = incoming + weight_src * fin_ref[src].astype(jnp.float32)
    weight = res_ref[...] * incoming
    steps = lax.broadcasted_iota(jnp.int32, (length, 1), 0).astype(jnp.float32) + 1.0
    total = local_ref[...]
    for m in range(mode_count):
        total = total + weight[m : m + 1, :] * jnp.exp(-rates[m : m + 1, :] * steps)
    long_out = total.astype(jnp.bfloat16).astype(jnp.float32)
    hidden = (
        resid_ref[...].astype(jnp.float32)
        + f1_ref[...] * (long_out + skip_ref[...] * prod_ref[...].astype(jnp.float32))
    ).astype(out_ref.dtype)
    out_ref[...] = jnp.broadcast_to(hidden[None], out_ref.shape)


def channel_blocks(kernel, index, inputs, outputs, block, scratch=()):
    def spec(shape):
        lead = tuple(0 for _ in shape[:-1])
        return pl.BlockSpec(tuple(shape[:-1]) + (block,), lambda j, idx: lead + (j,))

    grid_spec = pltpu.PrefetchScalarGridSpec(
        num_scalar_prefetch=1,
        grid=(outputs[0].shape[-1] // block,),
        in_specs=[spec(a.shape) for a in inputs],
        out_specs=[spec(o.shape) for o in outputs],
        scratch_shapes=list(scratch),
    )
    return pl.pallas_call(kernel, grid_spec=grid_spec, out_shape=outputs)(index, *inputs)


def cache_attention_kernel(scale, q_ref, k_ref, v_ref, max_ref, sum_ref, num_ref):
    scores = (
        lax.dot_general(
            q_ref[...], k_ref[...], (((1,), (1,)), ((), ())), preferred_element_type=jnp.float32
        )
        * scale
    )
    row_max = jnp.max(scores, axis=1, keepdims=True)
    weights = jnp.exp(scores - row_max).astype(jnp.bfloat16)
    ones = jnp.ones((weights.shape[1], 128), jnp.bfloat16)
    max_ref[...] = jnp.broadcast_to(row_max, max_ref.shape)
    sum_ref[...] = jnp.dot(weights, ones, preferred_element_type=jnp.float32)
    num_ref[...] = jnp.dot(weights, v_ref[...], preferred_element_type=jnp.float32)


def new_attention_kernel(scale, q_ref, k_ref, v_ref, qpos_ref, max_ref, sum_ref, num_ref, out_ref):
    scores = (
        lax.dot_general(
            q_ref[...], k_ref[...], (((1,), (1,)), ((), ())), preferred_element_type=jnp.float32
        )
        * scale
    )
    key_pos = lax.broadcasted_iota(jnp.int32, (1, scores.shape[1]), 1)
    scores = jnp.where(key_pos <= qpos_ref[...], scores, -jnp.inf)
    old_max = max_ref[:, :1]
    row_max = jnp.maximum(old_max, jnp.max(scores, axis=1, keepdims=True))
    rescale = jnp.exp(old_max - row_max)
    weights = jnp.exp(scores - row_max).astype(jnp.bfloat16)
    ones = jnp.ones((weights.shape[1], 128), jnp.bfloat16)
    weight_sum = sum_ref[:, :1] * rescale + jnp.dot(
        weights, ones, preferred_element_type=jnp.float32
    )[:, :1]
    numerator = num_ref[...] * rescale + jnp.dot(
        weights, v_ref[...], preferred_element_type=jnp.float32
    )
    out_ref[...] = (numerator / weight_sum).astype(out_ref.dtype)


def attend_cache(queries, keys, values, block=512):
    rows, width = queries.shape
    key_rows = keys.shape[0]
    piece = jax.ShapeDtypeStruct((rows, width), jnp.float32)
    row_spec = pl.BlockSpec((block, width), lambda i: (i, 0))
    return pl.pallas_call(
        functools.partial(cache_attention_kernel, 1.0 / math.sqrt(width)),
        grid=(rows // block,),
        in_specs=[
            row_spec,
            pl.BlockSpec((key_rows, width), lambda i: (0, 0)),
            pl.BlockSpec((key_rows, width), lambda i: (0, 0)),
        ],
        out_specs=[row_spec, row_spec, row_spec],
        out_shape=[piece, piece, piece],
        compiler_params=pltpu.CompilerParams(vmem_limit_bytes=48 * 1024 * 1024),
        cost_estimate=pl.CostEstimate(
            flops=6 * rows * key_rows * width,
            bytes_accessed=2 * rows * width + 4 * key_rows * width + 12 * rows * width,
            transcendentals=rows * key_rows,
        ),
    )(queries, keys, values)


def attend_new(queries, keys, values, query_pos, pieces, block=512):
    rows, width = queries.shape
    key_rows = keys.shape[0]
    row_spec = pl.BlockSpec((block, width), lambda i: (i, 0))
    return pl.pallas_call(
        functools.partial(new_attention_kernel, 1.0 / math.sqrt(width)),
        grid=(rows // block,),
        in_specs=[
            row_spec,
            pl.BlockSpec((key_rows, width), lambda i: (0, 0)),
            pl.BlockSpec((key_rows, width), lambda i: (0, 0)),
            pl.BlockSpec((block, 1), lambda i: (i, 0)),
            row_spec,
            row_spec,
            row_spec,
        ],
        out_specs=row_spec,
        out_shape=jax.ShapeDtypeStruct((rows, width), jnp.bfloat16),
        compiler_params=pltpu.CompilerParams(vmem_limit_bytes=48 * 1024 * 1024),
    )(queries, keys, values, query_pos.reshape(rows, 1), *pieces)


def project_kernel(x_ref, w_ref, out_ref):
    out_ref[...] = jnp.dot(x_ref[...], w_ref[...], preferred_element_type=jnp.float32)


def project(x, w, block=1024):
    rows, depth = x.shape
    groups, _, width = w.shape
    return pl.pallas_call(
        project_kernel,
        grid=(groups, width // block),
        in_specs=[
            pl.BlockSpec((rows, depth), lambda g, j: (0, 0)),
            pl.BlockSpec((None, depth, block), lambda g, j: (g, 0, j)),
        ],
        out_specs=pl.BlockSpec((None, rows, block), lambda g, j: (g, 0, j)),
        out_shape=jax.ShapeDtypeStruct((groups, rows, width), jnp.float32),
        compiler_params=pltpu.CompilerParams(vmem_limit_bytes=48 * 1024 * 1024),
        cost_estimate=pl.CostEstimate(
            flops=2 * rows * depth * width * groups,
            bytes_accessed=2 * (rows * depth + groups * depth * width) + 4 * groups * rows * width,
            transcendentals=0,
        ),
    )(x, w)


def shards(
    streams,
    stream_tail,
    short_taps,
    decay_rates,
    residues,
    hyena_state,
    skip_weight,
    residual,
    norm_gain,
    qkv_weight,
    start_offset,
    cache_keys,
    cache_values,
):
    row_count = streams.shape[0]
    tap_count = short_taps.shape[0]
    devices = lax.axis_size("context")
    device_index = lax.axis_index("context")
    head_width = qkv_weight.shape[2]
    heads_here = head_width // HEAD
    half_rows = row_count // 2

    def by_head(block):
        per_head = block.reshape(row_count, heads_here, HEAD).transpose(1, 0, 2)
        return jnp.repeat(per_head, devices // heads_here, axis=0)

    cache_kv = lax.all_to_all(
        jnp.concatenate([by_head(cache_keys), by_head(cache_values)], axis=1),
        "context", 0, 0, tiled=True,
    )
    cache_k, cache_v = cache_kv[:, :row_count], cache_kv[:, row_count:]

    received = shifted(streams[row_count - (tap_count - 1) :], "context", 1)
    channels = streams.shape[2]
    mode_count = decay_rates.shape[0]
    ways = lax.axis_size("tensor")
    index = device_index.astype(jnp.int32).reshape(1)
    block = 256
    product, filtered1, local_out, finals_out = channel_blocks(
        front_kernel,
        index,
        [
            streams.transpose(1, 0, 2),
            received.transpose(1, 0, 2),
            stream_tail.transpose(1, 0, 2),
            short_taps,
            decay_rates,
            residues,
        ],
        [
            jax.ShapeDtypeStruct((row_count, channels), jnp.bfloat16),
            jax.ShapeDtypeStruct((row_count, channels), jnp.float32),
            jax.ShapeDtypeStruct((row_count, channels), jnp.float32),
            jax.ShapeDtypeStruct((devices, mode_count, channels), jnp.bfloat16),
        ],
        block,
        [pltpu.VMEM((mode_count, block), jnp.float32)],
    )
    finals = lax.all_to_all(finals_out, "context", 0, 0, tiled=True)
    (hidden_out,) = channel_blocks(
        back_kernel,
        index,
        [
            local_out,
            decay_rates,
            residues,
            finals,
            hyena_state,
            filtered1,
            product,
            residual,
            skip_weight[None, :],
        ],
        [jax.ShapeDtypeStruct((ways, row_count, channels), jnp.bfloat16)],
        block,
    )
    gathered = lax.all_to_all(hidden_out, "tensor", 0, 0, tiled=True)
    gathered = gathered.transpose(1, 0, 2).reshape(row_count, ways * channels)
    hidden_float = gathered.astype(jnp.float32)
    mean_square = jnp.mean(hidden_float * hidden_float, axis=1, keepdims=True)
    normed = (hidden_float * lax.rsqrt(mean_square + NORM_EPSILON) * norm_gain[None, :]).astype(
        jnp.bfloat16
    )
    projected = (
        project(normed, qkv_weight.transpose(1, 0, 2))
        .transpose(1, 0, 2)
        .reshape(row_count, 3, heads_here, HEAD)
    )
    query_index = device_index * row_count + jnp.arange(row_count, dtype=jnp.int32)
    positions = (start_offset[0] + query_index).astype(jnp.float32)
    queries = rotate(projected[:, 0], positions).astype(jnp.bfloat16)
    new_keys = rotate(projected[:, 1], positions).astype(jnp.bfloat16)
    new_values = projected[:, 2].astype(jnp.bfloat16)

    query_parts = (
        queries.reshape(2, half_rows, heads_here, HEAD)
        .transpose(2, 0, 1, 3)
        .reshape(devices, half_rows, HEAD)
    )
    sent = lax.all_to_all(
        jnp.concatenate([query_parts, by_head(new_keys), by_head(new_values)], axis=1),
        "context", 0, 0, tiled=True,
    )
    my_queries = sent[:, :half_rows]
    new_k = sent[:, half_rows : half_rows + row_count]
    new_v = sent[:, half_rows + row_count :]

    q_flat = my_queries.reshape(-1, HEAD)
    src = jnp.arange(devices, dtype=jnp.int32)[:, None]
    row = jnp.arange(half_rows, dtype=jnp.int32)[None, :]
    query_pos = (src * row_count + (device_index % 2) * half_rows + row).reshape(-1)
    pieces = attend_cache(q_flat, cache_k.reshape(-1, HEAD), cache_v.reshape(-1, HEAD))
    mine = attend_new(
        q_flat, new_k.reshape(-1, HEAD), new_v.reshape(-1, HEAD), query_pos, pieces
    ).reshape(devices, half_rows, HEAD)
    back = lax.all_to_all(mine, "context", 0, 0, tiled=True)
    attended = (
        back.reshape(heads_here, 2, half_rows, HEAD)
        .transpose(1, 2, 0, 3)
        .reshape(row_count, head_width)
    )
    return attended


def solution(mesh):
    placed = (
        P(("dp", "context"), None, "tensor"),
        P("dp", None, "tensor"),
        P(None, None, "tensor"),
        P(None, "tensor"),
        P(None, "tensor"),
        P("dp", "tensor"),
        P("tensor"),
        P(("dp", "context"), "tensor"),
        P(),
        P(None, None, "tensor"),
        P("dp"),
        P(("dp", "context"), "tensor"),
        P(("dp", "context"), "tensor"),
    )
    return jax.shard_map(
        shards,
        mesh=mesh,
        in_specs=placed,
        out_specs=P(("dp", "context"), "tensor"),
        check_vma=False,
    )
```

```python
import functools
import math

import jax
import jax.numpy as jnp
from jax import lax
from jax.experimental import pallas as pl
from jax.experimental.pallas import tpu as pltpu
from jax.sharding import PartitionSpec as P

HEAD = 128


ROTARY_BASE = 1000000.0
NORM_EPSILON = 1e-06


def shifted(x, axis, by):
    devices = lax.axis_size(axis)
    pairs = [(i, i + by) for i in range(devices) if 0 <= i + by < devices]
    return lax.ppermute(x, axis, pairs)


def rotate(features, positions):
    half_width = features.shape[-1] // 2
    exponents = jnp.arange(half_width, dtype=jnp.float32) * (2.0 / features.shape[-1])
    frequency = jnp.exp(-math.log(ROTARY_BASE) * exponents)
    angles = positions[:, None] * frequency[None, :]
    cosine = jnp.cos(angles)[:, None, :]
    sine_values = jnp.sin(angles)[:, None, :]
    front = features[..., :half_width]
    back = features[..., half_width:]
    return jnp.concatenate(
        [front * cosine - back * sine_values, back * cosine + front * sine_values], axis=-1
    )


def front_kernel(
    idx_ref, s_ref, recv_ref, tail_ref, tap_ref, rate_ref, res_ref,
    prod_ref, f1_ref, out_ref, fin_ref, fin_scr,
):
    length = s_ref.shape[1]
    mode_count = rate_ref.shape[0]
    row = lax.broadcasted_iota(jnp.int32, (length, s_ref.shape[2]), 0)
    filtered = []
    for i in range(3):
        now = s_ref[i].astype(jnp.float32)
        before = jnp.where(
            idx_ref[0] == 0, tail_ref[i].astype(jnp.float32), recv_ref[i].astype(jnp.float32)
        )
        back1 = jnp.where(row == 0, before[1:2], pltpu.roll(now, 1, 0))
        back2 = jnp.where(
            row == 0, before[0:1], jnp.where(row == 1, before[1:2], pltpu.roll(now, 2, 0))
        )
        taps = tap_ref[:, i, :]
        filtered.append(taps[0:1] * now + taps[1:2] * back1 + taps[2:3] * back2)
    product = (filtered[0] * filtered[2]).astype(jnp.bfloat16)
    prod_ref[...] = product
    f1_ref[...] = filtered[1]
    x = product.astype(jnp.float32)
    rows = lax.broadcasted_iota(jnp.int32, (length, length), 0)
    cols = lax.broadcasted_iota(jnp.int32, (length, length), 1)
    lower = (rows >= cols).astype(jnp.bfloat16)
    offsets = lax.broadcasted_iota(jnp.int32, (length, 1), 0).astype(jnp.float32)
    gains = jnp.sqrt(1.0 - jnp.exp(-2.0 * rate_ref[...]))
    rgains = res_ref[...] * gains
    total = jnp.zeros(x.shape, jnp.float32)
    for m in range(mode_count):
        rate = rate_ref[m : m + 1, :]
        terms = jnp.exp(rate * offsets) * x
        high = terms.astype(jnp.bfloat16)
        low = (terms - high.astype(jnp.float32)).astype(jnp.bfloat16)
        prefix = jnp.dot(lower, high, preferred_element_type=jnp.float32) + jnp.dot(
            lower, low, preferred_element_type=jnp.float32
        )
        total = total + rgains[m : m + 1, :] * jnp.exp(-rate * offsets) * prefix
        fin_scr[m : m + 1, :] = (
            gains[m : m + 1, :] * jnp.exp(-rate * (length - 1.0)) * prefix[length - 1 : length, :]
        )
    out_ref[...] = total
    fin_ref[...] = jnp.broadcast_to(fin_scr[...][None], fin_ref.shape).astype(fin_ref.dtype)


def back_kernel(
    idx_ref, local_ref, rate_ref, res_ref, fin_ref, hs_ref,
    f1_ref, prod_ref, resid_ref, skip_ref, out_ref,
):
    length = local_ref.shape[0]
    mode_count = rate_ref.shape[0]
    rates = rate_ref[...]
    me = idx_ref[0]
    incoming = jnp.exp(-rates * (me * length).astype(jnp.float32)) * hs_ref[...]
    for src in range(fin_ref.shape[0]):
        steps_back = (jnp.maximum(me - 1 - src, 0) * length).astype(jnp.float32)
        weight_src = jnp.where(src < me, jnp.exp(-rates * steps_back), 0.0)
        incoming = incoming + weight_src * fin_ref[src].astype(jnp.float32)
    weight = res_ref[...] * incoming
    steps = lax.broadcasted_iota(jnp.int32, (length, 1), 0).astype(jnp.float32) + 1.0
    total = local_ref[...]
    for m in range(mode_count):
        total = total + weight[m : m + 1, :] * jnp.exp(-rates[m : m + 1, :] * steps)
    long_out = total.astype(jnp.bfloat16).astype(jnp.float32)
    hidden = (
        resid_ref[...].astype(jnp.float32)
        + f1_ref[...] * (long_out + skip_ref[...] * prod_ref[...].astype(jnp.float32))
    ).astype(out_ref.dtype)
    out_ref[...] = jnp.broadcast_to(hidden[None], out_ref.shape)


def channel_blocks(kernel, index, inputs, outputs, block, scratch=()):
    def spec(shape):
        lead = tuple(0 for _ in shape[:-1])
        return pl.BlockSpec(tuple(shape[:-1]) + (block,), lambda j, idx: lead + (j,))

    grid_spec = pltpu.PrefetchScalarGridSpec(
        num_scalar_prefetch=1,
        grid=(outputs[0].shape[-1] // block,),
        in_specs=[spec(a.shape) for a in inputs],
        out_specs=[spec(o.shape) for o in outputs],
        scratch_shapes=list(scratch),
    )
    return pl.pallas_call(kernel, grid_spec=grid_spec, out_shape=outputs)(index, *inputs)


def cache_attention_kernel(scale, q_ref, k_ref, v_ref, max_ref, sum_ref, num_ref):
    scores = (
        lax.dot_general(
            q_ref[...], k_ref[...], (((1,), (1,)), ((), ())), preferred_element_type=jnp.float32
        )
        * scale
    )
    row_max = jnp.max(scores, axis=1, keepdims=True)
    weights = jnp.exp(scores - row_max).astype(jnp.bfloat16)
    ones = jnp.ones((weights.shape[1], 128), jnp.bfloat16)
    max_ref[...] = jnp.broadcast_to(row_max, max_ref.shape)
    sum_ref[...] = jnp.dot(weights, ones, preferred_element_type=jnp.float32)
    num_ref[...] = jnp.dot(weights, v_ref[...], preferred_element_type=jnp.float32)


def new_attention_kernel(
    scale, reach, q_ref, k_ref, v_ref, qpos_ref, max_ref, sum_ref, num_ref, out_ref
):
    def block_with(keys):
        scores = (
            lax.dot_general(
                q_ref[...], k_ref[:keys], (((1,), (1,)), ((), ())),
                preferred_element_type=jnp.float32,
            )
            * scale
        )
        key_pos = lax.broadcasted_iota(jnp.int32, (1, keys), 1)
        scores = jnp.where(key_pos <= qpos_ref[...], scores, -jnp.inf)
        old_max = max_ref[:, :1]
        row_max = jnp.maximum(old_max, jnp.max(scores, axis=1, keepdims=True))
        rescale = jnp.exp(old_max - row_max)
        weights = jnp.exp(scores - row_max).astype(jnp.bfloat16)
        ones = jnp.ones((keys, 128), jnp.bfloat16)
        weight_sum = sum_ref[:, :1] * rescale + jnp.dot(
            weights, ones, preferred_element_type=jnp.float32
        )[:, :1]
        numerator = num_ref[...] * rescale + jnp.dot(
            weights, v_ref[:keys], preferred_element_type=jnp.float32
        )
        out_ref[...] = (numerator / weight_sum).astype(out_ref.dtype)

    key_rows = k_ref.shape[0]
    for i in range(pl.cdiv(key_rows, reach)):
        keys = min(key_rows, reach * (i + 1))
        last = keys == key_rows

        @pl.when((pl.program_id(0) >= i) if last else (pl.program_id(0) == i))
        def _():
            block_with(keys)


def attend_cache(queries, keys, values, block=512):
    rows, width = queries.shape
    key_rows = keys.shape[0]
    piece = jax.ShapeDtypeStruct((rows, width), jnp.float32)
    row_spec = pl.BlockSpec((block, width), lambda i: (i, 0))
    return pl.pallas_call(
        functools.partial(cache_attention_kernel, 1.0 / math.sqrt(width)),
        grid=(rows // block,),
        in_specs=[
            row_spec,
            pl.BlockSpec((key_rows, width), lambda i: (0, 0)),
            pl.BlockSpec((key_rows, width), lambda i: (0, 0)),
        ],
        out_specs=[row_spec, row_spec, row_spec],
        out_shape=[piece, piece, piece],
        compiler_params=pltpu.CompilerParams(vmem_limit_bytes=48 * 1024 * 1024),
        cost_estimate=pl.CostEstimate(
            flops=6 * rows * key_rows * width,
            bytes_accessed=2 * rows * width + 4 * key_rows * width + 12 * rows * width,
            transcendentals=rows * key_rows,
        ),
    )(queries, keys, values)


def attend_new(queries, keys, values, query_pos, pieces, spread, block=512):
    rows, width = queries.shape
    key_rows = keys.shape[0]
    row_spec = pl.BlockSpec((block, width), lambda i: (i, 0))
    return pl.pallas_call(
        functools.partial(new_attention_kernel, 1.0 / math.sqrt(width), block * spread),
        grid=(rows // block,),
        in_specs=[
            row_spec,
            pl.BlockSpec((key_rows, width), lambda i: (0, 0)),
            pl.BlockSpec((key_rows, width), lambda i: (0, 0)),
            pl.BlockSpec((block, 1), lambda i: (i, 0)),
            row_spec,
            row_spec,
            row_spec,
        ],
        out_specs=row_spec,
        out_shape=jax.ShapeDtypeStruct((rows, width), jnp.bfloat16),
        compiler_params=pltpu.CompilerParams(vmem_limit_bytes=48 * 1024 * 1024),
    )(queries, keys, values, query_pos.reshape(rows, 1), *pieces)


def project_kernel(x_ref, w_ref, out_ref):
    out_ref[...] = jnp.dot(x_ref[...], w_ref[...], preferred_element_type=jnp.float32)


def project(x, w, block=1024):
    rows, depth = x.shape
    groups, _, width = w.shape
    return pl.pallas_call(
        project_kernel,
        grid=(groups, width // block),
        in_specs=[
            pl.BlockSpec((rows, depth), lambda g, j: (0, 0)),
            pl.BlockSpec((None, depth, block), lambda g, j: (g, 0, j)),
        ],
        out_specs=pl.BlockSpec((None, rows, block), lambda g, j: (g, 0, j)),
        out_shape=jax.ShapeDtypeStruct((groups, rows, width), jnp.float32),
        compiler_params=pltpu.CompilerParams(vmem_limit_bytes=48 * 1024 * 1024),
        cost_estimate=pl.CostEstimate(
            flops=2 * rows * depth * width * groups,
            bytes_accessed=2 * (rows * depth + groups * depth * width) + 4 * groups * rows * width,
            transcendentals=0,
        ),
    )(x, w)


def shards(
    streams,
    stream_tail,
    short_taps,
    decay_rates,
    residues,
    hyena_state,
    skip_weight,
    residual,
    norm_gain,
    qkv_weight,
    start_offset,
    cache_keys,
    cache_values,
):
    row_count = streams.shape[0]
    tap_count = short_taps.shape[0]
    devices = lax.axis_size("context")
    device_index = lax.axis_index("context")
    head_width = qkv_weight.shape[2]
    heads_here = head_width // HEAD
    half_rows = row_count // 2

    def by_head(block):
        per_head = block.reshape(row_count, heads_here, HEAD).transpose(1, 0, 2)
        return jnp.repeat(per_head, devices // heads_here, axis=0)

    cache_kv = lax.all_to_all(
        jnp.concatenate([by_head(cache_keys), by_head(cache_values)], axis=1),
        "context", 0, 0, tiled=True,
    )
    cache_k, cache_v = cache_kv[:, :row_count], cache_kv[:, row_count:]

    received = shifted(streams[row_count - (tap_count - 1) :], "context", 1)
    channels = streams.shape[2]
    mode_count = decay_rates.shape[0]
    ways = lax.axis_size("tensor")
    index = device_index.astype(jnp.int32).reshape(1)
    block = 256
    product, filtered1, local_out, finals_out = channel_blocks(
        front_kernel,
        index,
        [
            streams.transpose(1, 0, 2),
            received.transpose(1, 0, 2),
            stream_tail.transpose(1, 0, 2),
            short_taps,
            decay_rates,
            residues,
        ],
        [
            jax.ShapeDtypeStruct((row_count, channels), jnp.bfloat16),
            jax.ShapeDtypeStruct((row_count, channels), jnp.float32),
            jax.ShapeDtypeStruct((row_count, channels), jnp.float32),
            jax.ShapeDtypeStruct((devices, mode_count, channels), jnp.bfloat16),
        ],
        block,
        [pltpu.VMEM((mode_count, block), jnp.float32)],
    )
    finals = lax.all_to_all(finals_out, "context", 0, 0, tiled=True)
    (hidden_out,) = channel_blocks(
        back_kernel,
        index,
        [
            local_out,
            decay_rates,
            residues,
            finals,
            hyena_state,
            filtered1,
            product,
            residual,
            skip_weight[None, :],
        ],
        [jax.ShapeDtypeStruct((ways, row_count, channels), jnp.bfloat16)],
        block,
    )
    gathered = lax.all_to_all(hidden_out, "tensor", 0, 0, tiled=True)
    gathered = gathered.transpose(1, 0, 2).reshape(row_count, ways * channels)
    hidden_float = gathered.astype(jnp.float32)
    mean_square = jnp.mean(hidden_float * hidden_float, axis=1, keepdims=True)
    normed = (hidden_float * lax.rsqrt(mean_square + NORM_EPSILON) * norm_gain[None, :]).astype(
        jnp.bfloat16
    )
    projected = (
        project(normed, qkv_weight.transpose(1, 0, 2))
        .transpose(1, 0, 2)
        .reshape(row_count, 3, heads_here, HEAD)
    )
    query_index = device_index * row_count + jnp.arange(row_count, dtype=jnp.int32)
    positions = (start_offset[0] + query_index).astype(jnp.float32)
    queries = rotate(projected[:, 0], positions).astype(jnp.bfloat16)
    new_keys = rotate(projected[:, 1], positions).astype(jnp.bfloat16)
    new_values = projected[:, 2].astype(jnp.bfloat16)

    query_parts = (
        queries.reshape(2, half_rows, heads_here, HEAD)
        .transpose(2, 0, 1, 3)
        .reshape(devices, half_rows, HEAD)
    )
    sent = lax.all_to_all(
        jnp.concatenate([query_parts, by_head(new_keys), by_head(new_values)], axis=1),
        "context", 0, 0, tiled=True,
    )
    my_queries = sent[:, :half_rows]
    new_k = sent[:, half_rows : half_rows + row_count]
    new_v = sent[:, half_rows + row_count :]

    q_flat = my_queries.reshape(-1, HEAD)
    src = jnp.arange(devices, dtype=jnp.int32)[:, None]
    row = jnp.arange(half_rows, dtype=jnp.int32)[None, :]
    query_pos = (src * row_count + (device_index % 2) * half_rows + row).reshape(-1)
    pieces = attend_cache(q_flat, cache_k.reshape(-1, HEAD), cache_v.reshape(-1, HEAD))
    mine = attend_new(
        q_flat, new_k.reshape(-1, HEAD), new_v.reshape(-1, HEAD), query_pos, pieces,
        row_count // half_rows,
    ).reshape(devices, half_rows, HEAD)
    back = lax.all_to_all(mine, "context", 0, 0, tiled=True)
    attended = (
        back.reshape(heads_here, 2, half_rows, HEAD)
        .transpose(1, 2, 0, 3)
        .reshape(row_count, head_width)
    )
    return attended


def solution(mesh):
    placed = (
        P(("dp", "context"), None, "tensor"),
        P("dp", None, "tensor"),
        P(None, None, "tensor"),
        P(None, "tensor"),
        P(None, "tensor"),
        P("dp", "tensor"),
        P("tensor"),
        P(("dp", "context"), "tensor"),
        P(),
        P(None, None, "tensor"),
        P("dp"),
        P(("dp", "context"), "tensor"),
        P(("dp", "context"), "tensor"),
    )
    return jax.shard_map(
        shards,
        mesh=mesh,
        in_specs=placed,
        out_specs=P(("dp", "context"), "tensor"),
        check_vma=False,
    )
```

```python
import functools
import math

import jax
import jax.numpy as jnp
from jax import lax
from jax.experimental import pallas as pl
from jax.experimental.pallas import tpu as pltpu
from jax.sharding import PartitionSpec as P

HEAD = 128


ROTARY_BASE = 1000000.0
NORM_EPSILON = 1e-06


def shifted(x, axis, by):
    devices = lax.axis_size(axis)
    pairs = [(i, i + by) for i in range(devices) if 0 <= i + by < devices]
    return lax.ppermute(x, axis, pairs)


def rotate(features, positions):
    half_width = features.shape[-1] // 2
    exponents = jnp.arange(half_width, dtype=jnp.float32) * (2.0 / features.shape[-1])
    frequency = jnp.exp(-math.log(ROTARY_BASE) * exponents)
    angles = positions[:, None] * frequency[None, :]
    cosine = jnp.cos(angles)[:, None, :]
    sine_values = jnp.sin(angles)[:, None, :]
    front = features[..., :half_width]
    back = features[..., half_width:]
    return jnp.concatenate(
        [front * cosine - back * sine_values, back * cosine + front * sine_values], axis=-1
    )


def front_kernel(
    idx_ref, s_ref, recv_ref, tail_ref, tap_ref, rate_ref, res_ref,
    prod_ref, f1_ref, out_ref, fin_ref, fin_scr,
):
    length = s_ref.shape[1]
    mode_count = rate_ref.shape[0]
    row = lax.broadcasted_iota(jnp.int32, (length, s_ref.shape[2]), 0)
    filtered = []
    for i in range(3):
        now = s_ref[i].astype(jnp.float32)
        before = jnp.where(
            idx_ref[0] == 0, tail_ref[i].astype(jnp.float32), recv_ref[i].astype(jnp.float32)
        )
        back1 = jnp.where(row == 0, before[1:2], pltpu.roll(now, 1, 0))
        back2 = jnp.where(
            row == 0, before[0:1], jnp.where(row == 1, before[1:2], pltpu.roll(now, 2, 0))
        )
        taps = tap_ref[:, i, :]
        filtered.append(taps[0:1] * now + taps[1:2] * back1 + taps[2:3] * back2)
    product = (filtered[0] * filtered[2]).astype(jnp.bfloat16)
    prod_ref[...] = product
    f1_ref[...] = filtered[1]
    x = product.astype(jnp.float32)
    rows = lax.broadcasted_iota(jnp.int32, (length, length), 0)
    cols = lax.broadcasted_iota(jnp.int32, (length, length), 1)
    lower = (rows >= cols).astype(jnp.bfloat16)
    offsets = lax.broadcasted_iota(jnp.int32, (length, 1), 0).astype(jnp.float32)
    gains = jnp.sqrt(1.0 - jnp.exp(-2.0 * rate_ref[...]))
    rgains = res_ref[...] * gains
    total = jnp.zeros(x.shape, jnp.float32)
    for m in range(mode_count):
        rate = rate_ref[m : m + 1, :]
        terms = jnp.exp(rate * offsets) * x
        high = terms.astype(jnp.bfloat16)
        low = (terms - high.astype(jnp.float32)).astype(jnp.bfloat16)
        prefix = jnp.dot(lower, high, preferred_element_type=jnp.float32) + jnp.dot(
            lower, low, preferred_element_type=jnp.float32
        )
        total = total + rgains[m : m + 1, :] * jnp.exp(-rate * offsets) * prefix
        fin_scr[m : m + 1, :] = (
            gains[m : m + 1, :] * jnp.exp(-rate * (length - 1.0)) * prefix[length - 1 : length, :]
        )
    out_ref[...] = total
    fin_ref[...] = jnp.broadcast_to(fin_scr[...][None], fin_ref.shape).astype(fin_ref.dtype)


def back_kernel(
    idx_ref, local_ref, rate_ref, res_ref, fin_ref, hs_ref,
    f1_ref, prod_ref, resid_ref, skip_ref, out_ref,
):
    length = local_ref.shape[0]
    mode_count = rate_ref.shape[0]
    rates = rate_ref[...]
    me = idx_ref[0]
    incoming = jnp.exp(-rates * (me * length).astype(jnp.float32)) * hs_ref[...]
    for src in range(fin_ref.shape[0]):
        steps_back = (jnp.maximum(me - 1 - src, 0) * length).astype(jnp.float32)
        weight_src = jnp.where(src < me, jnp.exp(-rates * steps_back), 0.0)
        incoming = incoming + weight_src * fin_ref[src].astype(jnp.float32)
    weight = res_ref[...] * incoming
    steps = lax.broadcasted_iota(jnp.int32, (length, 1), 0).astype(jnp.float32) + 1.0
    total = local_ref[...]
    for m in range(mode_count):
        total = total + weight[m : m + 1, :] * jnp.exp(-rates[m : m + 1, :] * steps)
    long_out = total.astype(jnp.bfloat16).astype(jnp.float32)
    hidden = (
        resid_ref[...].astype(jnp.float32)
        + f1_ref[...] * (long_out + skip_ref[...] * prod_ref[...].astype(jnp.float32))
    ).astype(out_ref.dtype)
    out_ref[...] = jnp.broadcast_to(hidden[None], out_ref.shape)


def channel_blocks(kernel, index, inputs, outputs, block, scratch=()):
    def spec(shape):
        lead = tuple(0 for _ in shape[:-1])
        return pl.BlockSpec(tuple(shape[:-1]) + (block,), lambda j, idx: lead + (j,))

    grid_spec = pltpu.PrefetchScalarGridSpec(
        num_scalar_prefetch=1,
        grid=(outputs[0].shape[-1] // block,),
        in_specs=[spec(a.shape) for a in inputs],
        out_specs=[spec(o.shape) for o in outputs],
        scratch_shapes=list(scratch),
    )
    return pl.pallas_call(kernel, grid_spec=grid_spec, out_shape=outputs)(index, *inputs)


def cache_attention_kernel(scale, q_ref, k_ref, v_ref, max_ref, sum_ref, num_ref):
    scores = (
        lax.dot_general(
            q_ref[...], k_ref[...], (((1,), (1,)), ((), ())), preferred_element_type=jnp.float32
        )
        * scale
    )
    row_max = jnp.max(scores, axis=1, keepdims=True)
    weights = jnp.exp(scores - row_max).astype(jnp.bfloat16)
    ones = jnp.ones((weights.shape[1], 128), jnp.bfloat16)
    max_ref[...] = jnp.broadcast_to(row_max, max_ref.shape)
    sum_ref[...] = jnp.dot(weights, ones, preferred_element_type=jnp.float32)
    num_ref[...] = jnp.dot(weights, v_ref[...], preferred_element_type=jnp.float32)


def new_attention_kernel(
    scale, reach, q_ref, k_ref, v_ref, qpos_ref, max_ref, sum_ref, num_ref, out_ref
):
    def block_with(keys):
        scores = (
            lax.dot_general(
                q_ref[...], k_ref[:keys], (((1,), (1,)), ((), ())),
                preferred_element_type=jnp.float32,
            )
            * scale
        )
        key_pos = lax.broadcasted_iota(jnp.int32, (1, keys), 1)
        scores = jnp.where(key_pos <= qpos_ref[...], scores, -jnp.inf)
        old_max = max_ref[:, :1]
        row_max = jnp.maximum(old_max, jnp.max(scores, axis=1, keepdims=True))
        rescale = jnp.exp(old_max - row_max)
        weights = jnp.exp(scores - row_max).astype(jnp.bfloat16)
        ones = jnp.ones((keys, 128), jnp.bfloat16)
        weight_sum = sum_ref[:, :1] * rescale + jnp.dot(
            weights, ones, preferred_element_type=jnp.float32
        )[:, :1]
        numerator = num_ref[...] * rescale + jnp.dot(
            weights, v_ref[:keys], preferred_element_type=jnp.float32
        )
        out_ref[...] = (numerator / weight_sum).astype(out_ref.dtype)

    key_rows = k_ref.shape[0]
    for i in range(pl.cdiv(key_rows, reach)):
        keys = min(key_rows, reach * (i + 1))
        last = keys == key_rows

        @pl.when((pl.program_id(0) >= i) if last else (pl.program_id(0) == i))
        def _():
            block_with(keys)


def attend_cache(queries, keys, values, block=512):
    rows, width = queries.shape
    key_rows = keys.shape[0]
    piece = jax.ShapeDtypeStruct((rows, width), jnp.float32)
    row_spec = pl.BlockSpec((block, width), lambda i: (i, 0))
    return pl.pallas_call(
        functools.partial(cache_attention_kernel, 1.0 / math.sqrt(width)),
        grid=(rows // block,),
        in_specs=[
            row_spec,
            pl.BlockSpec((key_rows, width), lambda i: (0, 0)),
            pl.BlockSpec((key_rows, width), lambda i: (0, 0)),
        ],
        out_specs=[row_spec, row_spec, row_spec],
        out_shape=[piece, piece, piece],
        compiler_params=pltpu.CompilerParams(vmem_limit_bytes=48 * 1024 * 1024),
        cost_estimate=pl.CostEstimate(
            flops=6 * rows * key_rows * width,
            bytes_accessed=2 * rows * width + 4 * key_rows * width + 12 * rows * width,
            transcendentals=rows * key_rows,
        ),
    )(queries, keys, values)


def attend_new(queries, keys, values, query_pos, pieces, spread, block=256):
    rows, width = queries.shape
    key_rows = keys.shape[0]
    row_spec = pl.BlockSpec((block, width), lambda i: (i, 0))
    return pl.pallas_call(
        functools.partial(new_attention_kernel, 1.0 / math.sqrt(width), block * spread),
        grid=(rows // block,),
        in_specs=[
            row_spec,
            pl.BlockSpec((key_rows, width), lambda i: (0, 0)),
            pl.BlockSpec((key_rows, width), lambda i: (0, 0)),
            pl.BlockSpec((block, 1), lambda i: (i, 0)),
            row_spec,
            row_spec,
            row_spec,
        ],
        out_specs=row_spec,
        out_shape=jax.ShapeDtypeStruct((rows, width), jnp.bfloat16),
        compiler_params=pltpu.CompilerParams(vmem_limit_bytes=48 * 1024 * 1024),
    )(queries, keys, values, query_pos.reshape(rows, 1), *pieces)


def project_kernel(x_ref, w_ref, out_ref):
    out_ref[...] = jnp.dot(x_ref[...], w_ref[...], preferred_element_type=jnp.float32)


def project(x, w, block=1024):
    rows, depth = x.shape
    groups, _, width = w.shape
    return pl.pallas_call(
        project_kernel,
        grid=(groups, width // block),
        in_specs=[
            pl.BlockSpec((rows, depth), lambda g, j: (0, 0)),
            pl.BlockSpec((None, depth, block), lambda g, j: (g, 0, j)),
        ],
        out_specs=pl.BlockSpec((None, rows, block), lambda g, j: (g, 0, j)),
        out_shape=jax.ShapeDtypeStruct((groups, rows, width), jnp.float32),
        compiler_params=pltpu.CompilerParams(vmem_limit_bytes=48 * 1024 * 1024),
        cost_estimate=pl.CostEstimate(
            flops=2 * rows * depth * width * groups,
            bytes_accessed=2 * (rows * depth + groups * depth * width) + 4 * groups * rows * width,
            transcendentals=0,
        ),
    )(x, w)


def shards(
    streams,
    stream_tail,
    short_taps,
    decay_rates,
    residues,
    hyena_state,
    skip_weight,
    residual,
    norm_gain,
    qkv_weight,
    start_offset,
    cache_keys,
    cache_values,
):
    row_count = streams.shape[0]
    tap_count = short_taps.shape[0]
    devices = lax.axis_size("context")
    device_index = lax.axis_index("context")
    head_width = qkv_weight.shape[2]
    heads_here = head_width // HEAD
    half_rows = row_count // 2

    def by_head(block):
        per_head = block.reshape(row_count, heads_here, HEAD).transpose(1, 0, 2)
        return jnp.repeat(per_head, devices // heads_here, axis=0)

    cache_kv = lax.all_to_all(
        jnp.concatenate([by_head(cache_keys), by_head(cache_values)], axis=1),
        "context", 0, 0, tiled=True,
    )
    cache_k, cache_v = cache_kv[:, :row_count], cache_kv[:, row_count:]

    received = shifted(streams[row_count - (tap_count - 1) :], "context", 1)
    channels = streams.shape[2]
    mode_count = decay_rates.shape[0]
    ways = lax.axis_size("tensor")
    index = device_index.astype(jnp.int32).reshape(1)
    block = 256
    product, filtered1, local_out, finals_out = channel_blocks(
        front_kernel,
        index,
        [
            streams.transpose(1, 0, 2),
            received.transpose(1, 0, 2),
            stream_tail.transpose(1, 0, 2),
            short_taps,
            decay_rates,
            residues,
        ],
        [
            jax.ShapeDtypeStruct((row_count, channels), jnp.bfloat16),
            jax.ShapeDtypeStruct((row_count, channels), jnp.float32),
            jax.ShapeDtypeStruct((row_count, channels), jnp.float32),
            jax.ShapeDtypeStruct((devices, mode_count, channels), jnp.bfloat16),
        ],
        block,
        [pltpu.VMEM((mode_count, block), jnp.float32)],
    )
    finals = lax.all_to_all(finals_out, "context", 0, 0, tiled=True)
    (hidden_out,) = channel_blocks(
        back_kernel,
        index,
        [
            local_out,
            decay_rates,
            residues,
            finals,
            hyena_state,
            filtered1,
            product,
            residual,
            skip_weight[None, :],
        ],
        [jax.ShapeDtypeStruct((ways, row_count, channels), jnp.bfloat16)],
        block,
    )
    gathered = lax.all_to_all(hidden_out, "tensor", 0, 0, tiled=True)
    gathered = gathered.transpose(1, 0, 2).reshape(row_count, ways * channels)
    hidden_float = gathered.astype(jnp.float32)
    mean_square = jnp.mean(hidden_float * hidden_float, axis=1, keepdims=True)
    normed = (hidden_float * lax.rsqrt(mean_square + NORM_EPSILON) * norm_gain[None, :]).astype(
        jnp.bfloat16
    )
    projected = (
        project(normed, qkv_weight.transpose(1, 0, 2))
        .transpose(1, 0, 2)
        .reshape(row_count, 3, heads_here, HEAD)
    )
    query_index = device_index * row_count + jnp.arange(row_count, dtype=jnp.int32)
    positions = (start_offset[0] + query_index).astype(jnp.float32)
    queries = rotate(projected[:, 0], positions).astype(jnp.bfloat16)
    new_keys = rotate(projected[:, 1], positions).astype(jnp.bfloat16)
    new_values = projected[:, 2].astype(jnp.bfloat16)

    query_parts = (
        queries.reshape(2, half_rows, heads_here, HEAD)
        .transpose(2, 0, 1, 3)
        .reshape(devices, half_rows, HEAD)
    )
    sent = lax.all_to_all(
        jnp.concatenate([query_parts, by_head(new_keys), by_head(new_values)], axis=1),
        "context", 0, 0, tiled=True,
    )
    my_queries = sent[:, :half_rows]
    new_k = sent[:, half_rows : half_rows + row_count]
    new_v = sent[:, half_rows + row_count :]

    q_flat = my_queries.reshape(-1, HEAD)
    src = jnp.arange(devices, dtype=jnp.int32)[:, None]
    row = jnp.arange(half_rows, dtype=jnp.int32)[None, :]
    query_pos = (src * row_count + (device_index % 2) * half_rows + row).reshape(-1)
    pieces = attend_cache(q_flat, cache_k.reshape(-1, HEAD), cache_v.reshape(-1, HEAD))
    mine = attend_new(
        q_flat, new_k.reshape(-1, HEAD), new_v.reshape(-1, HEAD), query_pos, pieces,
        row_count // half_rows,
    ).reshape(devices, half_rows, HEAD)
    back = lax.all_to_all(mine, "context", 0, 0, tiled=True)
    attended = (
        back.reshape(heads_here, 2, half_rows, HEAD)
        .transpose(1, 2, 0, 3)
        .reshape(row_count, head_width)
    )
    return attended


def solution(mesh):
    placed = (
        P(("dp", "context"), None, "tensor"),
        P("dp", None, "tensor"),
        P(None, None, "tensor"),
        P(None, "tensor"),
        P(None, "tensor"),
        P("dp", "tensor"),
        P("tensor"),
        P(("dp", "context"), "tensor"),
        P(),
        P(None, None, "tensor"),
        P("dp"),
        P(("dp", "context"), "tensor"),
        P(("dp", "context"), "tensor"),
    )
    return jax.shard_map(
        shards,
        mesh=mesh,
        in_specs=placed,
        out_specs=P(("dp", "context"), "tensor"),
        check_vma=False,
    )
```

```python
import functools
import math

import jax
import jax.numpy as jnp
from jax import lax
from jax.experimental import pallas as pl
from jax.experimental.pallas import tpu as pltpu
from jax.sharding import PartitionSpec as P

HEAD = 128


ROTARY_BASE = 1000000.0
NORM_EPSILON = 1e-06


def shifted(x, axis, by):
    devices = lax.axis_size(axis)
    pairs = [(i, i + by) for i in range(devices) if 0 <= i + by < devices]
    return lax.ppermute(x, axis, pairs)


def rotate(features, positions):
    half_width = features.shape[-1] // 2
    exponents = jnp.arange(half_width, dtype=jnp.float32) * (2.0 / features.shape[-1])
    frequency = jnp.exp(-math.log(ROTARY_BASE) * exponents)
    angles = positions[:, None] * frequency[None, :]
    cosine = jnp.cos(angles)[:, None, :]
    sine_values = jnp.sin(angles)[:, None, :]
    front = features[..., :half_width]
    back = features[..., half_width:]
    return jnp.concatenate(
        [front * cosine - back * sine_values, back * cosine + front * sine_values], axis=-1
    )


def front_kernel(
    idx_ref, s_ref, recv_ref, tail_ref, tap_ref, rate_ref, res_ref,
    prod_ref, f1_ref, out_ref, fin_ref, fin_scr,
):
    length = s_ref.shape[1]
    mode_count = rate_ref.shape[0]
    row = lax.broadcasted_iota(jnp.int32, (length, s_ref.shape[2]), 0)
    filtered = []
    for i in range(3):
        now = s_ref[i].astype(jnp.float32)
        before = jnp.where(
            idx_ref[0] == 0, tail_ref[i].astype(jnp.float32), recv_ref[i].astype(jnp.float32)
        )
        back1 = jnp.where(row == 0, before[1:2], pltpu.roll(now, 1, 0))
        back2 = jnp.where(
            row == 0, before[0:1], jnp.where(row == 1, before[1:2], pltpu.roll(now, 2, 0))
        )
        taps = tap_ref[:, i, :]
        filtered.append(taps[0:1] * now + taps[1:2] * back1 + taps[2:3] * back2)
    product = (filtered[0] * filtered[2]).astype(jnp.bfloat16)
    prod_ref[...] = product
    f1_ref[...] = filtered[1]
    x = product.astype(jnp.float32)
    rows = lax.broadcasted_iota(jnp.int32, (length, length), 0)
    cols = lax.broadcasted_iota(jnp.int32, (length, length), 1)
    lower = (rows >= cols).astype(jnp.bfloat16)
    offsets = lax.broadcasted_iota(jnp.int32, (length, 1), 0).astype(jnp.float32)
    gains = jnp.sqrt(1.0 - jnp.exp(-2.0 * rate_ref[...]))
    rgains = res_ref[...] * gains
    total = jnp.zeros(x.shape, jnp.float32)
    for m in range(mode_count):
        rate = rate_ref[m : m + 1, :]
        terms = jnp.exp(rate * offsets) * x
        high = terms.astype(jnp.bfloat16)
        low = (terms - high.astype(jnp.float32)).astype(jnp.bfloat16)
        prefix = jnp.dot(lower, high, preferred_element_type=jnp.float32) + jnp.dot(
            lower, low, preferred_element_type=jnp.float32
        )
        total = total + rgains[m : m + 1, :] * jnp.exp(-rate * offsets) * prefix
        fin_scr[m : m + 1, :] = (
            gains[m : m + 1, :] * jnp.exp(-rate * (length - 1.0)) * prefix[length - 1 : length, :]
        )
    out_ref[...] = total
    fin_ref[...] = jnp.broadcast_to(fin_scr[...][None], fin_ref.shape).astype(fin_ref.dtype)


def back_kernel(
    idx_ref, local_ref, rate_ref, res_ref, fin_ref, hs_ref,
    f1_ref, prod_ref, resid_ref, skip_ref, out_ref,
):
    length = local_ref.shape[0]
    mode_count = rate_ref.shape[0]
    rates = rate_ref[...]
    me = idx_ref[0]
    incoming = jnp.exp(-rates * (me * length).astype(jnp.float32)) * hs_ref[...]
    for src in range(fin_ref.shape[0]):
        steps_back = (jnp.maximum(me - 1 - src, 0) * length).astype(jnp.float32)
        weight_src = jnp.where(src < me, jnp.exp(-rates * steps_back), 0.0)
        incoming = incoming + weight_src * fin_ref[src].astype(jnp.float32)
    weight = res_ref[...] * incoming
    steps = lax.broadcasted_iota(jnp.int32, (length, 1), 0).astype(jnp.float32) + 1.0
    total = local_ref[...]
    for m in range(mode_count):
        total = total + weight[m : m + 1, :] * jnp.exp(-rates[m : m + 1, :] * steps)
    long_out = total.astype(jnp.bfloat16).astype(jnp.float32)
    hidden = (
        resid_ref[...].astype(jnp.float32)
        + f1_ref[...] * (long_out + skip_ref[...] * prod_ref[...].astype(jnp.float32))
    ).astype(out_ref.dtype)
    out_ref[...] = jnp.broadcast_to(hidden[None], out_ref.shape)


def channel_blocks(kernel, index, inputs, outputs, block, scratch=()):
    def spec(shape):
        lead = tuple(0 for _ in shape[:-1])
        return pl.BlockSpec(tuple(shape[:-1]) + (block,), lambda j, idx: lead + (j,))

    grid_spec = pltpu.PrefetchScalarGridSpec(
        num_scalar_prefetch=1,
        grid=(outputs[0].shape[-1] // block,),
        in_specs=[spec(a.shape) for a in inputs],
        out_specs=[spec(o.shape) for o in outputs],
        scratch_shapes=list(scratch),
    )
    return pl.pallas_call(kernel, grid_spec=grid_spec, out_shape=outputs)(index, *inputs)


def cache_attention_kernel(scale, q_ref, k_ref, v_ref, max_ref, sum_ref, num_ref):
    scores = (
        lax.dot_general(
            q_ref[...], k_ref[...], (((1,), (1,)), ((), ())), preferred_element_type=jnp.float32
        )
        * scale
    )
    row_max = jnp.max(scores, axis=1, keepdims=True)
    weights = jnp.exp(scores - row_max).astype(jnp.bfloat16)
    ones = jnp.ones((weights.shape[1], 128), jnp.bfloat16)
    max_ref[...] = jnp.broadcast_to(row_max, max_ref.shape)
    sum_ref[...] = jnp.dot(weights, ones, preferred_element_type=jnp.float32)
    num_ref[...] = jnp.dot(weights, v_ref[...], preferred_element_type=jnp.float32)


def new_attention_kernel(
    scale, reach, q_ref, k_ref, v_ref, qpos_ref, max_ref, sum_ref, num_ref, out_ref
):
    def block_with(keys):
        scores = (
            lax.dot_general(
                q_ref[...], k_ref[:keys], (((1,), (1,)), ((), ())),
                preferred_element_type=jnp.float32,
            )
            * scale
        )
        key_pos = lax.broadcasted_iota(jnp.int32, (1, keys), 1)
        scores = jnp.where(key_pos <= qpos_ref[...], scores, -jnp.inf)
        old_max = max_ref[:, :1]
        row_max = jnp.maximum(old_max, jnp.max(scores, axis=1, keepdims=True))
        rescale = jnp.exp(old_max - row_max)
        weights = jnp.exp(scores - row_max).astype(jnp.bfloat16)
        ones = jnp.ones((keys, 128), jnp.bfloat16)
        weight_sum = sum_ref[:, :1] * rescale + jnp.dot(
            weights, ones, preferred_element_type=jnp.float32
        )[:, :1]
        numerator = num_ref[...] * rescale + jnp.dot(
            weights, v_ref[:keys], preferred_element_type=jnp.float32
        )
        out_ref[...] = (numerator / weight_sum).astype(out_ref.dtype)

    key_rows = k_ref.shape[0]
    for i in range(pl.cdiv(key_rows, reach)):
        keys = min(key_rows, reach * (i + 1))
        last = keys == key_rows

        @pl.when((pl.program_id(0) >= i) if last else (pl.program_id(0) == i))
        def _():
            block_with(keys)


def attend_cache(queries, keys, values, block=512):
    rows, width = queries.shape
    key_rows = keys.shape[0]
    piece = jax.ShapeDtypeStruct((rows, width), jnp.float32)
    row_spec = pl.BlockSpec((block, width), lambda i: (i, 0))
    return pl.pallas_call(
        functools.partial(cache_attention_kernel, 1.0 / math.sqrt(width)),
        grid=(rows // block,),
        in_specs=[
            row_spec,
            pl.BlockSpec((key_rows, width), lambda i: (0, 0)),
            pl.BlockSpec((key_rows, width), lambda i: (0, 0)),
        ],
        out_specs=[row_spec, row_spec, row_spec],
        out_shape=[piece, piece, piece],
        compiler_params=pltpu.CompilerParams(vmem_limit_bytes=48 * 1024 * 1024),
        cost_estimate=pl.CostEstimate(
            flops=6 * rows * key_rows * width,
            bytes_accessed=2 * rows * width + 4 * key_rows * width + 12 * rows * width,
            transcendentals=rows * key_rows,
        ),
    )(queries, keys, values)


def attend_new(queries, keys, values, query_pos, pieces, spread, block=512):
    rows, width = queries.shape
    key_rows = keys.shape[0]
    row_spec = pl.BlockSpec((block, width), lambda i: (i, 0))
    return pl.pallas_call(
        functools.partial(new_attention_kernel, 1.0 / math.sqrt(width), block * spread),
        grid=(rows // block,),
        in_specs=[
            row_spec,
            pl.BlockSpec((key_rows, width), lambda i: (0, 0)),
            pl.BlockSpec((key_rows, width), lambda i: (0, 0)),
            pl.BlockSpec((block, 1), lambda i: (i, 0)),
            row_spec,
            row_spec,
            row_spec,
        ],
        out_specs=row_spec,
        out_shape=jax.ShapeDtypeStruct((rows, width), jnp.bfloat16),
        compiler_params=pltpu.CompilerParams(vmem_limit_bytes=48 * 1024 * 1024),
    )(queries, keys, values, query_pos.reshape(rows, 1), *pieces)


def project_kernel(x_ref, w_ref, out_ref):
    out_ref[...] = jnp.dot(x_ref[...], w_ref[...], preferred_element_type=jnp.float32)


def project(x, w, block=1024):
    rows, depth = x.shape
    groups, _, width = w.shape
    return pl.pallas_call(
        project_kernel,
        grid=(groups, width // block),
        in_specs=[
            pl.BlockSpec((rows, depth), lambda g, j: (0, 0)),
            pl.BlockSpec((None, depth, block), lambda g, j: (g, 0, j)),
        ],
        out_specs=pl.BlockSpec((None, rows, block), lambda g, j: (g, 0, j)),
        out_shape=jax.ShapeDtypeStruct((groups, rows, width), jnp.float32),
        compiler_params=pltpu.CompilerParams(vmem_limit_bytes=48 * 1024 * 1024),
        cost_estimate=pl.CostEstimate(
            flops=2 * rows * depth * width * groups,
            bytes_accessed=2 * (rows * depth + groups * depth * width) + 4 * groups * rows * width,
            transcendentals=0,
        ),
    )(x, w)


def shards(
    streams,
    stream_tail,
    short_taps,
    decay_rates,
    residues,
    hyena_state,
    skip_weight,
    residual,
    norm_gain,
    qkv_weight,
    start_offset,
    cache_keys,
    cache_values,
):
    row_count = streams.shape[0]
    tap_count = short_taps.shape[0]
    devices = lax.axis_size("context")
    device_index = lax.axis_index("context")
    head_width = qkv_weight.shape[2]
    heads_here = head_width // HEAD
    half_rows = row_count // 2

    def by_head(block):
        per_head = block.reshape(row_count, heads_here, HEAD).transpose(1, 0, 2)
        return jnp.repeat(per_head, devices // heads_here, axis=0)

    cache_kv = lax.all_to_all(
        jnp.concatenate([by_head(cache_keys), by_head(cache_values)], axis=1),
        "context", 0, 0, tiled=True,
    )
    cache_k, cache_v = cache_kv[:, :row_count], cache_kv[:, row_count:]

    received = shifted(streams[row_count - (tap_count - 1) :], "context", 1)
    channels = streams.shape[2]
    mode_count = decay_rates.shape[0]
    ways = lax.axis_size("tensor")
    index = device_index.astype(jnp.int32).reshape(1)
    block = 256
    product, filtered1, local_out, finals_out = channel_blocks(
        front_kernel,
        index,
        [
            streams.transpose(1, 0, 2),
            received.transpose(1, 0, 2),
            stream_tail.transpose(1, 0, 2),
            short_taps,
            decay_rates,
            residues,
        ],
        [
            jax.ShapeDtypeStruct((row_count, channels), jnp.bfloat16),
            jax.ShapeDtypeStruct((row_count, channels), jnp.float32),
            jax.ShapeDtypeStruct((row_count, channels), jnp.float32),
            jax.ShapeDtypeStruct((devices, mode_count, channels), jnp.bfloat16),
        ],
        block,
        [pltpu.VMEM((mode_count, block), jnp.float32)],
    )
    finals = lax.all_to_all(finals_out, "context", 0, 0, tiled=True)
    (hidden_out,) = channel_blocks(
        back_kernel,
        index,
        [
            local_out,
            decay_rates,
            residues,
            finals,
            hyena_state,
            filtered1,
            product,
            residual,
            skip_weight[None, :],
        ],
        [jax.ShapeDtypeStruct((ways, row_count, channels), jnp.bfloat16)],
        2 * block,
    )
    gathered = lax.all_to_all(hidden_out, "tensor", 0, 0, tiled=True)
    gathered = gathered.transpose(1, 0, 2).reshape(row_count, ways * channels)
    hidden_float = gathered.astype(jnp.float32)
    mean_square = jnp.mean(hidden_float * hidden_float, axis=1, keepdims=True)
    normed = (hidden_float * lax.rsqrt(mean_square + NORM_EPSILON) * norm_gain[None, :]).astype(
        jnp.bfloat16
    )
    projected = (
        project(normed, qkv_weight.transpose(1, 0, 2))
        .transpose(1, 0, 2)
        .reshape(row_count, 3, heads_here, HEAD)
    )
    query_index = device_index * row_count + jnp.arange(row_count, dtype=jnp.int32)
    positions = (start_offset[0] + query_index).astype(jnp.float32)
    queries = rotate(projected[:, 0], positions).astype(jnp.bfloat16)
    new_keys = rotate(projected[:, 1], positions).astype(jnp.bfloat16)
    new_values = projected[:, 2].astype(jnp.bfloat16)

    query_parts = (
        queries.reshape(2, half_rows, heads_here, HEAD)
        .transpose(2, 0, 1, 3)
        .reshape(devices, half_rows, HEAD)
    )
    sent = lax.all_to_all(
        jnp.concatenate([query_parts, by_head(new_keys), by_head(new_values)], axis=1),
        "context", 0, 0, tiled=True,
    )
    my_queries = sent[:, :half_rows]
    new_k = sent[:, half_rows : half_rows + row_count]
    new_v = sent[:, half_rows + row_count :]

    q_flat = my_queries.reshape(-1, HEAD)
    src = jnp.arange(devices, dtype=jnp.int32)[:, None]
    row = jnp.arange(half_rows, dtype=jnp.int32)[None, :]
    query_pos = (src * row_count + (device_index % 2) * half_rows + row).reshape(-1)
    pieces = attend_cache(q_flat, cache_k.reshape(-1, HEAD), cache_v.reshape(-1, HEAD))
    mine = attend_new(
        q_flat, new_k.reshape(-1, HEAD), new_v.reshape(-1, HEAD), query_pos, pieces,
        row_count // half_rows,
    ).reshape(devices, half_rows, HEAD)
    back = lax.all_to_all(mine, "context", 0, 0, tiled=True)
    attended = (
        back.reshape(heads_here, 2, half_rows, HEAD)
        .transpose(1, 2, 0, 3)
        .reshape(row_count, head_width)
    )
    return attended


def solution(mesh):
    placed = (
        P(("dp", "context"), None, "tensor"),
        P("dp", None, "tensor"),
        P(None, None, "tensor"),
        P(None, "tensor"),
        P(None, "tensor"),
        P("dp", "tensor"),
        P("tensor"),
        P(("dp", "context"), "tensor"),
        P(),
        P(None, None, "tensor"),
        P("dp"),
        P(("dp", "context"), "tensor"),
        P(("dp", "context"), "tensor"),
    )
    return jax.shard_map(
        shards,
        mesh=mesh,
        in_specs=placed,
        out_specs=P(("dp", "context"), "tensor"),
        check_vma=False,
    )
```

```python
import functools
import math

import jax
import jax.numpy as jnp
from jax import lax
from jax.experimental import pallas as pl
from jax.experimental.pallas import tpu as pltpu
from jax.sharding import PartitionSpec as P

HEAD = 128


ROTARY_BASE = 1000000.0
NORM_EPSILON = 1e-06


def shifted(x, axis, by):
    devices = lax.axis_size(axis)
    pairs = [(i, i + by) for i in range(devices) if 0 <= i + by < devices]
    return lax.ppermute(x, axis, pairs)


def rotate(features, positions):
    half_width = features.shape[-1] // 2
    exponents = jnp.arange(half_width, dtype=jnp.float32) * (2.0 / features.shape[-1])
    frequency = jnp.exp(-math.log(ROTARY_BASE) * exponents)
    angles = positions[:, None] * frequency[None, :]
    cosine = jnp.cos(angles)[:, None, :]
    sine_values = jnp.sin(angles)[:, None, :]
    front = features[..., :half_width]
    back = features[..., half_width:]
    return jnp.concatenate(
        [front * cosine - back * sine_values, back * cosine + front * sine_values], axis=-1
    )


def front_kernel(
    idx_ref, s_ref, recv_ref, tail_ref, tap_ref, rate_ref, res_ref,
    prod_ref, f1_ref, out_ref, fin_ref, fin_scr,
):
    length = s_ref.shape[1]
    mode_count = rate_ref.shape[0]
    row = lax.broadcasted_iota(jnp.int32, (length, s_ref.shape[2]), 0)
    filtered = []
    for i in range(3):
        now = s_ref[i].astype(jnp.float32)
        before = jnp.where(
            idx_ref[0] == 0, tail_ref[i].astype(jnp.float32), recv_ref[i].astype(jnp.float32)
        )
        back1 = jnp.where(row == 0, before[1:2], pltpu.roll(now, 1, 0))
        back2 = jnp.where(
            row == 0, before[0:1], jnp.where(row == 1, before[1:2], pltpu.roll(now, 2, 0))
        )
        taps = tap_ref[:, i, :]
        filtered.append(taps[0:1] * now + taps[1:2] * back1 + taps[2:3] * back2)
    product = (filtered[0] * filtered[2]).astype(jnp.bfloat16)
    prod_ref[...] = product
    f1_ref[...] = filtered[1]
    x = product.astype(jnp.float32)
    rows = lax.broadcasted_iota(jnp.int32, (length, length), 0)
    cols = lax.broadcasted_iota(jnp.int32, (length, length), 1)
    lower = (rows >= cols).astype(jnp.bfloat16)
    offsets = lax.broadcasted_iota(jnp.int32, (length, 1), 0).astype(jnp.float32)
    gains = jnp.sqrt(1.0 - jnp.exp(-2.0 * rate_ref[...]))
    rgains = res_ref[...] * gains
    total = jnp.zeros(x.shape, jnp.float32)
    for m in range(mode_count):
        rate = rate_ref[m : m + 1, :]
        terms = jnp.exp(rate * offsets) * x
        high = terms.astype(jnp.bfloat16)
        low = (terms - high.astype(jnp.float32)).astype(jnp.bfloat16)
        prefix = jnp.dot(lower, high, preferred_element_type=jnp.float32) + jnp.dot(
            lower, low, preferred_element_type=jnp.float32
        )
        total = total + rgains[m : m + 1, :] * jnp.exp(-rate * offsets) * prefix
        fin_scr[m : m + 1, :] = (
            gains[m : m + 1, :] * jnp.exp(-rate * (length - 1.0)) * prefix[length - 1 : length, :]
        )
    out_ref[...] = total
    fin_ref[...] = jnp.broadcast_to(fin_scr[...][None], fin_ref.shape).astype(fin_ref.dtype)


def back_kernel(
    idx_ref, local_ref, rate_ref, res_ref, fin_ref, hs_ref,
    f1_ref, prod_ref, resid_ref, skip_ref, out_ref,
):
    length = local_ref.shape[0]
    mode_count = rate_ref.shape[0]
    rates = rate_ref[...]
    me = idx_ref[0]
    incoming = jnp.exp(-rates * (me * length).astype(jnp.float32)) * hs_ref[...]
    for src in range(fin_ref.shape[0]):
        steps_back = (jnp.maximum(me - 1 - src, 0) * length).astype(jnp.float32)
        weight_src = jnp.where(src < me, jnp.exp(-rates * steps_back), 0.0)
        incoming = incoming + weight_src * fin_ref[src].astype(jnp.float32)
    weight = res_ref[...] * incoming
    steps = lax.broadcasted_iota(jnp.int32, (length, 1), 0).astype(jnp.float32) + 1.0
    total = local_ref[...]
    for m in range(mode_count):
        total = total + weight[m : m + 1, :] * jnp.exp(-rates[m : m + 1, :] * steps)
    long_out = total.astype(jnp.bfloat16).astype(jnp.float32)
    hidden = (
        resid_ref[...].astype(jnp.float32)
        + f1_ref[...] * (long_out + skip_ref[...] * prod_ref[...].astype(jnp.float32))
    ).astype(out_ref.dtype)
    out_ref[...] = jnp.broadcast_to(hidden[None], out_ref.shape)


def channel_blocks(kernel, index, inputs, outputs, block, scratch=()):
    def spec(shape):
        lead = tuple(0 for _ in shape[:-1])
        return pl.BlockSpec(tuple(shape[:-1]) + (block,), lambda j, idx: lead + (j,))

    grid_spec = pltpu.PrefetchScalarGridSpec(
        num_scalar_prefetch=1,
        grid=(outputs[0].shape[-1] // block,),
        in_specs=[spec(a.shape) for a in inputs],
        out_specs=[spec(o.shape) for o in outputs],
        scratch_shapes=list(scratch),
    )
    return pl.pallas_call(kernel, grid_spec=grid_spec, out_shape=outputs)(index, *inputs)


def cache_attention_kernel(scale, q_ref, k_ref, v_ref, max_ref, sum_ref, num_ref):
    scores = (
        lax.dot_general(
            q_ref[...], k_ref[...], (((1,), (1,)), ((), ())), preferred_element_type=jnp.float32
        )
        * scale
    )
    row_max = jnp.max(scores, axis=1, keepdims=True)
    weights = jnp.exp(scores - row_max).astype(jnp.bfloat16)
    ones = jnp.ones((weights.shape[1], 128), jnp.bfloat16)
    max_ref[...] = jnp.broadcast_to(row_max, max_ref.shape)
    sum_ref[...] = jnp.dot(weights, ones, preferred_element_type=jnp.float32)
    num_ref[...] = jnp.dot(weights, v_ref[...], preferred_element_type=jnp.float32)


def new_attention_kernel(
    scale, reach, q_ref, k_ref, v_ref, qpos_ref, max_ref, sum_ref, num_ref, out_ref
):
    def block_with(keys):
        scores = (
            lax.dot_general(
                q_ref[...], k_ref[:keys], (((1,), (1,)), ((), ())),
                preferred_element_type=jnp.float32,
            )
            * scale
        )
        key_pos = lax.broadcasted_iota(jnp.int32, (1, keys), 1)
        scores = jnp.where(key_pos <= qpos_ref[...], scores, -jnp.inf)
        old_max = max_ref[:, :1]
        row_max = jnp.maximum(old_max, jnp.max(scores, axis=1, keepdims=True))
        rescale = jnp.exp(old_max - row_max)
        weights = jnp.exp(scores - row_max).astype(jnp.bfloat16)
        ones = jnp.ones((keys, 128), jnp.bfloat16)
        weight_sum = sum_ref[:, :1] * rescale + jnp.dot(
            weights, ones, preferred_element_type=jnp.float32
        )[:, :1]
        numerator = num_ref[...] * rescale + jnp.dot(
            weights, v_ref[:keys], preferred_element_type=jnp.float32
        )
        out_ref[...] = (numerator / weight_sum).astype(out_ref.dtype)

    key_rows = k_ref.shape[0]
    for i in range(pl.cdiv(key_rows, reach)):
        keys = min(key_rows, reach * (i + 1))
        last = keys == key_rows

        @pl.when((pl.program_id(0) >= i) if last else (pl.program_id(0) == i))
        def _():
            block_with(keys)


def attend_cache(queries, keys, values, block=1024):
    rows, width = queries.shape
    key_rows = keys.shape[0]
    piece = jax.ShapeDtypeStruct((rows, width), jnp.float32)
    row_spec = pl.BlockSpec((block, width), lambda i: (i, 0))
    return pl.pallas_call(
        functools.partial(cache_attention_kernel, 1.0 / math.sqrt(width)),
        grid=(rows // block,),
        in_specs=[
            row_spec,
            pl.BlockSpec((key_rows, width), lambda i: (0, 0)),
            pl.BlockSpec((key_rows, width), lambda i: (0, 0)),
        ],
        out_specs=[row_spec, row_spec, row_spec],
        out_shape=[piece, piece, piece],
        compiler_params=pltpu.CompilerParams(vmem_limit_bytes=48 * 1024 * 1024),
        cost_estimate=pl.CostEstimate(
            flops=6 * rows * key_rows * width,
            bytes_accessed=2 * rows * width + 4 * key_rows * width + 12 * rows * width,
            transcendentals=rows * key_rows,
        ),
    )(queries, keys, values)


def attend_new(queries, keys, values, query_pos, pieces, spread, block=512):
    rows, width = queries.shape
    key_rows = keys.shape[0]
    row_spec = pl.BlockSpec((block, width), lambda i: (i, 0))
    return pl.pallas_call(
        functools.partial(new_attention_kernel, 1.0 / math.sqrt(width), block * spread),
        grid=(rows // block,),
        in_specs=[
            row_spec,
            pl.BlockSpec((key_rows, width), lambda i: (0, 0)),
            pl.BlockSpec((key_rows, width), lambda i: (0, 0)),
            pl.BlockSpec((block, 1), lambda i: (i, 0)),
            row_spec,
            row_spec,
            row_spec,
        ],
        out_specs=row_spec,
        out_shape=jax.ShapeDtypeStruct((rows, width), jnp.bfloat16),
        compiler_params=pltpu.CompilerParams(vmem_limit_bytes=48 * 1024 * 1024),
    )(queries, keys, values, query_pos.reshape(rows, 1), *pieces)


def project_kernel(x_ref, w_ref, out_ref):
    out_ref[...] = jnp.dot(x_ref[...], w_ref[...], preferred_element_type=jnp.float32)


def project(x, w, block=1024):
    rows, depth = x.shape
    groups, _, width = w.shape
    return pl.pallas_call(
        project_kernel,
        grid=(groups, width // block),
        in_specs=[
            pl.BlockSpec((rows, depth), lambda g, j: (0, 0)),
            pl.BlockSpec((None, depth, block), lambda g, j: (g, 0, j)),
        ],
        out_specs=pl.BlockSpec((None, rows, block), lambda g, j: (g, 0, j)),
        out_shape=jax.ShapeDtypeStruct((groups, rows, width), jnp.float32),
        compiler_params=pltpu.CompilerParams(vmem_limit_bytes=48 * 1024 * 1024),
        cost_estimate=pl.CostEstimate(
            flops=2 * rows * depth * width * groups,
            bytes_accessed=2 * (rows * depth + groups * depth * width) + 4 * groups * rows * width,
            transcendentals=0,
        ),
    )(x, w)


def shards(
    streams,
    stream_tail,
    short_taps,
    decay_rates,
    residues,
    hyena_state,
    skip_weight,
    residual,
    norm_gain,
    qkv_weight,
    start_offset,
    cache_keys,
    cache_values,
):
    row_count = streams.shape[0]
    tap_count = short_taps.shape[0]
    devices = lax.axis_size("context")
    device_index = lax.axis_index("context")
    head_width = qkv_weight.shape[2]
    heads_here = head_width // HEAD
    half_rows = row_count // 2

    def by_head(block):
        per_head = block.reshape(row_count, heads_here, HEAD).transpose(1, 0, 2)
        return jnp.repeat(per_head, devices // heads_here, axis=0)

    cache_kv = lax.all_to_all(
        jnp.concatenate([by_head(cache_keys), by_head(cache_values)], axis=1),
        "context", 0, 0, tiled=True,
    )
    cache_k, cache_v = cache_kv[:, :row_count], cache_kv[:, row_count:]

    received = shifted(streams[row_count - (tap_count - 1) :], "context", 1)
    channels = streams.shape[2]
    mode_count = decay_rates.shape[0]
    ways = lax.axis_size("tensor")
    index = device_index.astype(jnp.int32).reshape(1)
    block = 256
    product, filtered1, local_out, finals_out = channel_blocks(
        front_kernel,
        index,
        [
            streams.transpose(1, 0, 2),
            received.transpose(1, 0, 2),
            stream_tail.transpose(1, 0, 2),
            short_taps,
            decay_rates,
            residues,
        ],
        [
            jax.ShapeDtypeStruct((row_count, channels), jnp.bfloat16),
            jax.ShapeDtypeStruct((row_count, channels), jnp.float32),
            jax.ShapeDtypeStruct((row_count, channels), jnp.float32),
            jax.ShapeDtypeStruct((devices, mode_count, channels), jnp.bfloat16),
        ],
        block,
        [pltpu.VMEM((mode_count, block), jnp.float32)],
    )
    finals = lax.all_to_all(finals_out, "context", 0, 0, tiled=True)
    (hidden_out,) = channel_blocks(
        back_kernel,
        index,
        [
            local_out,
            decay_rates,
            residues,
            finals,
            hyena_state,
            filtered1,
            product,
            residual,
            skip_weight[None, :],
        ],
        [jax.ShapeDtypeStruct((ways, row_count, channels), jnp.bfloat16)],
        2 * block,
    )
    gathered = lax.all_to_all(hidden_out, "tensor", 0, 0, tiled=True)
    gathered = gathered.transpose(1, 0, 2).reshape(row_count, ways * channels)
    hidden_float = gathered.astype(jnp.float32)
    mean_square = jnp.mean(hidden_float * hidden_float, axis=1, keepdims=True)
    normed = (hidden_float * lax.rsqrt(mean_square + NORM_EPSILON) * norm_gain[None, :]).astype(
        jnp.bfloat16
    )
    projected = (
        project(normed, qkv_weight.transpose(1, 0, 2))
        .transpose(1, 0, 2)
        .reshape(row_count, 3, heads_here, HEAD)
    )
    query_index = device_index * row_count + jnp.arange(row_count, dtype=jnp.int32)
    positions = (start_offset[0] + query_index).astype(jnp.float32)
    queries = rotate(projected[:, 0], positions).astype(jnp.bfloat16)
    new_keys = rotate(projected[:, 1], positions).astype(jnp.bfloat16)
    new_values = projected[:, 2].astype(jnp.bfloat16)

    query_parts = (
        queries.reshape(2, half_rows, heads_here, HEAD)
        .transpose(2, 0, 1, 3)
        .reshape(devices, half_rows, HEAD)
    )
    sent = lax.all_to_all(
        jnp.concatenate([query_parts, by_head(new_keys), by_head(new_values)], axis=1),
        "context", 0, 0, tiled=True,
    )
    my_queries = sent[:, :half_rows]
    new_k = sent[:, half_rows : half_rows + row_count]
    new_v = sent[:, half_rows + row_count :]

    q_flat = my_queries.reshape(-1, HEAD)
    src = jnp.arange(devices, dtype=jnp.int32)[:, None]
    row = jnp.arange(half_rows, dtype=jnp.int32)[None, :]
    query_pos = (src * row_count + (device_index % 2) * half_rows + row).reshape(-1)
    pieces = attend_cache(q_flat, cache_k.reshape(-1, HEAD), cache_v.reshape(-1, HEAD))
    mine = attend_new(
        q_flat, new_k.reshape(-1, HEAD), new_v.reshape(-1, HEAD), query_pos, pieces,
        row_count // half_rows,
    ).reshape(devices, half_rows, HEAD)
    back = lax.all_to_all(mine, "context", 0, 0, tiled=True)
    attended = (
        back.reshape(heads_here, 2, half_rows, HEAD)
        .transpose(1, 2, 0, 3)
        .reshape(row_count, head_width)
    )
    return attended


def solution(mesh):
    placed = (
        P(("dp", "context"), None, "tensor"),
        P("dp", None, "tensor"),
        P(None, None, "tensor"),
        P(None, "tensor"),
        P(None, "tensor"),
        P("dp", "tensor"),
        P("tensor"),
        P(("dp", "context"), "tensor"),
        P(),
        P(None, None, "tensor"),
        P("dp"),
        P(("dp", "context"), "tensor"),
        P(("dp", "context"), "tensor"),
    )
    return jax.shard_map(
        shards,
        mesh=mesh,
        in_specs=placed,
        out_specs=P(("dp", "context"), "tensor"),
        check_vma=False,
    )
```

```python
import functools
import math

import jax
import jax.numpy as jnp
from jax import lax
from jax.experimental import pallas as pl
from jax.experimental.pallas import tpu as pltpu
from jax.sharding import PartitionSpec as P

HEAD = 128


ROTARY_BASE = 1000000.0
NORM_EPSILON = 1e-06


def shifted(x, axis, by):
    devices = lax.axis_size(axis)
    pairs = [(i, i + by) for i in range(devices) if 0 <= i + by < devices]
    return lax.ppermute(x, axis, pairs)


def rotate(features, positions):
    half_width = features.shape[-1] // 2
    exponents = jnp.arange(half_width, dtype=jnp.float32) * (2.0 / features.shape[-1])
    frequency = jnp.exp(-math.log(ROTARY_BASE) * exponents)
    angles = positions[:, None] * frequency[None, :]
    cosine = jnp.cos(angles)[:, None, :]
    sine_values = jnp.sin(angles)[:, None, :]
    front = features[..., :half_width]
    back = features[..., half_width:]
    return jnp.concatenate(
        [front * cosine - back * sine_values, back * cosine + front * sine_values], axis=-1
    )


def front_kernel(
    idx_ref, s_ref, recv_ref, tail_ref, tap_ref, rate_ref, res_ref,
    prod_ref, f1_ref, out_ref, fin_ref, fin_scr,
):
    length = s_ref.shape[1]
    mode_count = rate_ref.shape[0]
    row = lax.broadcasted_iota(jnp.int32, (length, s_ref.shape[2]), 0)
    filtered = []
    for i in range(3):
        now = s_ref[i].astype(jnp.float32)
        before = jnp.where(
            idx_ref[0] == 0, tail_ref[i].astype(jnp.float32), recv_ref[i].astype(jnp.float32)
        )
        back1 = jnp.where(row == 0, before[1:2], pltpu.roll(now, 1, 0))
        back2 = jnp.where(
            row == 0, before[0:1], jnp.where(row == 1, before[1:2], pltpu.roll(now, 2, 0))
        )
        taps = tap_ref[:, i, :]
        filtered.append(taps[0:1] * now + taps[1:2] * back1 + taps[2:3] * back2)
    product = (filtered[0] * filtered[2]).astype(jnp.bfloat16)
    prod_ref[...] = product
    f1_ref[...] = filtered[1]
    x = product.astype(jnp.float32)
    rows = lax.broadcasted_iota(jnp.int32, (length, length), 0)
    cols = lax.broadcasted_iota(jnp.int32, (length, length), 1)
    lower = (rows >= cols).astype(jnp.bfloat16)
    offsets = lax.broadcasted_iota(jnp.int32, (length, 1), 0).astype(jnp.float32)
    gains = jnp.sqrt(1.0 - jnp.exp(-2.0 * rate_ref[...]))
    rgains = res_ref[...] * gains
    total = jnp.zeros(x.shape, jnp.float32)
    for m in range(mode_count):
        rate = rate_ref[m : m + 1, :]
        terms = jnp.exp(rate * offsets) * x
        high = terms.astype(jnp.bfloat16)
        low = (terms - high.astype(jnp.float32)).astype(jnp.bfloat16)
        prefix = jnp.dot(lower, high, preferred_element_type=jnp.float32) + jnp.dot(
            lower, low, preferred_element_type=jnp.float32
        )
        total = total + rgains[m : m + 1, :] * jnp.exp(-rate * offsets) * prefix
        fin_scr[m : m + 1, :] = (
            gains[m : m + 1, :] * jnp.exp(-rate * (length - 1.0)) * prefix[length - 1 : length, :]
        )
    out_ref[...] = total
    fin_ref[...] = jnp.broadcast_to(fin_scr[...][None], fin_ref.shape).astype(fin_ref.dtype)


def back_kernel(
    idx_ref, local_ref, rate_ref, res_ref, fin_ref, hs_ref,
    f1_ref, prod_ref, resid_ref, skip_ref, out_ref,
):
    length = local_ref.shape[0]
    mode_count = rate_ref.shape[0]
    rates = rate_ref[...]
    me = idx_ref[0]
    incoming = jnp.exp(-rates * (me * length).astype(jnp.float32)) * hs_ref[...]
    for src in range(fin_ref.shape[0]):
        steps_back = (jnp.maximum(me - 1 - src, 0) * length).astype(jnp.float32)
        weight_src = jnp.where(src < me, jnp.exp(-rates * steps_back), 0.0)
        incoming = incoming + weight_src * fin_ref[src].astype(jnp.float32)
    weight = res_ref[...] * incoming
    steps = lax.broadcasted_iota(jnp.int32, (length, 1), 0).astype(jnp.float32) + 1.0
    total = local_ref[...]
    for m in range(mode_count):
        total = total + weight[m : m + 1, :] * jnp.exp(-rates[m : m + 1, :] * steps)
    long_out = total.astype(jnp.bfloat16).astype(jnp.float32)
    hidden = (
        resid_ref[...].astype(jnp.float32)
        + f1_ref[...] * (long_out + skip_ref[...] * prod_ref[...].astype(jnp.float32))
    ).astype(out_ref.dtype)
    out_ref[...] = jnp.broadcast_to(hidden[None], out_ref.shape)


def channel_blocks(kernel, index, inputs, outputs, block, scratch=()):
    def spec(shape):
        lead = tuple(0 for _ in shape[:-1])
        return pl.BlockSpec(tuple(shape[:-1]) + (block,), lambda j, idx: lead + (j,))

    grid_spec = pltpu.PrefetchScalarGridSpec(
        num_scalar_prefetch=1,
        grid=(outputs[0].shape[-1] // block,),
        in_specs=[spec(a.shape) for a in inputs],
        out_specs=[spec(o.shape) for o in outputs],
        scratch_shapes=list(scratch),
    )
    return pl.pallas_call(kernel, grid_spec=grid_spec, out_shape=outputs)(index, *inputs)


def cache_attention_kernel(scale, q_ref, k_ref, v_ref, max_ref, sum_ref, num_ref):
    scores = (
        lax.dot_general(
            q_ref[...], k_ref[...], (((1,), (1,)), ((), ())), preferred_element_type=jnp.float32
        )
        * scale
    )
    row_max = jnp.max(scores, axis=1, keepdims=True)
    weights = jnp.exp(scores - row_max).astype(jnp.bfloat16)
    ones = jnp.ones((weights.shape[1], 128), jnp.bfloat16)
    max_ref[...] = jnp.broadcast_to(row_max, max_ref.shape)
    sum_ref[...] = jnp.dot(weights, ones, preferred_element_type=jnp.float32)
    num_ref[...] = jnp.dot(weights, v_ref[...], preferred_element_type=jnp.float32)


def new_attention_kernel(
    scale, reach, q_ref, k_ref, v_ref, qpos_ref, max_ref, sum_ref, num_ref, out_ref
):
    def block_with(keys):
        scores = (
            lax.dot_general(
                q_ref[...], k_ref[:keys], (((1,), (1,)), ((), ())),
                preferred_element_type=jnp.float32,
            )
            * scale
        )
        key_pos = lax.broadcasted_iota(jnp.int32, (1, keys), 1)
        scores = jnp.where(key_pos <= qpos_ref[...], scores, -jnp.inf)
        old_max = max_ref[:, :1]
        row_max = jnp.maximum(old_max, jnp.max(scores, axis=1, keepdims=True))
        rescale = jnp.exp(old_max - row_max)
        weights = jnp.exp(scores - row_max).astype(jnp.bfloat16)
        ones = jnp.ones((keys, 128), jnp.bfloat16)
        weight_sum = sum_ref[:, :1] * rescale + jnp.dot(
            weights, ones, preferred_element_type=jnp.float32
        )[:, :1]
        numerator = num_ref[...] * rescale + jnp.dot(
            weights, v_ref[:keys], preferred_element_type=jnp.float32
        )
        out_ref[...] = (numerator / weight_sum).astype(out_ref.dtype)

    key_rows = k_ref.shape[0]
    for i in range(pl.cdiv(key_rows, reach)):
        keys = min(key_rows, reach * (i + 1))
        last = keys == key_rows

        @pl.when((pl.program_id(0) >= i) if last else (pl.program_id(0) == i))
        def _():
            block_with(keys)


def attend_cache(queries, keys, values, block=1024):
    rows, width = queries.shape
    key_rows = keys.shape[0]
    piece = jax.ShapeDtypeStruct((rows, width), jnp.float32)
    row_spec = pl.BlockSpec((block, width), lambda i: (i, 0))
    return pl.pallas_call(
        functools.partial(cache_attention_kernel, 1.0 / math.sqrt(width)),
        grid=(rows // block,),
        in_specs=[
            row_spec,
            pl.BlockSpec((key_rows, width), lambda i: (0, 0)),
            pl.BlockSpec((key_rows, width), lambda i: (0, 0)),
        ],
        out_specs=[row_spec, row_spec, row_spec],
        out_shape=[piece, piece, piece],
        compiler_params=pltpu.CompilerParams(vmem_limit_bytes=48 * 1024 * 1024),
        cost_estimate=pl.CostEstimate(
            flops=6 * rows * key_rows * width,
            bytes_accessed=2 * rows * width + 4 * key_rows * width + 12 * rows * width,
            transcendentals=rows * key_rows,
        ),
    )(queries, keys, values)


def attend_new(queries, keys, values, query_pos, pieces, spread, block=512):
    rows, width = queries.shape
    key_rows = keys.shape[0]
    row_spec = pl.BlockSpec((block, width), lambda i: (i, 0))
    return pl.pallas_call(
        functools.partial(new_attention_kernel, 1.0 / math.sqrt(width), block * spread),
        grid=(rows // block,),
        in_specs=[
            row_spec,
            pl.BlockSpec((key_rows, width), lambda i: (0, 0)),
            pl.BlockSpec((key_rows, width), lambda i: (0, 0)),
            pl.BlockSpec((block, 1), lambda i: (i, 0)),
            row_spec,
            row_spec,
            row_spec,
        ],
        out_specs=row_spec,
        out_shape=jax.ShapeDtypeStruct((rows, width), jnp.bfloat16),
        compiler_params=pltpu.CompilerParams(vmem_limit_bytes=48 * 1024 * 1024),
    )(queries, keys, values, query_pos.reshape(rows, 1), *pieces)


def project_kernel(x_ref, w_ref, out_ref):
    out_ref[...] = jnp.dot(x_ref[...], w_ref[...], preferred_element_type=jnp.float32)


def project(x, w, block=1024):
    rows, depth = x.shape
    groups, _, width = w.shape
    return pl.pallas_call(
        project_kernel,
        grid=(groups, width // block),
        in_specs=[
            pl.BlockSpec((rows, depth), lambda g, j: (0, 0)),
            pl.BlockSpec((None, depth, block), lambda g, j: (g, 0, j)),
        ],
        out_specs=pl.BlockSpec((None, rows, block), lambda g, j: (g, 0, j)),
        out_shape=jax.ShapeDtypeStruct((groups, rows, width), jnp.float32),
        compiler_params=pltpu.CompilerParams(vmem_limit_bytes=48 * 1024 * 1024),
        cost_estimate=pl.CostEstimate(
            flops=2 * rows * depth * width * groups,
            bytes_accessed=2 * (rows * depth + groups * depth * width) + 4 * groups * rows * width,
            transcendentals=0,
        ),
    )(x, w)


def shards(
    streams,
    stream_tail,
    short_taps,
    decay_rates,
    residues,
    hyena_state,
    skip_weight,
    residual,
    norm_gain,
    qkv_weight,
    start_offset,
    cache_keys,
    cache_values,
):
    row_count = streams.shape[0]
    tap_count = short_taps.shape[0]
    devices = lax.axis_size("context")
    device_index = lax.axis_index("context")
    head_width = qkv_weight.shape[2]
    heads_here = head_width // HEAD
    half_rows = row_count // 2

    def by_head(block):
        per_head = block.reshape(row_count, heads_here, HEAD).transpose(1, 0, 2)
        return jnp.repeat(per_head, devices // heads_here, axis=0)

    cache_kv = lax.all_to_all(
        jnp.concatenate([by_head(cache_keys), by_head(cache_values)], axis=1),
        "context", 0, 0, tiled=True,
    )
    cache_k, cache_v = cache_kv[:, :row_count], cache_kv[:, row_count:]

    received = shifted(streams[row_count - (tap_count - 1) :], "context", 1)
    channels = streams.shape[2]
    mode_count = decay_rates.shape[0]
    ways = lax.axis_size("tensor")
    index = device_index.astype(jnp.int32).reshape(1)
    block = 256
    product, filtered1, local_out, finals_out = channel_blocks(
        front_kernel,
        index,
        [
            streams.transpose(1, 0, 2),
            received.transpose(1, 0, 2),
            stream_tail.transpose(1, 0, 2),
            short_taps,
            decay_rates,
            residues,
        ],
        [
            jax.ShapeDtypeStruct((row_count, channels), jnp.bfloat16),
            jax.ShapeDtypeStruct((row_count, channels), jnp.float32),
            jax.ShapeDtypeStruct((row_count, channels), jnp.float32),
            jax.ShapeDtypeStruct((devices, mode_count, channels), jnp.bfloat16),
        ],
        block,
        [pltpu.VMEM((mode_count, block), jnp.float32)],
    )
    finals = lax.all_to_all(finals_out, "context", 0, 0, tiled=True)
    (hidden_out,) = channel_blocks(
        back_kernel,
        index,
        [
            local_out,
            decay_rates,
            residues,
            finals,
            hyena_state,
            filtered1,
            product,
            residual,
            skip_weight[None, :],
        ],
        [jax.ShapeDtypeStruct((ways, row_count, channels), jnp.bfloat16)],
        4 * block,
    )
    gathered = lax.all_to_all(hidden_out, "tensor", 0, 0, tiled=True)
    gathered = gathered.transpose(1, 0, 2).reshape(row_count, ways * channels)
    hidden_float = gathered.astype(jnp.float32)
    mean_square = jnp.mean(hidden_float * hidden_float, axis=1, keepdims=True)
    normed = (hidden_float * lax.rsqrt(mean_square + NORM_EPSILON) * norm_gain[None, :]).astype(
        jnp.bfloat16
    )
    projected = (
        project(normed, qkv_weight.transpose(1, 0, 2))
        .transpose(1, 0, 2)
        .reshape(row_count, 3, heads_here, HEAD)
    )
    query_index = device_index * row_count + jnp.arange(row_count, dtype=jnp.int32)
    positions = (start_offset[0] + query_index).astype(jnp.float32)
    queries = rotate(projected[:, 0], positions).astype(jnp.bfloat16)
    new_keys = rotate(projected[:, 1], positions).astype(jnp.bfloat16)
    new_values = projected[:, 2].astype(jnp.bfloat16)

    query_parts = (
        queries.reshape(2, half_rows, heads_here, HEAD)
        .transpose(2, 0, 1, 3)
        .reshape(devices, half_rows, HEAD)
    )
    sent = lax.all_to_all(
        jnp.concatenate([query_parts, by_head(new_keys), by_head(new_values)], axis=1),
        "context", 0, 0, tiled=True,
    )
    my_queries = sent[:, :half_rows]
    new_k = sent[:, half_rows : half_rows + row_count]
    new_v = sent[:, half_rows + row_count :]

    q_flat = my_queries.reshape(-1, HEAD)
    src = jnp.arange(devices, dtype=jnp.int32)[:, None]
    row = jnp.arange(half_rows, dtype=jnp.int32)[None, :]
    query_pos = (src * row_count + (device_index % 2) * half_rows + row).reshape(-1)
    pieces = attend_cache(q_flat, cache_k.reshape(-1, HEAD), cache_v.reshape(-1, HEAD))
    mine = attend_new(
        q_flat, new_k.reshape(-1, HEAD), new_v.reshape(-1, HEAD), query_pos, pieces,
        row_count // half_rows,
    ).reshape(devices, half_rows, HEAD)
    back = lax.all_to_all(mine, "context", 0, 0, tiled=True)
    attended = (
        back.reshape(heads_here, 2, half_rows, HEAD)
        .transpose(1, 2, 0, 3)
        .reshape(row_count, head_width)
    )
    return attended


def solution(mesh):
    placed = (
        P(("dp", "context"), None, "tensor"),
        P("dp", None, "tensor"),
        P(None, None, "tensor"),
        P(None, "tensor"),
        P(None, "tensor"),
        P("dp", "tensor"),
        P("tensor"),
        P(("dp", "context"), "tensor"),
        P(),
        P(None, None, "tensor"),
        P("dp"),
        P(("dp", "context"), "tensor"),
        P(("dp", "context"), "tensor"),
    )
    return jax.shard_map(
        shards,
        mesh=mesh,
        in_specs=placed,
        out_specs=P(("dp", "context"), "tensor"),
        check_vma=False,
    )
```
